32 devices in a mesh: ctx: 4 (over y, core), row: 8 (over z, x).
Axes of the slice: x: 2, y: 2, z: 4, core: 2. Of those that a mesh axis runs over, the one named last changes fastest.
Arguments:
- queries: bfloat16 [16, 2, 4096], P('row'), may hold values from -400 to 400
- prefix_id: int32 [16], P('row'), may hold values from 0 to 7
- prefix_keys: bfloat16 [8, 1024, 512], P(None, ('ctx', 'row')), may hold values from -8 to 8
- prefix_values: bfloat16 [8, 1024, 512], P(None, ('ctx', 'row')), may hold values from -6 to 6
- pool_keys: bfloat16 [512, 64, 512], P(('ctx', 'row')), may hold values from -5 to 5
- pool_values: bfloat16 [512, 64, 512], P(('ctx', 'row')), may hold values from -6 to 6
- page_table: int32 [16, 32], P('row'), may hold values from 0 to 511, as said below
- suffix_len: int32 [16], P('row'), may hold values from 256 to 2048
- new_keys: bfloat16 [16, 2, 512], P('row'), may hold values from -6.25 to 6.25
- new_values: bfloat16 [16, 2, 512], P('row'), may hold values from -6 to 6
Outputs:
- attended: bfloat16 [16, 2, 4096], P('row')
The draws below stay inside these ranges and needn't reach their ends.
Inputs may be any that keep to these rules, and one draw needn't show every extreme that they name: `page_table`: the 64 entries of the rows i with one value of i // 2 name different pool pages p with (p // 16) % (8) == i // 2, and together they name all such pages.
All inputs are finite; a program needn't handle non-finite values.
Results may differ from the reference program's by a relative error of at most 0.003.
Values may be sent and summed in bfloat16 or wider, within the bound.
No kernel may reach another device: no remote copies, remote signals or barrier semaphores. Data moves between devices by JAX's collectives and lax.ppermute only.
A program may use at most 64 MiB of HBM per device.

```python
import math
import jax
import jax.numpy as jnp
from jax import lax

H = 32
KVH = 4
HD = 128
STEPS = 2
PREFIXES = 8
LP_DEV = 32
PAGE = 64
MAXP = 32
ROWS_DEV = 2
LP = 1024
ROWS = 16
POOL_DEV = 16
SLOTS = 512
N_CTX = 4
N_ROW = 8


def draw_queries(key, part):
    full_shape = (ROWS, STEPS, H, HD)
    base_draw = 3.0 * jax.random.truncated_normal(key, -6.0, 6.0, full_shape, jnp.float32)
    return base_draw.reshape(ROWS, STEPS, H * HD).astype(jnp.bfloat16)


def draw_prefix_keys(key, part):
    full_shape = (PREFIXES, LP, KVH, HD)
    base_draw = jax.random.truncated_normal(key, -6.0, 6.0, full_shape, jnp.float32)
    return base_draw.reshape(PREFIXES, LP, KVH * HD).astype(jnp.bfloat16)


def draw_page_table(key, part):
    per_device = ROWS_DEV * MAXP
    row_devices = ROWS // ROWS_DEV

    def device_pages(row_device):
        slot_order = jax.random.permutation(jax.random.fold_in(key, row_device), per_device)
        ctx_index = slot_order // POOL_DEV
        local_slot = slot_order % POOL_DEV
        return ((ctx_index * row_devices + row_device) * POOL_DEV + local_slot).reshape(ROWS_DEV, MAXP)
    table = jax.vmap(device_pages)(jnp.arange(row_devices, dtype=jnp.int32))
    return table.reshape(ROWS, MAXP).astype(jnp.int32)


def plant(values, stream_key, low, largest):
    longest = values.shape.index(max(values.shape))
    spots = []
    for shift in (0, 1):
        where = [jax.random.randint(jax.random.fold_in(stream_key, axis), (), 0, length) for axis, length in enumerate(values.shape)]
        where[longest] = (where[longest] + shift) % values.shape[longest]
        spots.append(tuple(where))
    return values.at[spots[0]].set(low).at[spots[1]].set(largest)


def steps_of(stream_key, extent, shards, low, top_value):
    gain = 1.0
    for position, parts in shards:
        draws = jax.random.uniform(jax.random.fold_in(jax.random.fold_in(stream_key, 6), position), (parts,), jnp.float32, low / len(shards), top_value / len(shards))
        gain = gain * jnp.repeat(jnp.exp(draws), extent[position] // parts).reshape((-1,) + (1,) * (len(extent) - 1 - position))
    return gain


def gaussian(own_key, extent, scale, reach, shards=(), kind=jnp.bfloat16):
    array = scale * jax.random.normal(own_key, extent, jnp.float32)
    if shards:
        array = array * steps_of(own_key, extent, shards, -0.22, 0.18)
    return jnp.clip(array, -reach, reach).astype(kind)


def setup_inputs(seed: int = 0) -> dict:
    seeds = jax.random.split(jax.random.key(seed), 11)
    return {
        "queries": draw_queries(jax.random.fold_in(seeds[10], 71), 0),
        "prefix_id": plant(jax.random.randint(seeds[1], (ROWS,), 0, PREFIXES), jax.random.fold_in(seeds[1], 1), 0, PREFIXES - 1).astype(jnp.int32),
        "prefix_keys": draw_prefix_keys(jax.random.fold_in(seeds[10], 71), 0),
        "prefix_values": gaussian(seeds[3], (PREFIXES, LP, KVH * HD), 1.0, 6.0, ((1, 32),)),
        "pool_keys": gaussian(seeds[4], (SLOTS, PAGE, KVH * HD), 1.25, 5.0, ((0, 32),)),
        "pool_values": gaussian(seeds[5], (SLOTS, PAGE, KVH * HD), 1.0, 6.0, ((0, 32),)),
        "page_table": draw_page_table(jax.random.fold_in(seeds[10], 71), 0),
        "suffix_len": plant(jax.random.randint(seeds[7], (ROWS,), MAXP * PAGE // 8, MAXP * PAGE + 1), jax.random.fold_in(seeds[7], 1), MAXP * PAGE // 8, MAXP * PAGE).astype(jnp.int32),
        "new_keys": gaussian(seeds[8], (ROWS, STEPS, KVH * HD), 2.5, 6.25, ((0, 8),)),
        "new_values": gaussian(seeds[9], (ROWS, STEPS, KVH * HD), 1.0, 6.0, ((0, 8),)),
    }


MASKED_SCORE = -1e+30

def rounded_weights(scores, valid_mask, peaks):
    raw = jnp.where(valid_mask, jnp.exp(scores - peaks[..., None]), 0.0)
    return raw.astype(jnp.bfloat16).astype(jnp.float32)

def reference(queries, prefix_id, prefix_keys, prefix_values, pool_keys, pool_values, page_table, suffix_len, new_keys, new_values):
    groups = H // KVH
    score_scale = 1.0 / math.sqrt(HD)
    blocks = LP // LP_DEV

    def attend_row(row_item):
        row_query, prefix_index, row_pages, length, fresh_keys_row, fresh_values_row = row_item
        step_count = row_query.shape[0]
        query_heads = row_query.astype(jnp.float32).reshape(step_count, KVH, groups, HD)
        prefix_index = prefix_index.astype(jnp.int32)
        prefix_k = lax.dynamic_index_in_dim(prefix_keys, prefix_index, 0, keepdims=False)
        prefix_k = prefix_k.astype(jnp.float32).reshape(blocks, LP_DEV, KVH, HD)
        prefix_v = lax.dynamic_index_in_dim(prefix_values, prefix_index, 0, keepdims=False)
        prefix_v = prefix_v.astype(jnp.float32).reshape(blocks, LP_DEV, KVH, HD)
        pre_scores = jnp.einsum('skgd,btkd->skgbt', query_heads, prefix_k) * score_scale
        pre_peak = lax.optimization_barrier(jnp.max(pre_scores, axis=-1))
        pre_weights = rounded_weights(pre_scores, True, pre_peak)
        row_pages = row_pages.astype(jnp.int32)
        suffix_k = jnp.take(pool_keys, row_pages, axis=0).astype(jnp.float32).reshape(MAXP, PAGE, KVH, HD)
        suffix_v = jnp.take(pool_values, row_pages, axis=0).astype(jnp.float32).reshape(MAXP, PAGE, KVH, HD)
        suf_scores = jnp.einsum('skgd,jukd->skgju', query_heads, suffix_k) * score_scale
        positions = jnp.arange(MAXP, dtype=jnp.int32)[:, None] * PAGE + jnp.arange(PAGE, dtype=jnp.int32)[None, :]
        kept = positions < length
        ctx_of_page = row_pages // POOL_DEV // N_ROW
        member = ctx_of_page[:, None] == jnp.arange(N_CTX, dtype=jnp.int32)[None, :]
        page_peak = lax.optimization_barrier(jnp.max(jnp.where(kept, suf_scores, MASKED_SCORE), axis=-1))
        block_peak = lax.optimization_barrier(jnp.max(jnp.where(member, page_peak[..., :, None], MASKED_SCORE), axis=-2))
        token_peak = lax.optimization_barrier(jnp.max(jnp.where(member, block_peak[..., None, :], MASKED_SCORE), axis=-1))
        suf_weights = rounded_weights(suf_scores, kept, token_peak)
        fresh_k = fresh_keys_row.astype(jnp.float32).reshape(step_count, KVH, HD)
        fresh_v = fresh_values_row.astype(jnp.float32).reshape(step_count, KVH, HD)
        fresh_scores = jnp.einsum('skgd,tkd->skgt', query_heads, fresh_k) * score_scale
        causal = jnp.arange(step_count)[None, :] <= jnp.arange(step_count)[:, None]
        causal = causal[:, None, None, :]
        fresh_peak = lax.optimization_barrier(jnp.max(jnp.where(causal, fresh_scores, MASKED_SCORE), axis=-1))
        fresh_weights = rounded_weights(fresh_scores, causal, fresh_peak)
        highest = jnp.maximum(jnp.maximum(lax.optimization_barrier(jnp.max(pre_peak, axis=-1)), lax.optimization_barrier(jnp.max(block_peak, axis=-1))), fresh_peak)
        pre_factor = jnp.exp(pre_peak - highest[..., None])
        suf_factor = jnp.exp(token_peak - highest[..., None])
        fresh_factor = jnp.exp(fresh_peak - highest)
        total_all = lax.optimization_barrier(jnp.sum(lax.optimization_barrier(jnp.sum(pre_weights, axis=-1)) * pre_factor, axis=-1))
        total_all = total_all + lax.optimization_barrier(jnp.sum(lax.optimization_barrier(jnp.sum(suf_weights, axis=-1)) * suf_factor, axis=-1))
        total_all = total_all + lax.optimization_barrier(jnp.sum(fresh_weights, axis=-1)) * fresh_factor
        sum_all = jnp.einsum('skgbt,btkd->skgd', pre_weights * pre_factor[..., None], prefix_v)
        sum_all = sum_all + jnp.einsum('skgju,jukd->skgd', suf_weights * suf_factor[..., None], suffix_v)
        sum_all = sum_all + jnp.einsum('skgt,tkd->skgd', fresh_weights, fresh_v) * fresh_factor[..., None]
        return (sum_all / total_all[..., None]).astype(jnp.bfloat16).reshape(step_count, H * HD)
    return lax.map(attend_row, (queries, prefix_id, page_table, suffix_len, new_keys, new_values))
```

```python
import math

import jax
import jax.numpy as jnp
from jax import lax
from jax.sharding import PartitionSpec as P

H = 32
KVH = 4
HD = 128
LANES = 128


MASKED_SCORE = -1e30


def block_stats(scores, valid_mask, values, einsum_form):
    block_peak = jnp.max(jnp.where(valid_mask, scores, MASKED_SCORE), axis=-1)
    weights = jnp.where(valid_mask, jnp.exp(scores - block_peak[..., None]), 0.0).astype(
        jnp.bfloat16
    )
    block_total = jnp.sum(weights.astype(jnp.float32), axis=-1)
    block_sum = jnp.einsum(einsum_form, weights, values, preferred_element_type=jnp.float32)
    return (block_peak, block_total, block_sum)


def combine_pair(earlier, later):
    highest = jnp.maximum(earlier[0], later[0])
    left_factor = jnp.exp(earlier[0] - highest)
    right_factor = jnp.exp(later[0] - highest)
    totals = left_factor * earlier[1] + right_factor * later[1]
    sums = left_factor[..., None] * earlier[2] + right_factor[..., None] * later[2]
    return (highest, totals, sums)


def per_device(
    queries,
    prefix_id,
    prefix_keys,
    prefix_values,
    pool_keys,
    pool_values,
    page_table,
    suffix_len,
    new_keys,
    new_values,
):
    rows_dev, step_count, feature_width = queries.shape
    groups = H // KVH
    score_scale = 1.0 / math.sqrt(HD)
    row_count = lax.axis_size("row")
    ctx_count = lax.axis_size("ctx")
    row_index = lax.axis_index("row")
    ctx_index = lax.axis_index("ctx")
    flat_index = ctx_index * row_count + row_index
    own_query = queries.reshape(rows_dev, step_count, KVH, groups, HD)

    slot_count, page_len, kv_width = pool_keys.shape
    slot_ids = flat_index * slot_count + jnp.arange(slot_count, dtype=jnp.int32)
    slot_match = page_table[:, :, None] == slot_ids[None, None, :]
    entry_pos = jnp.arange(page_table.shape[1], dtype=jnp.int32)
    page_of = jnp.sum(jnp.where(slot_match, entry_pos[None, :, None], 0), axis=1)
    owned = jnp.any(slot_match, axis=1)
    token_pos = (
        page_of[:, :, None] * page_len + jnp.arange(page_len, dtype=jnp.int32)[None, None, :]
    )
    live_mask = owned[:, :, None] & (token_pos < suffix_len[:, None, None])
    live_mask = live_mask.reshape(rows_dev, 1, 1, 1, slot_count * page_len)
    flat_keys = pool_keys.reshape(slot_count * page_len, KVH, HD)
    flat_values = pool_values.reshape(slot_count * page_len, KVH, HD)
    suffix_scores = (
        jnp.einsum("rskgd,tkd->rskgt", own_query, flat_keys, preferred_element_type=jnp.float32)
        * score_scale
    )
    suffix_stats = block_stats(suffix_scores, live_mask, flat_values, "rskgt,tkd->rskgd")

    fresh_keys = new_keys.reshape(rows_dev, step_count, KVH, HD)
    fresh_values = new_values.reshape(rows_dev, step_count, KVH, HD)
    fresh_scores = (
        jnp.einsum("rskgd,rtkd->rskgt", own_query, fresh_keys, preferred_element_type=jnp.float32)
        * score_scale
    )
    causal = jnp.arange(step_count)[None, :] <= jnp.arange(step_count)[:, None]
    causal = causal.reshape(1, step_count, 1, 1, step_count)
    fresh_stats = block_stats(fresh_scores, causal, fresh_values, "rskgt,rtkd->rskgd")

    query_cols = step_count * feature_width
    id_cols = jnp.broadcast_to(prefix_id.astype(jnp.bfloat16)[:, None], (rows_dev, LANES))
    packed = jnp.concatenate([queries.reshape(rows_dev, query_cols), id_cols], axis=1)
    gathered = lax.all_gather(packed, "row", axis=0, tiled=True)
    total_rows = gathered.shape[0]
    every_query = gathered[:, :query_cols].reshape(total_rows, step_count, KVH, groups, HD)
    every_prefix = gathered[:, query_cols].astype(jnp.int32)

    span_len = prefix_keys.shape[1]
    row_keys = jnp.take(prefix_keys, every_prefix, axis=0).reshape(total_rows, span_len, KVH, HD)
    row_values = jnp.take(prefix_values, every_prefix, axis=0).reshape(
        total_rows, span_len, KVH, HD
    )
    prefix_scores = (
        jnp.einsum("rskgd,rtkd->rskgt", every_query, row_keys, preferred_element_type=jnp.float32)
        * score_scale
    )
    always = jnp.ones((1, 1, 1, 1, span_len), dtype=bool)
    prefix_stats = block_stats(prefix_scores, always, row_values, "rskgt,rtkd->rskgd")

    row_start = row_index * rows_dev
    own_prefix = tuple(
        lax.dynamic_slice_in_dim(member, row_start, rows_dev, 0) for member in prefix_stats
    )
    own_merged = combine_pair(own_prefix, suffix_stats)
    peak_all, total_all, sum_all = tuple(
        lax.dynamic_update_slice_in_dim(whole_arr, piece_arr, row_start, 0)
        for whole_arr, piece_arr in zip(prefix_stats, own_merged)
    )

    units = rows_dev * step_count * H
    share = units // ctx_count
    pt_rows = -(-2 * share // LANES)
    peak_u = peak_all.reshape(row_count, ctx_count, share)
    total_u = total_all.reshape(row_count, ctx_count, share)
    sum_u = sum_all.reshape(row_count, ctx_count, share, HD)
    pt = jnp.concatenate([peak_u, total_u], axis=-1)
    pt = jnp.pad(pt, ((0, 0), (0, 0), (0, pt_rows * LANES - 2 * share)))
    pt = pt.reshape(row_count, ctx_count, pt_rows, LANES)
    outgoing = jnp.concatenate([sum_u, pt], axis=2)
    outgoing = jnp.swapaxes(outgoing, 0, 1).reshape(ctx_count * row_count, share + pt_rows, LANES)
    incoming = lax.all_to_all(
        outgoing, ("ctx", "row"), split_axis=0, concat_axis=0, tiled=True
    )
    sources = incoming.shape[0]
    got_sum = incoming[:, :share, :]
    got_pt = incoming[:, share:, :].reshape(sources, pt_rows * LANES)
    got_peak = got_pt[:, :share]
    got_total = got_pt[:, share : 2 * share]

    unit_start = ctx_index * share
    fresh_peak = lax.dynamic_slice_in_dim(fresh_stats[0].reshape(units), unit_start, share)
    fresh_total = lax.dynamic_slice_in_dim(fresh_stats[1].reshape(units), unit_start, share)
    fresh_sum = lax.dynamic_slice_in_dim(fresh_stats[2].reshape(units, HD), unit_start, share)

    top = jnp.maximum(jnp.max(got_peak, axis=0), fresh_peak)
    factor = jnp.exp(got_peak - top[None])
    fresh_factor = jnp.exp(fresh_peak - top)
    denom = jnp.sum(factor * got_total, axis=0) + fresh_factor * fresh_total
    numer = jnp.sum(factor[..., None] * got_sum, axis=0) + fresh_factor[..., None] * fresh_sum
    result = (numer / denom[..., None]).astype(jnp.bfloat16)
    whole = lax.all_gather(result, "ctx", axis=0, tiled=True)
    return whole.reshape(rows_dev, step_count, H * HD)


def solution(mesh):
    in_specs = (
        P("row", None, None),
        P("row"),
        P(None, ("ctx", "row"), None),
        P(None, ("ctx", "row"), None),
        P(("ctx", "row"), None, None),
        P(("ctx", "row"), None, None),
        P("row", None),
        P("row"),
        P("row", None, None),
        P("row", None, None),
    )
    out_specs = P("row", None, None)
    return jax.shard_map(
        per_device, mesh=mesh, in_specs=in_specs, out_specs=out_specs, check_vma=False
    )
```

```python
import math

import jax
import jax.numpy as jnp
from jax import lax
from jax.sharding import PartitionSpec as P

H = 32
KVH = 4
HD = 128
LANES = 128


MASKED_SCORE = -1e30


def block_stats(scores, valid_mask, values, einsum_form):
    block_peak = jnp.max(jnp.where(valid_mask, scores, MASKED_SCORE), axis=-1)
    weights = jnp.where(valid_mask, jnp.exp(scores - block_peak[..., None]), 0.0).astype(
        jnp.bfloat16
    )
    block_total = jnp.sum(weights.astype(jnp.float32), axis=-1)
    block_sum = jnp.einsum(einsum_form, weights, values, preferred_element_type=jnp.float32)
    return (block_peak, block_total, block_sum)


def combine_pair(earlier, later):
    highest = jnp.maximum(earlier[0], later[0])
    left_factor = jnp.exp(earlier[0] - highest)
    right_factor = jnp.exp(later[0] - highest)
    totals = left_factor * earlier[1] + right_factor * later[1]
    sums = left_factor[..., None] * earlier[2] + right_factor[..., None] * later[2]
    return (highest, totals, sums)


def per_device(
    queries,
    prefix_id,
    prefix_keys,
    prefix_values,
    pool_keys,
    pool_values,
    page_table,
    suffix_len,
    new_keys,
    new_values,
):
    rows_dev, step_count, feature_width = queries.shape
    groups = H // KVH
    score_scale = 1.0 / math.sqrt(HD)
    row_count = lax.axis_size("row")
    ctx_count = lax.axis_size("ctx")
    row_index = lax.axis_index("row")
    ctx_index = lax.axis_index("ctx")
    flat_index = ctx_index * row_count + row_index
    own_query = queries.reshape(rows_dev, step_count, KVH, groups, HD)

    slot_count, page_len, kv_width = pool_keys.shape
    slot_ids = flat_index * slot_count + jnp.arange(slot_count, dtype=jnp.int32)
    slot_match = page_table[:, :, None] == slot_ids[None, None, :]
    entry_pos = jnp.arange(page_table.shape[1], dtype=jnp.int32)
    page_of = jnp.sum(jnp.where(slot_match, entry_pos[None, :, None], 0), axis=1)
    owned = jnp.any(slot_match, axis=1)
    token_pos = (
        page_of[:, :, None] * page_len + jnp.arange(page_len, dtype=jnp.int32)[None, None, :]
    )
    live_mask = owned[:, :, None] & (token_pos < suffix_len[:, None, None])
    live_mask = live_mask.reshape(rows_dev, 1, 1, 1, slot_count * page_len)
    flat_keys = pool_keys.reshape(slot_count * page_len, KVH, HD)
    flat_values = pool_values.reshape(slot_count * page_len, KVH, HD)
    suffix_scores = (
        jnp.einsum("rskgd,tkd->rskgt", own_query, flat_keys, preferred_element_type=jnp.float32)
        * score_scale
    )
    suffix_stats = block_stats(suffix_scores, live_mask, flat_values, "rskgt,tkd->rskgd")

    fresh_keys = new_keys.reshape(rows_dev, step_count, KVH, HD)
    fresh_values = new_values.reshape(rows_dev, step_count, KVH, HD)
    fresh_scores = (
        jnp.einsum("rskgd,rtkd->rskgt", own_query, fresh_keys, preferred_element_type=jnp.float32)
        * score_scale
    )
    causal = jnp.arange(step_count)[None, :] <= jnp.arange(step_count)[:, None]
    causal = causal.reshape(1, step_count, 1, 1, step_count)
    fresh_stats = block_stats(fresh_scores, causal, fresh_values, "rskgt,rtkd->rskgd")

    query_cols = step_count * feature_width
    id_cols = jnp.broadcast_to(prefix_id.astype(jnp.bfloat16)[:, None], (rows_dev, LANES))
    packed = jnp.concatenate([queries.reshape(rows_dev, query_cols), id_cols], axis=1)
    fanned = jnp.broadcast_to(packed[None], (row_count,) + packed.shape)
    gathered = lax.all_to_all(fanned, "row", split_axis=0, concat_axis=0, tiled=True)
    gathered = gathered.reshape(row_count * rows_dev, packed.shape[1])
    total_rows = gathered.shape[0]
    every_query = gathered[:, :query_cols].reshape(total_rows, step_count, KVH, groups, HD)
    every_prefix = gathered[:, query_cols].astype(jnp.int32)

    span_len = prefix_keys.shape[1]
    row_keys = jnp.take(prefix_keys, every_prefix, axis=0).reshape(total_rows, span_len, KVH, HD)
    row_values = jnp.take(prefix_values, every_prefix, axis=0).reshape(
        total_rows, span_len, KVH, HD
    )
    prefix_scores = (
        jnp.einsum("rskgd,rtkd->rskgt", every_query, row_keys, preferred_element_type=jnp.float32)
        * score_scale
    )
    always = jnp.ones((1, 1, 1, 1, span_len), dtype=bool)
    prefix_stats = block_stats(prefix_scores, always, row_values, "rskgt,rtkd->rskgd")

    row_start = row_index * rows_dev
    own_prefix = tuple(
        lax.dynamic_slice_in_dim(member, row_start, rows_dev, 0) for member in prefix_stats
    )
    own_merged = combine_pair(own_prefix, suffix_stats)
    peak_all, total_all, sum_all = tuple(
        lax.dynamic_update_slice_in_dim(whole_arr, piece_arr, row_start, 0)
        for whole_arr, piece_arr in zip(prefix_stats, own_merged)
    )

    units = rows_dev * step_count * H
    share = units // ctx_count
    pt_rows = -(-2 * share // LANES)
    peak_u = peak_all.reshape(row_count, ctx_count, share)
    total_u = total_all.reshape(row_count, ctx_count, share)
    sum_u = sum_all.reshape(row_count, ctx_count, share, HD)
    pt = jnp.concatenate([peak_u, total_u], axis=-1)
    pt = jnp.pad(pt, ((0, 0), (0, 0), (0, pt_rows * LANES - 2 * share)))
    pt = pt.reshape(row_count, ctx_count, pt_rows, LANES)
    outgoing = jnp.concatenate([sum_u, pt], axis=2)
    outgoing = jnp.swapaxes(outgoing, 0, 1).reshape(ctx_count * row_count, share + pt_rows, LANES)
    incoming = lax.all_to_all(
        outgoing, ("ctx", "row"), split_axis=0, concat_axis=0, tiled=True
    )
    sources = incoming.shape[0]
    got_sum = incoming[:, :share, :]
    got_pt = incoming[:, share:, :].reshape(sources, pt_rows * LANES)
    got_peak = got_pt[:, :share]
    got_total = got_pt[:, share : 2 * share]

    unit_start = ctx_index * share
    fresh_peak = lax.dynamic_slice_in_dim(fresh_stats[0].reshape(units), unit_start, share)
    fresh_total = lax.dynamic_slice_in_dim(fresh_stats[1].reshape(units), unit_start, share)
    fresh_sum = lax.dynamic_slice_in_dim(fresh_stats[2].reshape(units, HD), unit_start, share)

    top = jnp.maximum(jnp.max(got_peak, axis=0), fresh_peak)
    factor = jnp.exp(got_peak - top[None])
    fresh_factor = jnp.exp(fresh_peak - top)
    denom = jnp.sum(factor * got_total, axis=0) + fresh_factor * fresh_total
    numer = jnp.sum(factor[..., None] * got_sum, axis=0) + fresh_factor[..., None] * fresh_sum
    result = (numer / denom[..., None]).astype(jnp.bfloat16)
    whole = lax.all_gather(result, "ctx", axis=0, tiled=True)
    return whole.reshape(rows_dev, step_count, H * HD)


def solution(mesh):
    in_specs = (
        P("row", None, None),
        P("row"),
        P(None, ("ctx", "row"), None),
        P(None, ("ctx", "row"), None),
        P(("ctx", "row"), None, None),
        P(("ctx", "row"), None, None),
        P("row", None),
        P("row"),
        P("row", None, None),
        P("row", None, None),
    )
    out_specs = P("row", None, None)
    return jax.shard_map(
        per_device, mesh=mesh, in_specs=in_specs, out_specs=out_specs, check_vma=False
    )
```

```python
import math

import jax
import jax.numpy as jnp
from jax import lax
from jax.sharding import PartitionSpec as P

H = 32
KVH = 4
HD = 128
LANES = 128


MASKED_SCORE = -1e30


def block_stats(scores, valid_mask, values, einsum_form):
    block_peak = jnp.max(jnp.where(valid_mask, scores, MASKED_SCORE), axis=-1)
    weights = jnp.where(valid_mask, jnp.exp(scores - block_peak[..., None]), 0.0).astype(
        jnp.bfloat16
    )
    block_total = jnp.sum(weights.astype(jnp.float32), axis=-1)
    block_sum = jnp.einsum(einsum_form, weights, values, preferred_element_type=jnp.float32)
    return (block_peak, block_total, block_sum)


def combine_pair(earlier, later):
    highest = jnp.maximum(earlier[0], later[0])
    left_factor = jnp.exp(earlier[0] - highest)
    right_factor = jnp.exp(later[0] - highest)
    totals = left_factor * earlier[1] + right_factor * later[1]
    sums = left_factor[..., None] * earlier[2] + right_factor[..., None] * later[2]
    return (highest, totals, sums)


def per_device(
    queries,
    prefix_id,
    prefix_keys,
    prefix_values,
    pool_keys,
    pool_values,
    page_table,
    suffix_len,
    new_keys,
    new_values,
):
    rows_dev, step_count, feature_width = queries.shape
    groups = H // KVH
    score_scale = 1.0 / math.sqrt(HD)
    row_count = lax.axis_size("row")
    ctx_count = lax.axis_size("ctx")
    row_index = lax.axis_index("row")
    ctx_index = lax.axis_index("ctx")
    flat_index = ctx_index * row_count + row_index
    own_query = queries.reshape(rows_dev, step_count, KVH, groups, HD)

    slot_count, page_len, kv_width = pool_keys.shape
    slot_ids = flat_index * slot_count + jnp.arange(slot_count, dtype=jnp.int32)
    slot_match = page_table[:, :, None] == slot_ids[None, None, :]
    entry_pos = jnp.arange(page_table.shape[1], dtype=jnp.int32)
    page_of = jnp.sum(jnp.where(slot_match, entry_pos[None, :, None], 0), axis=1)
    owned = jnp.any(slot_match, axis=1)
    token_pos = (
        page_of[:, :, None] * page_len + jnp.arange(page_len, dtype=jnp.int32)[None, None, :]
    )
    live_mask = owned[:, :, None] & (token_pos < suffix_len[:, None, None])
    live_mask = live_mask.reshape(rows_dev, 1, 1, 1, slot_count * page_len)
    flat_keys = pool_keys.reshape(slot_count * page_len, KVH, HD)
    flat_values = pool_values.reshape(slot_count * page_len, KVH, HD)
    suffix_scores = (
        jnp.einsum("rskgd,tkd->rskgt", own_query, flat_keys, preferred_element_type=jnp.float32)
        * score_scale
    )
    suffix_stats = block_stats(suffix_scores, live_mask, flat_values, "rskgt,tkd->rskgd")

    fresh_keys = new_keys.reshape(rows_dev, step_count, KVH, HD)
    fresh_values = new_values.reshape(rows_dev, step_count, KVH, HD)
    fresh_scores = (
        jnp.einsum("rskgd,rtkd->rskgt", own_query, fresh_keys, preferred_element_type=jnp.float32)
        * score_scale
    )
    causal = jnp.arange(step_count)[None, :] <= jnp.arange(step_count)[:, None]
    causal = causal.reshape(1, step_count, 1, 1, step_count)
    fresh_stats = block_stats(fresh_scores, causal, fresh_values, "rskgt,rtkd->rskgd")

    query_cols = step_count * feature_width
    id_cols = jnp.broadcast_to(prefix_id.astype(jnp.bfloat16)[:, None], (rows_dev, LANES))
    packed = jnp.concatenate([queries.reshape(rows_dev, query_cols), id_cols], axis=1)
    fanned = jnp.broadcast_to(packed[None], (row_count,) + packed.shape)
    gathered = lax.all_to_all(fanned, "row", split_axis=0, concat_axis=0, tiled=True)
    gathered = gathered.reshape(row_count * rows_dev, packed.shape[1])
    total_rows = gathered.shape[0]
    every_query = gathered[:, :query_cols].reshape(total_rows, step_count, KVH, groups, HD)
    every_prefix = gathered[:, query_cols].astype(jnp.int32)

    span_len = prefix_keys.shape[1]
    row_keys = jnp.take(prefix_keys, every_prefix, axis=0).reshape(total_rows, span_len, KVH, HD)
    row_values = jnp.take(prefix_values, every_prefix, axis=0).reshape(
        total_rows, span_len, KVH, HD
    )
    prefix_scores = (
        jnp.einsum("rskgd,rtkd->rskgt", every_query, row_keys, preferred_element_type=jnp.float32)
        * score_scale
    )
    always = jnp.ones((1, 1, 1, 1, span_len), dtype=bool)
    prefix_stats = block_stats(prefix_scores, always, row_values, "rskgt,rtkd->rskgd")

    row_start = row_index * rows_dev
    own_prefix = tuple(
        lax.dynamic_slice_in_dim(member, row_start, rows_dev, 0) for member in prefix_stats
    )
    own_merged = combine_pair(own_prefix, suffix_stats)
    peak_all, total_all, sum_all = tuple(
        lax.dynamic_update_slice_in_dim(whole_arr, piece_arr, row_start, 0)
        for whole_arr, piece_arr in zip(prefix_stats, own_merged)
    )

    units = rows_dev * step_count * H
    share = units // ctx_count
    half = share // 2
    pt_rows = -(-2 * half // LANES)
    dests = ctx_count * row_count

    def by_dest(member, tail=()):
        shaped = member.reshape((row_count, ctx_count, share) + tail)
        return jnp.swapaxes(shaped, 0, 1).reshape((dests, share) + tail)

    def pack(peak, total, sums):
        pt = jnp.concatenate([peak, total], axis=-1)
        pt = jnp.pad(pt, ((0, 0), (0, pt_rows * LANES - 2 * half)))
        return jnp.concatenate([sums, pt.reshape(dests, pt_rows, LANES)], axis=1)

    def unpack(packed):
        pt = packed[:, half:, :].reshape(packed.shape[0], pt_rows * LANES)
        return (pt[:, :half], pt[:, half : 2 * half], packed[:, :half, :])

    core_bit = ctx_index % 2
    peak_d, total_d, sum_d = by_dest(peak_all), by_dest(total_all), by_dest(sum_all, (HD,))
    keep_at = core_bit * half
    give_at = (1 - core_bit) * half
    kept = tuple(
        lax.dynamic_slice_in_dim(member, keep_at, half, 1) for member in (peak_d, total_d, sum_d)
    )
    given = pack(
        *(lax.dynamic_slice_in_dim(member, give_at, half, 1) for member in (peak_d, total_d, sum_d))
    )
    partner = lax.ppermute(given, "ctx", [(c, c ^ 1) for c in range(ctx_count)])
    chip_stats = combine_pair(kept, unpack(partner))
    outgoing = pack(*chip_stats)
    incoming = lax.all_to_all(
        outgoing, ("ctx", "row"), split_axis=0, concat_axis=0, tiled=True
    )
    got_peak, got_total, got_sum = unpack(incoming)
    got_peak = got_peak.reshape(ctx_count // 2, 2, row_count, half)
    got_total = got_total.reshape(ctx_count // 2, 2, row_count, half)
    got_sum = got_sum.reshape(ctx_count // 2, 2, row_count, half, HD)
    got_peak = jnp.swapaxes(got_peak, 1, 2).reshape(dests // 2, share)
    got_total = jnp.swapaxes(got_total, 1, 2).reshape(dests // 2, share)
    got_sum = jnp.swapaxes(got_sum, 1, 2).reshape(dests // 2, share, HD)

    unit_start = ctx_index * share
    fresh_peak = lax.dynamic_slice_in_dim(fresh_stats[0].reshape(units), unit_start, share)
    fresh_total = lax.dynamic_slice_in_dim(fresh_stats[1].reshape(units), unit_start, share)
    fresh_sum = lax.dynamic_slice_in_dim(fresh_stats[2].reshape(units, HD), unit_start, share)

    top = jnp.maximum(jnp.max(got_peak, axis=0), fresh_peak)
    factor = jnp.exp(got_peak - top[None])
    fresh_factor = jnp.exp(fresh_peak - top)
    denom = jnp.sum(factor * got_total, axis=0) + fresh_factor * fresh_total
    numer = jnp.sum(factor[..., None] * got_sum, axis=0) + fresh_factor[..., None] * fresh_sum
    result = (numer / denom[..., None]).astype(jnp.bfloat16)
    whole = lax.all_gather(result, "ctx", axis=0, tiled=True)
    return whole.reshape(rows_dev, step_count, H * HD)


def solution(mesh):
    in_specs = (
        P("row", None, None),
        P("row"),
        P(None, ("ctx", "row"), None),
        P(None, ("ctx", "row"), None),
        P(("ctx", "row"), None, None),
        P(("ctx", "row"), None, None),
        P("row", None),
        P("row"),
        P("row", None, None),
        P("row", None, None),
    )
    out_specs = P("row", None, None)
    return jax.shard_map(
        per_device, mesh=mesh, in_specs=in_specs, out_specs=out_specs, check_vma=False
    )
```

```python
import math

import jax
import jax.numpy as jnp
from jax import lax
from jax.sharding import PartitionSpec as P

H = 32
KVH = 4
HD = 128
LANES = 128


MASKED_SCORE = -1e30


def block_stats(scores, valid_mask, values, einsum_form):
    block_peak = jnp.max(jnp.where(valid_mask, scores, MASKED_SCORE), axis=-1)
    weights = jnp.where(valid_mask, jnp.exp(scores - block_peak[..., None]), 0.0).astype(
        jnp.bfloat16
    )
    block_total = jnp.sum(weights.astype(jnp.float32), axis=-1)
    block_sum = jnp.einsum(einsum_form, weights, values, preferred_element_type=jnp.float32)
    return (block_peak, block_total, block_sum)


def combine_pair(earlier, later):
    highest = jnp.maximum(earlier[0], later[0])
    left_factor = jnp.exp(earlier[0] - highest)
    right_factor = jnp.exp(later[0] - highest)
    totals = left_factor * earlier[1] + right_factor * later[1]
    sums = left_factor[..., None] * earlier[2] + right_factor[..., None] * later[2]
    return (highest, totals, sums)


def per_device(
    queries,
    prefix_id,
    prefix_keys,
    prefix_values,
    pool_keys,
    pool_values,
    page_table,
    suffix_len,
    new_keys,
    new_values,
):
    rows_dev, step_count, feature_width = queries.shape
    groups = H // KVH
    score_scale = 1.0 / math.sqrt(HD)
    row_count = lax.axis_size("row")
    ctx_count = lax.axis_size("ctx")
    row_index = lax.axis_index("row")
    ctx_index = lax.axis_index("ctx")
    flat_index = ctx_index * row_count + row_index
    own_query = queries.reshape(rows_dev, step_count, KVH, groups, HD)

    slot_count, page_len, kv_width = pool_keys.shape
    slot_ids = flat_index * slot_count + jnp.arange(slot_count, dtype=jnp.int32)
    slot_match = page_table[:, :, None] == slot_ids[None, None, :]
    entry_pos = jnp.arange(page_table.shape[1], dtype=jnp.int32)
    page_of = jnp.sum(jnp.where(slot_match, entry_pos[None, :, None], 0), axis=1)
    owned = jnp.any(slot_match, axis=1)
    token_pos = (
        page_of[:, :, None] * page_len + jnp.arange(page_len, dtype=jnp.int32)[None, None, :]
    )
    live_mask = owned[:, :, None] & (token_pos < suffix_len[:, None, None])
    live_mask = live_mask.reshape(rows_dev, 1, 1, 1, slot_count * page_len)
    flat_keys = pool_keys.reshape(slot_count * page_len, KVH, HD)
    flat_values = pool_values.reshape(slot_count * page_len, KVH, HD)
    suffix_scores = (
        jnp.einsum("rskgd,tkd->rskgt", own_query, flat_keys, preferred_element_type=jnp.float32)
        * score_scale
    )
    suffix_stats = block_stats(suffix_scores, live_mask, flat_values, "rskgt,tkd->rskgd")

    fresh_keys = new_keys.reshape(rows_dev, step_count, KVH, HD)
    fresh_values = new_values.reshape(rows_dev, step_count, KVH, HD)
    fresh_scores = (
        jnp.einsum("rskgd,rtkd->rskgt", own_query, fresh_keys, preferred_element_type=jnp.float32)
        * score_scale
    )
    causal = jnp.arange(step_count)[None, :] <= jnp.arange(step_count)[:, None]
    causal = causal.reshape(1, step_count, 1, 1, step_count)
    fresh_stats = block_stats(fresh_scores, causal, fresh_values, "rskgt,rtkd->rskgd")

    query_cols = step_count * feature_width
    id_cols = jnp.broadcast_to(prefix_id.astype(jnp.bfloat16)[:, None], (rows_dev, LANES))
    packed = jnp.concatenate([queries.reshape(rows_dev, query_cols), id_cols], axis=1)
    parts = [packed] + [
        lax.ppermute(packed, "row", [(j, (j + k) % row_count) for j in range(row_count)])
        for k in range(1, row_count)
    ]
    order = (row_index - jnp.arange(row_count, dtype=jnp.int32)) % row_count
    gathered = jnp.take(jnp.stack(parts), order, axis=0)
    gathered = gathered.reshape(row_count * rows_dev, packed.shape[1])
    total_rows = gathered.shape[0]
    every_query = gathered[:, :query_cols].reshape(total_rows, step_count, KVH, groups, HD)
    every_prefix = gathered[:, query_cols].astype(jnp.int32)

    span_len = prefix_keys.shape[1]
    row_keys = jnp.take(prefix_keys, every_prefix, axis=0).reshape(total_rows, span_len, KVH, HD)
    row_values = jnp.take(prefix_values, every_prefix, axis=0).reshape(
        total_rows, span_len, KVH, HD
    )
    prefix_scores = (
        jnp.einsum("rskgd,rtkd->rskgt", every_query, row_keys, preferred_element_type=jnp.float32)
        * score_scale
    )
    always = jnp.ones((1, 1, 1, 1, span_len), dtype=bool)
    prefix_stats = block_stats(prefix_scores, always, row_values, "rskgt,rtkd->rskgd")

    row_start = row_index * rows_dev
    own_prefix = tuple(
        lax.dynamic_slice_in_dim(member, row_start, rows_dev, 0) for member in prefix_stats
    )
    own_merged = combine_pair(own_prefix, suffix_stats)
    peak_all, total_all, sum_all = tuple(
        lax.dynamic_update_slice_in_dim(whole_arr, piece_arr, row_start, 0)
        for whole_arr, piece_arr in zip(prefix_stats, own_merged)
    )

    units = rows_dev * step_count * H
    share = units // ctx_count
    half = share // 2
    pt_rows = -(-2 * half // LANES)
    dests = ctx_count * row_count

    def by_dest(member, tail=()):
        shaped = member.reshape((row_count, ctx_count, share) + tail)
        return jnp.swapaxes(shaped, 0, 1).reshape((dests, share) + tail)

    def pack(peak, total, sums):
        pt = jnp.concatenate([peak, total], axis=-1)
        pt = jnp.pad(pt, ((0, 0), (0, pt_rows * LANES - 2 * half)))
        return jnp.concatenate([sums, pt.reshape(dests, pt_rows, LANES)], axis=1)

    def unpack(packed):
        pt = packed[:, half:, :].reshape(packed.shape[0], pt_rows * LANES)
        return (pt[:, :half], pt[:, half : 2 * half], packed[:, :half, :])

    core_bit = ctx_index % 2
    peak_d, total_d, sum_d = by_dest(peak_all), by_dest(total_all), by_dest(sum_all, (HD,))
    keep_at = core_bit * half
    give_at = (1 - core_bit) * half
    kept = tuple(
        lax.dynamic_slice_in_dim(member, keep_at, half, 1) for member in (peak_d, total_d, sum_d)
    )
    given = pack(
        *(lax.dynamic_slice_in_dim(member, give_at, half, 1) for member in (peak_d, total_d, sum_d))
    )
    partner = lax.ppermute(given, "ctx", [(c, c ^ 1) for c in range(ctx_count)])
    chip_stats = combine_pair(kept, unpack(partner))
    outgoing = pack(*chip_stats)
    incoming = lax.all_to_all(
        outgoing, ("ctx", "row"), split_axis=0, concat_axis=0, tiled=True
    )
    got_peak, got_total, got_sum = unpack(incoming)
    got_peak = got_peak.reshape(ctx_count // 2, 2, row_count, half)
    got_total = got_total.reshape(ctx_count // 2, 2, row_count, half)
    got_sum = got_sum.reshape(ctx_count // 2, 2, row_count, half, HD)
    got_peak = jnp.swapaxes(got_peak, 1, 2).reshape(dests // 2, share)
    got_total = jnp.swapaxes(got_total, 1, 2).reshape(dests // 2, share)
    got_sum = jnp.swapaxes(got_sum, 1, 2).reshape(dests // 2, share, HD)

    unit_start = ctx_index * share
    fresh_peak = lax.dynamic_slice_in_dim(fresh_stats[0].reshape(units), unit_start, share)
    fresh_total = lax.dynamic_slice_in_dim(fresh_stats[1].reshape(units), unit_start, share)
    fresh_sum = lax.dynamic_slice_in_dim(fresh_stats[2].reshape(units, HD), unit_start, share)

    top = jnp.maximum(jnp.max(got_peak, axis=0), fresh_peak)
    factor = jnp.exp(got_peak - top[None])
    fresh_factor = jnp.exp(fresh_peak - top)
    denom = jnp.sum(factor * got_total, axis=0) + fresh_factor * fresh_total
    numer = jnp.sum(factor[..., None] * got_sum, axis=0) + fresh_factor[..., None] * fresh_sum
    result = (numer / denom[..., None]).astype(jnp.bfloat16)
    if share % H == 0:
        result = result.reshape(share // H, H * HD)
    whole = lax.all_gather(result, "ctx", axis=0, tiled=True)
    return whole.reshape(rows_dev, step_count, H * HD)


def solution(mesh):
    in_specs = (
        P("row", None, None),
        P("row"),
        P(None, ("ctx", "row"), None),
        P(None, ("ctx", "row"), None),
        P(("ctx", "row"), None, None),
        P(("ctx", "row"), None, None),
        P("row", None),
        P("row"),
        P("row", None, None),
        P("row", None, None),
    )
    out_specs = P("row", None, None)
    return jax.shard_map(
        per_device, mesh=mesh, in_specs=in_specs, out_specs=out_specs, check_vma=False
    )
```

```python
import math

import jax
import jax.numpy as jnp
from jax import lax
from jax.sharding import PartitionSpec as P

H = 32
KVH = 4
HD = 128
LANES = 128


MASKED_SCORE = -1e30


def block_stats(scores, valid_mask, values, einsum_form):
    block_peak = jnp.max(jnp.where(valid_mask, scores, MASKED_SCORE), axis=-1)
    weights = jnp.where(valid_mask, jnp.exp(scores - block_peak[..., None]), 0.0).astype(
        jnp.bfloat16
    )
    block_total = jnp.sum(weights.astype(jnp.float32), axis=-1)
    block_sum = jnp.einsum(einsum_form, weights, values, preferred_element_type=jnp.float32)
    return (block_peak, block_total, block_sum)


def combine_pair(earlier, later):
    highest = jnp.maximum(earlier[0], later[0])
    left_factor = jnp.exp(earlier[0] - highest)
    right_factor = jnp.exp(later[0] - highest)
    totals = left_factor * earlier[1] + right_factor * later[1]
    sums = left_factor[..., None] * earlier[2] + right_factor[..., None] * later[2]
    return (highest, totals, sums)


def per_device(
    queries,
    prefix_id,
    prefix_keys,
    prefix_values,
    pool_keys,
    pool_values,
    page_table,
    suffix_len,
    new_keys,
    new_values,
):
    rows_dev, step_count, feature_width = queries.shape
    groups = H // KVH
    score_scale = 1.0 / math.sqrt(HD)
    row_count = lax.axis_size("row")
    ctx_count = lax.axis_size("ctx")
    row_index = lax.axis_index("row")
    ctx_index = lax.axis_index("ctx")
    flat_index = ctx_index * row_count + row_index
    own_query = queries.reshape(rows_dev, step_count, KVH, groups, HD)

    slot_count, page_len, kv_width = pool_keys.shape
    slot_ids = flat_index * slot_count + jnp.arange(slot_count, dtype=jnp.int32)
    slot_match = page_table[:, :, None] == slot_ids[None, None, :]
    entry_pos = jnp.arange(page_table.shape[1], dtype=jnp.int32)
    page_of = jnp.sum(jnp.where(slot_match, entry_pos[None, :, None], 0), axis=1)
    owned = jnp.any(slot_match, axis=1)
    token_pos = (
        page_of[:, :, None] * page_len + jnp.arange(page_len, dtype=jnp.int32)[None, None, :]
    )
    live_mask = owned[:, :, None] & (token_pos < suffix_len[:, None, None])
    live_mask = live_mask.reshape(rows_dev, 1, 1, 1, slot_count * page_len)
    flat_keys = pool_keys.reshape(slot_count * page_len, KVH, HD)
    flat_values = pool_values.reshape(slot_count * page_len, KVH, HD)
    suffix_scores = (
        jnp.einsum("rskgd,tkd->rskgt", own_query, flat_keys, preferred_element_type=jnp.float32)
        * score_scale
    )
    suffix_stats = block_stats(suffix_scores, live_mask, flat_values, "rskgt,tkd->rskgd")

    fresh_keys = new_keys.reshape(rows_dev, step_count, KVH, HD)
    fresh_values = new_values.reshape(rows_dev, step_count, KVH, HD)
    fresh_scores = (
        jnp.einsum("rskgd,rtkd->rskgt", own_query, fresh_keys, preferred_element_type=jnp.float32)
        * score_scale
    )
    causal = jnp.arange(step_count)[None, :] <= jnp.arange(step_count)[:, None]
    causal = causal.reshape(1, step_count, 1, 1, step_count)
    fresh_stats = block_stats(fresh_scores, causal, fresh_values, "rskgt,rtkd->rskgd")

    query_rows = rows_dev * step_count * feature_width // LANES
    id_rows = -(-rows_dev // 16) * 16
    id_block = jnp.zeros((id_rows, LANES), jnp.bfloat16)
    id_block = id_block.at[:rows_dev, :].set(
        jnp.broadcast_to(prefix_id.astype(jnp.bfloat16)[:, None], (rows_dev, LANES))
    )
    packed = jnp.concatenate([queries.reshape(query_rows, LANES), id_block], axis=0)
    fanned = jnp.broadcast_to(packed[None], (row_count,) + packed.shape)
    gathered = lax.all_to_all(fanned, "row", split_axis=0, concat_axis=0, tiled=True)
    total_rows = row_count * rows_dev
    every_query = gathered[:, :query_rows, :].reshape(total_rows, step_count, KVH, groups, HD)
    every_prefix = gathered[:, query_rows : query_rows + rows_dev, 0].reshape(total_rows)
    every_prefix = every_prefix.astype(jnp.int32)

    span_len = prefix_keys.shape[1]
    row_keys = jnp.take(prefix_keys, every_prefix, axis=0).reshape(total_rows, span_len, KVH, HD)
    row_values = jnp.take(prefix_values, every_prefix, axis=0).reshape(
        total_rows, span_len, KVH, HD
    )
    prefix_scores = (
        jnp.einsum("rskgd,rtkd->rskgt", every_query, row_keys, preferred_element_type=jnp.float32)
        * score_scale
    )
    always = jnp.ones((1, 1, 1, 1, span_len), dtype=bool)
    prefix_stats = block_stats(prefix_scores, always, row_values, "rskgt,rtkd->rskgd")

    row_start = row_index * rows_dev
    own_prefix = tuple(
        lax.dynamic_slice_in_dim(member, row_start, rows_dev, 0) for member in prefix_stats
    )
    own_merged = combine_pair(own_prefix, suffix_stats)
    peak_all, total_all, sum_all = tuple(
        lax.dynamic_update_slice_in_dim(whole_arr, piece_arr, row_start, 0)
        for whole_arr, piece_arr in zip(prefix_stats, own_merged)
    )

    units = rows_dev * step_count * H
    share = units // ctx_count
    half = share // 2
    pt_rows = -(-2 * half // LANES)
    dests = ctx_count * row_count

    def by_dest(member, tail=()):
        shaped = member.reshape((row_count, ctx_count, share) + tail)
        return jnp.swapaxes(shaped, 0, 1).reshape((dests, share) + tail)

    def pack(peak, total, sums):
        pt = jnp.concatenate([peak, total], axis=-1)
        pt = jnp.pad(pt, ((0, 0), (0, pt_rows * LANES - 2 * half)))
        return jnp.concatenate([sums, pt.reshape(dests, pt_rows, LANES)], axis=1)

    def unpack(packed):
        pt = packed[:, half:, :].reshape(packed.shape[0], pt_rows * LANES)
        return (pt[:, :half], pt[:, half : 2 * half], packed[:, :half, :])

    core_bit = ctx_index % 2
    peak_d, total_d, sum_d = by_dest(peak_all), by_dest(total_all), by_dest(sum_all, (HD,))
    keep_at = core_bit * half
    give_at = (1 - core_bit) * half
    kept = tuple(
        lax.dynamic_slice_in_dim(member, keep_at, half, 1) for member in (peak_d, total_d, sum_d)
    )
    given = pack(
        *(lax.dynamic_slice_in_dim(member, give_at, half, 1) for member in (peak_d, total_d, sum_d))
    )
    partner = lax.ppermute(given, "ctx", [(c, c ^ 1) for c in range(ctx_count)])
    chip_stats = combine_pair(kept, unpack(partner))
    outgoing = pack(*chip_stats)
    incoming = lax.all_to_all(
        outgoing, ("ctx", "row"), split_axis=0, concat_axis=0, tiled=True
    )
    got_peak, got_total, got_sum = unpack(incoming)
    got_peak = got_peak.reshape(ctx_count // 2, 2, row_count, half)
    got_total = got_total.reshape(ctx_count // 2, 2, row_count, half)
    got_sum = got_sum.reshape(ctx_count // 2, 2, row_count, half, HD)
    got_peak = jnp.swapaxes(got_peak, 1, 2).reshape(dests // 2, share)
    got_total = jnp.swapaxes(got_total, 1, 2).reshape(dests // 2, share)
    got_sum = jnp.swapaxes(got_sum, 1, 2).reshape(dests // 2, share, HD)

    unit_start = ctx_index * share
    fresh_peak = lax.dynamic_slice_in_dim(fresh_stats[0].reshape(units), unit_start, share)
    fresh_total = lax.dynamic_slice_in_dim(fresh_stats[1].reshape(units), unit_start, share)
    fresh_sum = lax.dynamic_slice_in_dim(fresh_stats[2].reshape(units, HD), unit_start, share)

    top = jnp.maximum(jnp.max(got_peak, axis=0), fresh_peak)
    factor = jnp.exp(got_peak - top[None])
    fresh_factor = jnp.exp(fresh_peak - top)
    denom = jnp.sum(factor * got_total, axis=0) + fresh_factor * fresh_total
    numer = jnp.sum(factor[..., None] * got_sum, axis=0) + fresh_factor[..., None] * fresh_sum
    result = (numer / denom[..., None]).astype(jnp.bfloat16)
    whole = lax.all_gather(result, "ctx", axis=0, tiled=True)
    return whole.reshape(rows_dev, step_count, H * HD)


def solution(mesh):
    in_specs = (
        P("row", None, None),
        P("row"),
        P(None, ("ctx", "row"), None),
        P(None, ("ctx", "row"), None),
        P(("ctx", "row"), None, None),
        P(("ctx", "row"), None, None),
        P("row", None),
        P("row"),
        P("row", None, None),
        P("row", None, None),
    )
    out_specs = P("row", None, None)
    return jax.shard_map(
        per_device, mesh=mesh, in_specs=in_specs, out_specs=out_specs, check_vma=False
    )
```

```python
import math

import jax
import jax.numpy as jnp
from jax import lax
from jax.sharding import PartitionSpec as P

H = 32
KVH = 4
HD = 128
LANES = 128


MASKED_SCORE = -1e30


def block_stats(scores, valid_mask, values, einsum_form):
    block_peak = jnp.max(jnp.where(valid_mask, scores, MASKED_SCORE), axis=-1)
    weights = jnp.where(valid_mask, jnp.exp(scores - block_peak[..., None]), 0.0).astype(
        jnp.bfloat16
    )
    block_total = jnp.sum(weights.astype(jnp.float32), axis=-1)
    block_sum = jnp.einsum(einsum_form, weights, values, preferred_element_type=jnp.float32)
    return (block_peak, block_total, block_sum)


def combine_pair(earlier, later):
    highest = jnp.maximum(earlier[0], later[0])
    left_factor = jnp.exp(earlier[0] - highest)
    right_factor = jnp.exp(later[0] - highest)
    totals = left_factor * earlier[1] + right_factor * later[1]
    sums = left_factor[..., None] * earlier[2] + right_factor[..., None] * later[2]
    return (highest, totals, sums)


def per_device(
    queries,
    prefix_id,
    prefix_keys,
    prefix_values,
    pool_keys,
    pool_values,
    page_table,
    suffix_len,
    new_keys,
    new_values,
):
    rows_dev, step_count, feature_width = queries.shape
    groups = H // KVH
    score_scale = 1.0 / math.sqrt(HD)
    row_count = lax.axis_size("row")
    ctx_count = lax.axis_size("ctx")
    row_index = lax.axis_index("row")
    ctx_index = lax.axis_index("ctx")
    flat_index = ctx_index * row_count + row_index
    own_query = queries.reshape(rows_dev, step_count, KVH, groups, HD)

    slot_count, page_len, kv_width = pool_keys.shape
    slot_ids = flat_index * slot_count + jnp.arange(slot_count, dtype=jnp.int32)
    slot_match = page_table[:, :, None] == slot_ids[None, None, :]
    entry_pos = jnp.arange(page_table.shape[1], dtype=jnp.int32)
    page_of = jnp.sum(jnp.where(slot_match, entry_pos[None, :, None], 0), axis=1)
    owned = jnp.any(slot_match, axis=1)
    token_pos = (
        page_of[:, :, None] * page_len + jnp.arange(page_len, dtype=jnp.int32)[None, None, :]
    )
    live_mask = owned[:, :, None] & (token_pos < suffix_len[:, None, None])
    live_mask = live_mask.reshape(rows_dev, 1, 1, 1, slot_count * page_len)
    flat_keys = pool_keys.reshape(slot_count * page_len, KVH, HD)
    flat_values = pool_values.reshape(slot_count * page_len, KVH, HD)
    suffix_scores = (
        jnp.einsum("rskgd,tkd->rskgt", own_query, flat_keys, preferred_element_type=jnp.float32)
        * score_scale
    )
    suffix_stats = block_stats(suffix_scores, live_mask, flat_values, "rskgt,tkd->rskgd")

    fresh_keys = new_keys.reshape(rows_dev, step_count, KVH, HD)
    fresh_values = new_values.reshape(rows_dev, step_count, KVH, HD)
    fresh_scores = (
        jnp.einsum("rskgd,rtkd->rskgt", own_query, fresh_keys, preferred_element_type=jnp.float32)
        * score_scale
    )
    causal = jnp.arange(step_count)[None, :] <= jnp.arange(step_count)[:, None]
    causal = causal.reshape(1, step_count, 1, 1, step_count)
    fresh_stats = block_stats(fresh_scores, causal, fresh_values, "rskgt,rtkd->rskgd")

    query_rows = rows_dev * step_count * feature_width // LANES
    id_rows = -(-rows_dev // 16) * 16
    id_block = jnp.zeros((id_rows, LANES), jnp.bfloat16)
    id_block = id_block.at[:rows_dev, :].set(
        jnp.broadcast_to(prefix_id.astype(jnp.bfloat16)[:, None], (rows_dev, LANES))
    )
    packed = jnp.concatenate([queries.reshape(query_rows, LANES), id_block], axis=0)
    fanned = jnp.broadcast_to(packed[None], (row_count,) + packed.shape)
    gathered = lax.all_to_all(fanned, "row", split_axis=0, concat_axis=0, tiled=True)
    total_rows = row_count * rows_dev
    every_query = gathered[:, :query_rows, :].reshape(total_rows, step_count, KVH, groups, HD)
    every_prefix = gathered[:, query_rows : query_rows + rows_dev, 0].reshape(total_rows)
    every_prefix = every_prefix.astype(jnp.int32)

    core_bit = ctx_index % 2
    half_kv = KVH // 2
    half_heads = H // 2
    swap = [(c, c ^ 1) for c in range(ctx_count)]
    span_len = prefix_keys.shape[1]
    prefix_count = prefix_keys.shape[0]
    kv_both = jnp.stack(
        [
            prefix_keys.reshape(prefix_count, span_len, KVH, HD),
            prefix_values.reshape(prefix_count, span_len, KVH, HD),
        ]
    )
    own_kv = lax.dynamic_slice_in_dim(kv_both, core_bit * half_kv, half_kv, 3)
    given_kv = lax.dynamic_slice_in_dim(kv_both, (1 - core_bit) * half_kv, half_kv, 3)
    partner_kv = lax.ppermute(given_kv, "ctx", swap)

    half_query = lax.dynamic_slice_in_dim(every_query, core_bit * half_kv, half_kv, 2)

    def prefix_block(kv):
        row_keys = jnp.take(kv[0], every_prefix, axis=0)
        row_values = jnp.take(kv[1], every_prefix, axis=0)
        scores = (
            jnp.einsum(
                "rskgd,rtkd->rskgt", half_query, row_keys, preferred_element_type=jnp.float32
            )
            * score_scale
        )
        always = jnp.ones((1, 1, 1, 1, span_len), dtype=bool)
        return block_stats(scores, always, row_values, "rskgt,rtkd->rskgd")

    prefix_stats = combine_pair(prefix_block(own_kv), prefix_block(partner_kv))

    def head_half(member, at):
        return lax.dynamic_slice_in_dim(member, at * half_kv, half_kv, 2)

    suffix_packed = jnp.concatenate(
        [suffix_stats[2], suffix_stats[0][..., None], suffix_stats[1][..., None]], axis=-1
    )
    suffix_moved = lax.ppermute(head_half(suffix_packed, 1 - core_bit), "ctx", swap)
    suffix_partner = (suffix_moved[..., HD], suffix_moved[..., HD + 1], suffix_moved[..., :HD])
    suffix_kept = tuple(head_half(member, core_bit) for member in suffix_stats)
    suffix_half = combine_pair(suffix_kept, suffix_partner)

    row_start = row_index * rows_dev
    own_prefix = tuple(
        lax.dynamic_slice_in_dim(member, row_start, rows_dev, 0) for member in prefix_stats
    )
    own_merged = combine_pair(own_prefix, suffix_half)
    peak_all, total_all, sum_all = tuple(
        lax.dynamic_update_slice_in_dim(whole_arr, piece_arr, row_start, 0)
        for whole_arr, piece_arr in zip(prefix_stats, own_merged)
    )

    half_units = rows_dev * step_count * half_heads
    chunk = half_units // ctx_count
    pt_rows = -(-2 * chunk // LANES)
    dests = ctx_count * row_count

    def by_dest(member, tail=()):
        shaped = member.reshape((row_count, ctx_count, chunk) + tail)
        return jnp.swapaxes(shaped, 0, 1).reshape((dests, chunk) + tail)

    pt = jnp.concatenate([by_dest(peak_all), by_dest(total_all)], axis=-1)
    pt = jnp.pad(pt, ((0, 0), (0, pt_rows * LANES - 2 * chunk)))
    outgoing = jnp.concatenate(
        [by_dest(sum_all, (HD,)), pt.reshape(dests, pt_rows, LANES)], axis=1
    )
    incoming = lax.all_to_all(
        outgoing, ("ctx", "row"), split_axis=0, concat_axis=0, tiled=True
    )
    got_pt = incoming[:, chunk:, :].reshape(dests, pt_rows * LANES)
    pairs = ctx_count // 2

    def by_half(member, tail=()):
        shaped = member.reshape((pairs, 2, row_count, chunk) + tail)
        return jnp.swapaxes(shaped, 0, 1).reshape((2, pairs * row_count, chunk) + tail)

    got_peak = by_half(got_pt[:, :chunk])
    got_total = by_half(got_pt[:, chunk : 2 * chunk])
    got_sum = by_half(incoming[:, :chunk, :], (HD,))

    def fresh_chunk(member, tail=()):
        shaped = member.reshape((rows_dev, step_count, 2, half_heads) + tail)
        shaped = jnp.moveaxis(shaped, 2, 0).reshape((2, half_units) + tail)
        return lax.dynamic_slice_in_dim(shaped, ctx_index * chunk, chunk, 1)

    fresh_peak = fresh_chunk(fresh_stats[0])
    fresh_total = fresh_chunk(fresh_stats[1])
    fresh_sum = fresh_chunk(fresh_stats[2], (HD,))

    top = jnp.maximum(jnp.max(got_peak, axis=1), fresh_peak)
    factor = jnp.exp(got_peak - top[:, None])
    fresh_factor = jnp.exp(fresh_peak - top)
    denom = jnp.sum(factor * got_total, axis=1) + fresh_factor * fresh_total
    numer = jnp.sum(factor[..., None] * got_sum, axis=1) + fresh_factor[..., None] * fresh_sum
    result = (numer / denom[..., None]).astype(jnp.bfloat16)
    whole = lax.all_gather(result, "ctx", axis=0, tiled=False)
    whole = jnp.swapaxes(whole, 0, 1).reshape(2, rows_dev, step_count, half_heads, HD)
    whole = jnp.moveaxis(whole, 0, 2)
    return whole.reshape(rows_dev, step_count, H * HD)


def solution(mesh):
    in_specs = (
        P("row", None, None),
        P("row"),
        P(None, ("ctx", "row"), None),
        P(None, ("ctx", "row"), None),
        P(("ctx", "row"), None, None),
        P(("ctx", "row"), None, None),
        P("row", None),
        P("row"),
        P("row", None, None),
        P("row", None, None),
    )
    out_specs = P("row", None, None)
    return jax.shard_map(
        per_device, mesh=mesh, in_specs=in_specs, out_specs=out_specs, check_vma=False
    )
```

```python
import math

import jax
import jax.numpy as jnp
from jax import lax
from jax.sharding import PartitionSpec as P

H = 32
KVH = 4
HD = 128
LANES = 128


MASKED_SCORE = -1e30


def block_stats(scores, valid_mask, values, einsum_form):
    block_peak = jnp.max(jnp.where(valid_mask, scores, MASKED_SCORE), axis=-1)
    weights = jnp.where(valid_mask, jnp.exp(scores - block_peak[..., None]), 0.0).astype(
        jnp.bfloat16
    )
    block_total = jnp.sum(weights.astype(jnp.float32), axis=-1)
    block_sum = jnp.einsum(einsum_form, weights, values, preferred_element_type=jnp.float32)
    return (block_peak, block_total, block_sum)


def combine_pair(earlier, later):
    highest = jnp.maximum(earlier[0], later[0])
    left_factor = jnp.exp(earlier[0] - highest)
    right_factor = jnp.exp(later[0] - highest)
    totals = left_factor * earlier[1] + right_factor * later[1]
    sums = left_factor[..., None] * earlier[2] + right_factor[..., None] * later[2]
    return (highest, totals, sums)


def per_device(
    queries,
    prefix_id,
    prefix_keys,
    prefix_values,
    pool_keys,
    pool_values,
    page_table,
    suffix_len,
    new_keys,
    new_values,
):
    rows_dev, step_count, feature_width = queries.shape
    groups = H // KVH
    score_scale = 1.0 / math.sqrt(HD)
    row_count = lax.axis_size("row")
    ctx_count = lax.axis_size("ctx")
    row_index = lax.axis_index("row")
    ctx_index = lax.axis_index("ctx")
    flat_index = ctx_index * row_count + row_index
    own_query = queries.reshape(rows_dev, step_count, KVH, groups, HD)

    slot_count, page_len, kv_width = pool_keys.shape
    slot_ids = flat_index * slot_count + jnp.arange(slot_count, dtype=jnp.int32)
    slot_match = page_table[:, :, None] == slot_ids[None, None, :]
    entry_pos = jnp.arange(page_table.shape[1], dtype=jnp.int32)
    page_of = jnp.sum(jnp.where(slot_match, entry_pos[None, :, None], 0), axis=1)
    owned = jnp.any(slot_match, axis=1)
    token_pos = (
        page_of[:, :, None] * page_len + jnp.arange(page_len, dtype=jnp.int32)[None, None, :]
    )
    live_mask = owned[:, :, None] & (token_pos < suffix_len[:, None, None])
    live_mask = live_mask.reshape(rows_dev, 1, 1, 1, slot_count * page_len)
    flat_keys = pool_keys.reshape(slot_count * page_len, KVH, HD)
    flat_values = pool_values.reshape(slot_count * page_len, KVH, HD)
    suffix_scores = (
        jnp.einsum("rskgd,tkd->rskgt", own_query, flat_keys, preferred_element_type=jnp.float32)
        * score_scale
    )
    suffix_stats = block_stats(suffix_scores, live_mask, flat_values, "rskgt,tkd->rskgd")

    fresh_keys = new_keys.reshape(rows_dev, step_count, KVH, HD)
    fresh_values = new_values.reshape(rows_dev, step_count, KVH, HD)
    fresh_scores = (
        jnp.einsum("rskgd,rtkd->rskgt", own_query, fresh_keys, preferred_element_type=jnp.float32)
        * score_scale
    )
    causal = jnp.arange(step_count)[None, :] <= jnp.arange(step_count)[:, None]
    causal = causal.reshape(1, step_count, 1, 1, step_count)
    fresh_stats = block_stats(fresh_scores, causal, fresh_values, "rskgt,rtkd->rskgd")

    query_rows = rows_dev * step_count * feature_width // LANES
    id_rows = -(-rows_dev // 16) * 16
    id_block = jnp.zeros((id_rows, LANES), jnp.bfloat16)
    id_block = id_block.at[:rows_dev, :].set(
        jnp.broadcast_to(prefix_id.astype(jnp.bfloat16)[:, None], (rows_dev, LANES))
    )
    packed = jnp.concatenate([queries.reshape(query_rows, LANES), id_block], axis=0)
    fanned = jnp.broadcast_to(packed[None], (row_count,) + packed.shape)
    gathered = lax.all_to_all(fanned, "row", split_axis=0, concat_axis=0, tiled=True)
    total_rows = row_count * rows_dev
    every_query = gathered[:, :query_rows, :].reshape(total_rows, step_count, KVH, groups, HD)
    every_prefix = gathered[:, query_rows : query_rows + rows_dev, 0].reshape(total_rows)
    every_prefix = every_prefix.astype(jnp.int32)

    core_bit = ctx_index % 2
    half_kv = KVH // 2
    half_heads = H // 2
    swap = [(c, c ^ 1) for c in range(ctx_count)]
    span_len = prefix_keys.shape[1]
    prefix_count = prefix_keys.shape[0]
    kv_both = jnp.stack(
        [
            prefix_keys.reshape(prefix_count, span_len, KVH, HD),
            prefix_values.reshape(prefix_count, span_len, KVH, HD),
        ]
    )
    own_kv = lax.dynamic_slice_in_dim(kv_both, core_bit * half_kv, half_kv, 3)
    given_kv = lax.dynamic_slice_in_dim(kv_both, (1 - core_bit) * half_kv, half_kv, 3)
    partner_kv = lax.ppermute(given_kv, "ctx", swap)

    half_query = lax.dynamic_slice_in_dim(every_query, core_bit * half_kv, half_kv, 2)

    def prefix_block(kv):
        row_keys = jnp.take(kv[0], every_prefix, axis=0)
        row_values = jnp.take(kv[1], every_prefix, axis=0)
        scores = (
            jnp.einsum(
                "rskgd,rtkd->rskgt", half_query, row_keys, preferred_element_type=jnp.float32
            )
            * score_scale
        )
        always = jnp.ones((1, 1, 1, 1, span_len), dtype=bool)
        return block_stats(scores, always, row_values, "rskgt,rtkd->rskgd")

    prefix_stats = combine_pair(prefix_block(own_kv), prefix_block(partner_kv))

    def head_half(member, at):
        return lax.dynamic_slice_in_dim(member, at * half_kv, half_kv, 2)

    suffix_packed = jnp.concatenate(
        [suffix_stats[2], suffix_stats[0][..., None], suffix_stats[1][..., None]], axis=-1
    )
    suffix_moved = lax.ppermute(head_half(suffix_packed, 1 - core_bit), "ctx", swap)
    suffix_partner = (suffix_moved[..., HD], suffix_moved[..., HD + 1], suffix_moved[..., :HD])
    suffix_kept = tuple(head_half(member, core_bit) for member in suffix_stats)
    suffix_half = combine_pair(suffix_kept, suffix_partner)

    row_start = row_index * rows_dev
    own_prefix = tuple(
        lax.dynamic_slice_in_dim(member, row_start, rows_dev, 0) for member in prefix_stats
    )
    own_merged = combine_pair(own_prefix, suffix_half)
    peak_all, total_all, sum_all = tuple(
        lax.dynamic_update_slice_in_dim(whole_arr, piece_arr, row_start, 0)
        for whole_arr, piece_arr in zip(prefix_stats, own_merged)
    )

    half_units = rows_dev * step_count * half_heads
    chunk = half_units // ctx_count
    pt_rows = -(-2 * chunk // LANES)
    dests = ctx_count * row_count

    def by_dest(member, tail=()):
        shaped = member.reshape((row_count, ctx_count, chunk) + tail)
        return jnp.swapaxes(shaped, 0, 1).reshape((dests, chunk) + tail)

    pt = jnp.concatenate([by_dest(peak_all), by_dest(total_all)], axis=-1)
    pt = jnp.pad(pt, ((0, 0), (0, pt_rows * LANES - 2 * chunk)))
    outgoing = jnp.concatenate(
        [by_dest(sum_all, (HD,)), pt.reshape(dests, pt_rows, LANES)], axis=1
    )
    incoming = lax.all_to_all(
        outgoing.reshape(dests, 1, (chunk + pt_rows) * LANES),
        ("ctx", "row"),
        split_axis=0,
        concat_axis=0,
        tiled=True,
    )
    incoming = incoming.reshape(dests, chunk + pt_rows, LANES)
    got_pt = incoming[:, chunk:, :].reshape(dests, pt_rows * LANES)
    pairs = ctx_count // 2

    def by_half(member, tail=()):
        shaped = member.reshape((pairs, 2, row_count, chunk) + tail)
        return jnp.swapaxes(shaped, 0, 1).reshape((2, pairs * row_count, chunk) + tail)

    got_peak = by_half(got_pt[:, :chunk])
    got_total = by_half(got_pt[:, chunk : 2 * chunk])
    got_sum = by_half(incoming[:, :chunk, :], (HD,))

    def fresh_chunk(member, tail=()):
        shaped = member.reshape((rows_dev, step_count, 2, half_heads) + tail)
        shaped = jnp.moveaxis(shaped, 2, 0).reshape((2, half_units) + tail)
        return lax.dynamic_slice_in_dim(shaped, ctx_index * chunk, chunk, 1)

    fresh_peak = fresh_chunk(fresh_stats[0])
    fresh_total = fresh_chunk(fresh_stats[1])
    fresh_sum = fresh_chunk(fresh_stats[2], (HD,))

    top = jnp.maximum(jnp.max(got_peak, axis=1), fresh_peak)
    factor = jnp.exp(got_peak - top[:, None])
    fresh_factor = jnp.exp(fresh_peak - top)
    denom = jnp.sum(factor * got_total, axis=1) + fresh_factor * fresh_total
    numer = jnp.sum(factor[..., None] * got_sum, axis=1) + fresh_factor[..., None] * fresh_sum
    result = (numer / denom[..., None]).astype(jnp.bfloat16)
    whole = lax.all_gather(result, "ctx", axis=0, tiled=False)
    whole = jnp.swapaxes(whole, 0, 1).reshape(2, rows_dev, step_count, half_heads, HD)
    whole = jnp.moveaxis(whole, 0, 2)
    return whole.reshape(rows_dev, step_count, H * HD)


def solution(mesh):
    in_specs = (
        P("row", None, None),
        P("row"),
        P(None, ("ctx", "row"), None),
        P(None, ("ctx", "row"), None),
        P(("ctx", "row"), None, None),
        P(("ctx", "row"), None, None),
        P("row", None),
        P("row"),
        P("row", None, None),
        P("row", None, None),
    )
    out_specs = P("row", None, None)
    return jax.shard_map(
        per_device, mesh=mesh, in_specs=in_specs, out_specs=out_specs, check_vma=False
    )
```

```python
import math

import jax
import jax.numpy as jnp
from jax import lax
from jax.sharding import PartitionSpec as P

H = 32
KVH = 4
HD = 128
LANES = 128


MASKED_SCORE = -1e30


def block_stats(scores, valid_mask, values, einsum_form):
    block_peak = jnp.max(jnp.where(valid_mask, scores, MASKED_SCORE), axis=-1)
    weights = jnp.where(valid_mask, jnp.exp(scores - block_peak[..., None]), 0.0).astype(
        jnp.bfloat16
    )
    block_total = jnp.sum(weights.astype(jnp.float32), axis=-1)
    block_sum = jnp.einsum(einsum_form, weights, values, preferred_element_type=jnp.float32)
    return (block_peak, block_total, block_sum)


def combine_pair(earlier, later):
    highest = jnp.maximum(earlier[0], later[0])
    left_factor = jnp.exp(earlier[0] - highest)
    right_factor = jnp.exp(later[0] - highest)
    totals = left_factor * earlier[1] + right_factor * later[1]
    sums = left_factor[..., None] * earlier[2] + right_factor[..., None] * later[2]
    return (highest, totals, sums)


def per_device(
    queries,
    prefix_id,
    prefix_keys,
    prefix_values,
    pool_keys,
    pool_values,
    page_table,
    suffix_len,
    new_keys,
    new_values,
):
    rows_dev, step_count, feature_width = queries.shape
    groups = H // KVH
    score_scale = 1.0 / math.sqrt(HD)
    row_count = lax.axis_size("row")
    ctx_count = lax.axis_size("ctx")
    row_index = lax.axis_index("row")
    ctx_index = lax.axis_index("ctx")
    flat_index = ctx_index * row_count + row_index
    own_query = queries.reshape(rows_dev, step_count, KVH, groups, HD)

    slot_count, page_len, kv_width = pool_keys.shape
    slot_ids = flat_index * slot_count + jnp.arange(slot_count, dtype=jnp.int32)
    slot_match = page_table[:, :, None] == slot_ids[None, None, :]
    entry_pos = jnp.arange(page_table.shape[1], dtype=jnp.int32)
    page_of = jnp.sum(jnp.where(slot_match, entry_pos[None, :, None], 0), axis=1)
    owned = jnp.any(slot_match, axis=1)
    token_pos = (
        page_of[:, :, None] * page_len + jnp.arange(page_len, dtype=jnp.int32)[None, None, :]
    )
    live_mask = owned[:, :, None] & (token_pos < suffix_len[:, None, None])
    live_mask = live_mask.reshape(rows_dev, 1, 1, 1, slot_count * page_len)
    flat_keys = pool_keys.reshape(slot_count * page_len, KVH, HD)
    flat_values = pool_values.reshape(slot_count * page_len, KVH, HD)
    suffix_scores = (
        jnp.einsum("rskgd,tkd->rskgt", own_query, flat_keys, preferred_element_type=jnp.float32)
        * score_scale
    )
    suffix_stats = block_stats(suffix_scores, live_mask, flat_values, "rskgt,tkd->rskgd")

    fresh_keys = new_keys.reshape(rows_dev, step_count, KVH, HD)
    fresh_values = new_values.reshape(rows_dev, step_count, KVH, HD)
    fresh_scores = (
        jnp.einsum("rskgd,rtkd->rskgt", own_query, fresh_keys, preferred_element_type=jnp.float32)
        * score_scale
    )
    causal = jnp.arange(step_count)[None, :] <= jnp.arange(step_count)[:, None]
    causal = causal.reshape(1, step_count, 1, 1, step_count)
    fresh_stats = block_stats(fresh_scores, causal, fresh_values, "rskgt,rtkd->rskgd")

    query_rows = rows_dev * step_count * feature_width // LANES
    id_rows = -(-rows_dev // 16) * 16
    id_block = jnp.zeros((id_rows, LANES), jnp.bfloat16)
    id_block = id_block.at[:rows_dev, :].set(
        jnp.broadcast_to(prefix_id.astype(jnp.bfloat16)[:, None], (rows_dev, LANES))
    )
    packed = jnp.concatenate([queries.reshape(query_rows, LANES), id_block], axis=0)
    fanned = jnp.broadcast_to(packed[None], (row_count,) + packed.shape)
    gathered = lax.all_to_all(fanned, "row", split_axis=0, concat_axis=0, tiled=True)
    total_rows = row_count * rows_dev
    every_query = gathered[:, :query_rows, :].reshape(total_rows, step_count, KVH, groups, HD)
    every_prefix = gathered[:, query_rows : query_rows + rows_dev, 0].reshape(total_rows)
    every_prefix = every_prefix.astype(jnp.int32)

    core_bit = ctx_index % 2
    half_kv = KVH // 2
    half_heads = H // 2
    swap = [(c, c ^ 1) for c in range(ctx_count)]
    span_len = prefix_keys.shape[1]
    prefix_count = prefix_keys.shape[0]
    kv_both = jnp.stack(
        [
            prefix_keys.reshape(prefix_count, span_len, KVH, HD),
            prefix_values.reshape(prefix_count, span_len, KVH, HD),
        ]
    )
    own_kv = lax.dynamic_slice_in_dim(kv_both, core_bit * half_kv, half_kv, 3)
    given_kv = lax.dynamic_slice_in_dim(kv_both, (1 - core_bit) * half_kv, half_kv, 3)
    partner_kv = lax.ppermute(given_kv, "ctx", swap)

    half_query = lax.dynamic_slice_in_dim(every_query, core_bit * half_kv, half_kv, 2)

    def prefix_block(kv):
        row_keys = jnp.take(kv[0], every_prefix, axis=0)
        row_values = jnp.take(kv[1], every_prefix, axis=0)
        scores = (
            jnp.einsum(
                "rskgd,rtkd->rskgt", half_query, row_keys, preferred_element_type=jnp.float32
            )
            * score_scale
        )
        always = jnp.ones((1, 1, 1, 1, span_len), dtype=bool)
        return block_stats(scores, always, row_values, "rskgt,rtkd->rskgd")

    prefix_stats = combine_pair(prefix_block(own_kv), prefix_block(partner_kv))

    def head_half(member, at):
        return lax.dynamic_slice_in_dim(member, at * half_kv, half_kv, 2)

    suffix_packed = jnp.concatenate(
        [suffix_stats[2], suffix_stats[0][..., None], suffix_stats[1][..., None]], axis=-1
    )
    suffix_moved = lax.ppermute(head_half(suffix_packed, 1 - core_bit), "ctx", swap)
    suffix_partner = (suffix_moved[..., HD], suffix_moved[..., HD + 1], suffix_moved[..., :HD])
    suffix_kept = tuple(head_half(member, core_bit) for member in suffix_stats)
    suffix_half = combine_pair(suffix_kept, suffix_partner)

    row_start = row_index * rows_dev
    own_prefix = tuple(
        lax.dynamic_slice_in_dim(member, row_start, rows_dev, 0) for member in prefix_stats
    )
    own_merged = combine_pair(own_prefix, suffix_half)
    peak_all, total_all, sum_all = tuple(
        lax.dynamic_update_slice_in_dim(whole_arr, piece_arr, row_start, 0)
        for whole_arr, piece_arr in zip(prefix_stats, own_merged)
    )

    half_units = rows_dev * step_count * half_heads
    chunk = half_units // ctx_count
    pt_rows = -(-2 * chunk // LANES)
    dests = ctx_count * row_count

    def by_dest(member, tail=()):
        shaped = member.reshape((row_count, ctx_count, chunk) + tail)
        return jnp.swapaxes(shaped, 0, 1).reshape((dests, chunk) + tail)

    pt = jnp.concatenate([by_dest(peak_all), by_dest(total_all)], axis=-1)
    pt = jnp.pad(pt, ((0, 0), (0, pt_rows * LANES - 2 * chunk)))
    flat_len = (chunk + pt_rows) * LANES
    outgoing = jnp.concatenate([by_dest(sum_all, (HD,)).reshape(dests, chunk * HD), pt], axis=1)
    incoming = lax.all_to_all(
        outgoing.reshape(dests, 1, flat_len),
        ("ctx", "row"),
        split_axis=0,
        concat_axis=0,
        tiled=True,
    )
    incoming = incoming.reshape(dests, chunk + pt_rows, LANES)
    got_pt = incoming[:, chunk:, :].reshape(dests, pt_rows * LANES)
    pairs = ctx_count // 2

    def by_half(member, tail=()):
        shaped = member.reshape((pairs, 2, row_count, chunk) + tail)
        return jnp.swapaxes(shaped, 0, 1).reshape((2, pairs * row_count, chunk) + tail)

    got_peak = by_half(got_pt[:, :chunk])
    got_total = by_half(got_pt[:, chunk : 2 * chunk])
    got_sum = by_half(incoming[:, :chunk, :], (HD,))

    def fresh_chunk(member, tail=()):
        shaped = member.reshape((rows_dev, step_count, 2, half_heads) + tail)
        shaped = jnp.moveaxis(shaped, 2, 0).reshape((2, half_units) + tail)
        return lax.dynamic_slice_in_dim(shaped, ctx_index * chunk, chunk, 1)

    fresh_peak = fresh_chunk(fresh_stats[0])
    fresh_total = fresh_chunk(fresh_stats[1])
    fresh_sum = fresh_chunk(fresh_stats[2], (HD,))

    top = jnp.maximum(jnp.max(got_peak, axis=1), fresh_peak)
    factor = jnp.exp(got_peak - top[:, None])
    fresh_factor = jnp.exp(fresh_peak - top)
    denom = jnp.sum(factor * got_total, axis=1) + fresh_factor * fresh_total
    numer = jnp.sum(factor[..., None] * got_sum, axis=1) + fresh_factor[..., None] * fresh_sum
    result = (numer / denom[..., None]).astype(jnp.bfloat16)
    whole = lax.all_gather(result, "ctx", axis=0, tiled=False)
    whole = jnp.swapaxes(whole, 0, 1).reshape(2, rows_dev, step_count, half_heads, HD)
    whole = jnp.moveaxis(whole, 0, 2)
    return whole.reshape(rows_dev, step_count, H * HD)


def solution(mesh):
    in_specs = (
        P("row", None, None),
        P("row"),
        P(None, ("ctx", "row"), None),
        P(None, ("ctx", "row"), None),
        P(("ctx", "row"), None, None),
        P(("ctx", "row"), None, None),
        P("row", None),
        P("row"),
        P("row", None, None),
        P("row", None, None),
    )
    out_specs = P("row", None, None)
    return jax.shard_map(
        per_device, mesh=mesh, in_specs=in_specs, out_specs=out_specs, check_vma=False
    )
```

```python
import math

import jax
import jax.numpy as jnp
from jax import lax
from jax.sharding import PartitionSpec as P

H = 32
KVH = 4
HD = 128
LANES = 128


MASKED_SCORE = -1e30


def block_stats(scores, valid_mask, values, einsum_form):
    block_peak = jnp.max(jnp.where(valid_mask, scores, MASKED_SCORE), axis=-1)
    weights = jnp.where(valid_mask, jnp.exp(scores - block_peak[..., None]), 0.0).astype(
        jnp.bfloat16
    )
    block_total = jnp.sum(weights.astype(jnp.float32), axis=-1)
    block_sum = jnp.einsum(einsum_form, weights, values, preferred_element_type=jnp.float32)
    return (block_peak, block_total, block_sum)


def combine_pair(earlier, later):
    highest = jnp.maximum(earlier[0], later[0])
    left_factor = jnp.exp(earlier[0] - highest)
    right_factor = jnp.exp(later[0] - highest)
    totals = left_factor * earlier[1] + right_factor * later[1]
    sums = left_factor[..., None] * earlier[2] + right_factor[..., None] * later[2]
    return (highest, totals, sums)


def per_device(
    queries,
    prefix_id,
    prefix_keys,
    prefix_values,
    pool_keys,
    pool_values,
    page_table,
    suffix_len,
    new_keys,
    new_values,
):
    rows_dev, step_count, feature_width = queries.shape
    groups = H // KVH
    score_scale = 1.0 / math.sqrt(HD)
    row_count = lax.axis_size("row")
    ctx_count = lax.axis_size("ctx")
    row_index = lax.axis_index("row")
    ctx_index = lax.axis_index("ctx")
    flat_index = ctx_index * row_count + row_index
    own_query = queries.reshape(rows_dev, step_count, KVH, groups, HD)

    slot_count, page_len, kv_width = pool_keys.shape
    slot_ids = flat_index * slot_count + jnp.arange(slot_count, dtype=jnp.int32)
    slot_match = page_table[:, :, None] == slot_ids[None, None, :]
    entry_pos = jnp.arange(page_table.shape[1], dtype=jnp.int32)
    page_of = jnp.sum(jnp.where(slot_match, entry_pos[None, :, None], 0), axis=1)
    owned = jnp.any(slot_match, axis=1)
    token_pos = (
        page_of[:, :, None] * page_len + jnp.arange(page_len, dtype=jnp.int32)[None, None, :]
    )
    live_mask = owned[:, :, None] & (token_pos < suffix_len[:, None, None])
    live_mask = live_mask.reshape(rows_dev, 1, 1, 1, slot_count * page_len)
    flat_keys = pool_keys.reshape(slot_count * page_len, KVH, HD)
    flat_values = pool_values.reshape(slot_count * page_len, KVH, HD)
    suffix_scores = (
        jnp.einsum("rskgd,tkd->rskgt", own_query, flat_keys, preferred_element_type=jnp.float32)
        * score_scale
    )
    suffix_stats = block_stats(suffix_scores, live_mask, flat_values, "rskgt,tkd->rskgd")

    fresh_keys = new_keys.reshape(rows_dev, step_count, KVH, HD)
    fresh_values = new_values.reshape(rows_dev, step_count, KVH, HD)
    fresh_scores = (
        jnp.einsum("rskgd,rtkd->rskgt", own_query, fresh_keys, preferred_element_type=jnp.float32)
        * score_scale
    )
    causal = jnp.arange(step_count)[None, :] <= jnp.arange(step_count)[:, None]
    causal = causal.reshape(1, step_count, 1, 1, step_count)
    fresh_stats = block_stats(fresh_scores, causal, fresh_values, "rskgt,rtkd->rskgd")

    query_rows = rows_dev * step_count * feature_width // LANES
    id_rows = -(-rows_dev // 16) * 16
    id_block = jnp.zeros((id_rows, LANES), jnp.bfloat16)
    id_block = id_block.at[:rows_dev, :].set(
        jnp.broadcast_to(prefix_id.astype(jnp.bfloat16)[:, None], (rows_dev, LANES))
    )
    packed = jnp.concatenate([queries.reshape(query_rows, LANES), id_block], axis=0)
    fanned = jnp.broadcast_to(packed[None], (row_count,) + packed.shape)
    gathered = lax.all_to_all(fanned, "row", split_axis=0, concat_axis=0, tiled=True)
    total_rows = row_count * rows_dev
    every_query = gathered[:, :query_rows, :].reshape(total_rows, step_count, KVH, groups, HD)
    every_prefix = gathered[:, query_rows : query_rows + rows_dev, 0].reshape(total_rows)
    every_prefix = every_prefix.astype(jnp.int32)

    core_bit = ctx_index % 2
    half_kv = KVH // 2
    half_heads = H // 2
    swap = [(c, c ^ 1) for c in range(ctx_count)]
    span_len = prefix_keys.shape[1]
    prefix_count = prefix_keys.shape[0]
    kv_both = jnp.stack(
        [
            prefix_keys.reshape(prefix_count, span_len, KVH, HD),
            prefix_values.reshape(prefix_count, span_len, KVH, HD),
        ]
    )
    own_kv = lax.dynamic_slice_in_dim(kv_both, core_bit * half_kv, half_kv, 3)
    given_kv = lax.dynamic_slice_in_dim(kv_both, (1 - core_bit) * half_kv, half_kv, 3)
    partner_kv = lax.ppermute(given_kv, "ctx", swap)

    half_query = lax.dynamic_slice_in_dim(every_query, core_bit * half_kv, half_kv, 2)

    prefix_count_iota = jnp.arange(prefix_count, dtype=jnp.int32)
    chosen = (every_prefix[:, None] == prefix_count_iota[None, :]).reshape(
        total_rows, 1, 1, 1, prefix_count, 1
    )

    def prefix_block(kv):
        scores = (
            jnp.einsum(
                "rskgd,ptkd->rskgpt", half_query, kv[0], preferred_element_type=jnp.float32
            )
            * score_scale
        )
        block_peak = jnp.max(jnp.where(chosen, scores, MASKED_SCORE), axis=(4, 5))
        weights = jnp.where(
            chosen, jnp.exp(scores - block_peak[..., None, None]), 0.0
        ).astype(jnp.bfloat16)
        block_total = jnp.sum(weights.astype(jnp.float32), axis=(4, 5))
        block_sum = jnp.einsum(
            "rskgpt,ptkd->rskgd", weights, kv[1], preferred_element_type=jnp.float32
        )
        return (block_peak, block_total, block_sum)

    prefix_stats = combine_pair(prefix_block(own_kv), prefix_block(partner_kv))

    def head_half(member, at):
        return lax.dynamic_slice_in_dim(member, at * half_kv, half_kv, 2)

    suffix_packed = jnp.concatenate(
        [suffix_stats[2], suffix_stats[0][..., None], suffix_stats[1][..., None]], axis=-1
    )
    suffix_moved = lax.ppermute(head_half(suffix_packed, 1 - core_bit), "ctx", swap)
    suffix_partner = (suffix_moved[..., HD], suffix_moved[..., HD + 1], suffix_moved[..., :HD])
    suffix_kept = tuple(head_half(member, core_bit) for member in suffix_stats)
    suffix_half = combine_pair(suffix_kept, suffix_partner)

    row_start = row_index * rows_dev
    own_prefix = tuple(
        lax.dynamic_slice_in_dim(member, row_start, rows_dev, 0) for member in prefix_stats
    )
    own_merged = combine_pair(own_prefix, suffix_half)
    peak_all, total_all, sum_all = tuple(
        lax.dynamic_update_slice_in_dim(whole_arr, piece_arr, row_start, 0)
        for whole_arr, piece_arr in zip(prefix_stats, own_merged)
    )

    half_units = rows_dev * step_count * half_heads
    chunk = half_units // ctx_count
    pt_rows = -(-2 * chunk // LANES)
    dests = ctx_count * row_count

    def by_dest(member, tail=()):
        shaped = member.reshape((row_count, ctx_count, chunk) + tail)
        return jnp.swapaxes(shaped, 0, 1).reshape((dests, chunk) + tail)

    pt = jnp.concatenate([by_dest(peak_all), by_dest(total_all)], axis=-1)
    pt = jnp.pad(pt, ((0, 0), (0, pt_rows * LANES - 2 * chunk)))
    flat_len = (chunk + pt_rows) * LANES
    outgoing = jnp.concatenate([by_dest(sum_all, (HD,)).reshape(dests, chunk * HD), pt], axis=1)
    incoming = lax.all_to_all(
        outgoing.reshape(dests, 1, flat_len),
        ("ctx", "row"),
        split_axis=0,
        concat_axis=0,
        tiled=True,
    )
    incoming = incoming.reshape(dests, chunk + pt_rows, LANES)
    got_pt = incoming[:, chunk:, :].reshape(dests, pt_rows * LANES)
    pairs = ctx_count // 2

    def by_half(member, tail=()):
        shaped = member.reshape((pairs, 2, row_count, chunk) + tail)
        return jnp.swapaxes(shaped, 0, 1).reshape((2, pairs * row_count, chunk) + tail)

    got_peak = by_half(got_pt[:, :chunk])
    got_total = by_half(got_pt[:, chunk : 2 * chunk])
    got_sum = by_half(incoming[:, :chunk, :], (HD,))

    def fresh_chunk(member, tail=()):
        shaped = member.reshape((rows_dev, step_count, 2, half_heads) + tail)
        shaped = jnp.moveaxis(shaped, 2, 0).reshape((2, half_units) + tail)
        return lax.dynamic_slice_in_dim(shaped, ctx_index * chunk, chunk, 1)

    fresh_peak = fresh_chunk(fresh_stats[0])
    fresh_total = fresh_chunk(fresh_stats[1])
    fresh_sum = fresh_chunk(fresh_stats[2], (HD,))

    top = jnp.maximum(jnp.max(got_peak, axis=1), fresh_peak)
    factor = jnp.exp(got_peak - top[:, None])
    fresh_factor = jnp.exp(fresh_peak - top)
    denom = jnp.sum(factor * got_total, axis=1) + fresh_factor * fresh_total
    numer = jnp.sum(factor[..., None] * got_sum, axis=1) + fresh_factor[..., None] * fresh_sum
    result = (numer / denom[..., None]).astype(jnp.bfloat16)
    whole = lax.all_gather(result, "ctx", axis=0, tiled=False)
    whole = jnp.swapaxes(whole, 0, 1).reshape(2, rows_dev, step_count, half_heads, HD)
    whole = jnp.moveaxis(whole, 0, 2)
    return whole.reshape(rows_dev, step_count, H * HD)


def solution(mesh):
    in_specs = (
        P("row", None, None),
        P("row"),
        P(None, ("ctx", "row"), None),
        P(None, ("ctx", "row"), None),
        P(("ctx", "row"), None, None),
        P(("ctx", "row"), None, None),
        P("row", None),
        P("row"),
        P("row", None, None),
        P("row", None, None),
    )
    out_specs = P("row", None, None)
    return jax.shard_map(
        per_device, mesh=mesh, in_specs=in_specs, out_specs=out_specs, check_vma=False
    )
```

```python
import math

import jax
import jax.numpy as jnp
from jax import lax
from jax.sharding import PartitionSpec as P

H = 32
KVH = 4
HD = 128
LANES = 128


MASKED_SCORE = -1e30


def block_stats(scores, valid_mask, values, einsum_form):
    block_peak = jnp.max(jnp.where(valid_mask, scores, MASKED_SCORE), axis=-1)
    weights = jnp.where(valid_mask, jnp.exp(scores - block_peak[..., None]), 0.0).astype(
        jnp.bfloat16
    )
    block_total = jnp.sum(weights.astype(jnp.float32), axis=-1)
    block_sum = jnp.einsum(einsum_form, weights, values, preferred_element_type=jnp.float32)
    return (block_peak, block_total, block_sum)


def combine_pair(earlier, later):
    highest = jnp.maximum(earlier[0], later[0])
    left_factor = jnp.exp(earlier[0] - highest)
    right_factor = jnp.exp(later[0] - highest)
    totals = left_factor * earlier[1] + right_factor * later[1]
    sums = left_factor[..., None] * earlier[2] + right_factor[..., None] * later[2]
    return (highest, totals, sums)


def per_device(
    queries,
    prefix_id,
    prefix_keys,
    prefix_values,
    pool_keys,
    pool_values,
    page_table,
    suffix_len,
    new_keys,
    new_values,
):
    rows_dev, step_count, feature_width = queries.shape
    groups = H // KVH
    score_scale = 1.0 / math.sqrt(HD)
    row_count = lax.axis_size("row")
    ctx_count = lax.axis_size("ctx")
    row_index = lax.axis_index("row")
    ctx_index = lax.axis_index("ctx")
    flat_index = ctx_index * row_count + row_index
    own_query = queries.reshape(rows_dev, step_count, KVH, groups, HD)

    slot_count, page_len, kv_width = pool_keys.shape
    slot_ids = flat_index * slot_count + jnp.arange(slot_count, dtype=jnp.int32)
    slot_match = page_table[:, :, None] == slot_ids[None, None, :]
    entry_pos = jnp.arange(page_table.shape[1], dtype=jnp.int32)
    page_of = jnp.sum(jnp.where(slot_match, entry_pos[None, :, None], 0), axis=1)
    owned = jnp.any(slot_match, axis=1)
    token_pos = (
        page_of[:, :, None] * page_len + jnp.arange(page_len, dtype=jnp.int32)[None, None, :]
    )
    live_mask = owned[:, :, None] & (token_pos < suffix_len[:, None, None])
    live_mask = live_mask.reshape(rows_dev, 1, 1, 1, slot_count * page_len)
    flat_keys = pool_keys.reshape(slot_count * page_len, KVH, HD)
    flat_values = pool_values.reshape(slot_count * page_len, KVH, HD)
    suffix_scores = (
        jnp.einsum("rskgd,tkd->rskgt", own_query, flat_keys, preferred_element_type=jnp.float32)
        * score_scale
    )
    suffix_stats = block_stats(suffix_scores, live_mask, flat_values, "rskgt,tkd->rskgd")

    fresh_keys = new_keys.reshape(rows_dev, step_count, KVH, HD)
    fresh_values = new_values.reshape(rows_dev, step_count, KVH, HD)
    fresh_scores = (
        jnp.einsum("rskgd,rtkd->rskgt", own_query, fresh_keys, preferred_element_type=jnp.float32)
        * score_scale
    )
    causal = jnp.arange(step_count)[None, :] <= jnp.arange(step_count)[:, None]
    causal = causal.reshape(1, step_count, 1, 1, step_count)
    fresh_stats = block_stats(fresh_scores, causal, fresh_values, "rskgt,rtkd->rskgd")

    query_rows = rows_dev * step_count * feature_width // LANES
    id_rows = -(-rows_dev // 16) * 16
    id_block = jnp.zeros((id_rows, LANES), jnp.bfloat16)
    id_block = id_block.at[:rows_dev, :].set(
        jnp.broadcast_to(prefix_id.astype(jnp.bfloat16)[:, None], (rows_dev, LANES))
    )
    packed = jnp.concatenate([queries.reshape(query_rows, LANES), id_block], axis=0)
    fanned = jnp.broadcast_to(packed[None], (row_count,) + packed.shape)
    gathered = lax.all_to_all(fanned, "row", split_axis=0, concat_axis=0, tiled=True)
    total_rows = row_count * rows_dev
    every_query = gathered[:, :query_rows, :].reshape(total_rows, step_count, KVH, groups, HD)
    every_prefix = gathered[:, query_rows : query_rows + rows_dev, 0].reshape(total_rows)
    every_prefix = every_prefix.astype(jnp.int32)

    core_bit = ctx_index % 2
    half_kv = KVH // 2
    half_heads = H // 2
    swap = [(c, c ^ 1) for c in range(ctx_count)]
    span_len = prefix_keys.shape[1]
    prefix_count = prefix_keys.shape[0]
    kv_both = jnp.stack(
        [
            prefix_keys.reshape(prefix_count, span_len, KVH, HD),
            prefix_values.reshape(prefix_count, span_len, KVH, HD),
        ]
    )
    own_kv = lax.dynamic_slice_in_dim(kv_both, core_bit * half_kv, half_kv, 3)
    given_kv = lax.dynamic_slice_in_dim(kv_both, (1 - core_bit) * half_kv, half_kv, 3)
    partner_kv = lax.ppermute(given_kv, "ctx", swap)

    half_query = lax.dynamic_slice_in_dim(every_query, core_bit * half_kv, half_kv, 2)

    kv_pair = jnp.concatenate([own_kv, partner_kv], axis=2)
    row_kv = jnp.take(kv_pair, every_prefix, axis=1).reshape(
        2, total_rows, 2, span_len, half_kv, HD
    )
    pair_scores = (
        jnp.einsum(
            "rskgd,rbtkd->rskgbt", half_query, row_kv[0], preferred_element_type=jnp.float32
        )
        * score_scale
    )
    pair_peak = jnp.max(pair_scores, axis=-1)
    pair_weights = jnp.exp(pair_scores - pair_peak[..., None]).astype(jnp.bfloat16)
    pair_total = jnp.sum(pair_weights.astype(jnp.float32), axis=-1)
    pair_sum = jnp.einsum(
        "rskgbt,rbtkd->rskgbd", pair_weights, row_kv[1], preferred_element_type=jnp.float32
    )
    prefix_stats = combine_pair(
        (pair_peak[..., 0], pair_total[..., 0], pair_sum[..., 0, :]),
        (pair_peak[..., 1], pair_total[..., 1], pair_sum[..., 1, :]),
    )

    def head_half(member, at):
        return lax.dynamic_slice_in_dim(member, at * half_kv, half_kv, 2)

    suffix_packed = jnp.concatenate(
        [suffix_stats[2], suffix_stats[0][..., None], suffix_stats[1][..., None]], axis=-1
    )
    suffix_moved = lax.ppermute(head_half(suffix_packed, 1 - core_bit), "ctx", swap)
    suffix_partner = (suffix_moved[..., HD], suffix_moved[..., HD + 1], suffix_moved[..., :HD])
    suffix_kept = tuple(head_half(member, core_bit) for member in suffix_stats)
    suffix_half = combine_pair(suffix_kept, suffix_partner)

    row_start = row_index * rows_dev
    own_prefix = tuple(
        lax.dynamic_slice_in_dim(member, row_start, rows_dev, 0) for member in prefix_stats
    )
    own_merged = combine_pair(own_prefix, suffix_half)
    peak_all, total_all, sum_all = tuple(
        lax.dynamic_update_slice_in_dim(whole_arr, piece_arr, row_start, 0)
        for whole_arr, piece_arr in zip(prefix_stats, own_merged)
    )

    half_units = rows_dev * step_count * half_heads
    chunk = half_units // ctx_count
    pt_rows = -(-2 * chunk // LANES)
    dests = ctx_count * row_count

    def by_dest(member, tail=()):
        shaped = member.reshape((row_count, ctx_count, chunk) + tail)
        return jnp.swapaxes(shaped, 0, 1).reshape((dests, chunk) + tail)

    pt = jnp.concatenate([by_dest(peak_all), by_dest(total_all)], axis=-1)
    pt = jnp.pad(pt, ((0, 0), (0, pt_rows * LANES - 2 * chunk)))
    outgoing = jnp.concatenate(
        [by_dest(sum_all, (HD,)), pt.reshape(dests, pt_rows, LANES)], axis=1
    )
    incoming = lax.all_to_all(
        outgoing.reshape(dests, 1, (chunk + pt_rows) * LANES),
        ("ctx", "row"),
        split_axis=0,
        concat_axis=0,
        tiled=True,
    )
    incoming = incoming.reshape(dests, chunk + pt_rows, LANES)
    got_pt = incoming[:, chunk:, :].reshape(dests, pt_rows * LANES)
    pairs = ctx_count // 2

    def by_half(member, tail=()):
        shaped = member.reshape((pairs, 2, row_count, chunk) + tail)
        return jnp.swapaxes(shaped, 0, 1).reshape((2, pairs * row_count, chunk) + tail)

    got_peak = by_half(got_pt[:, :chunk])
    got_total = by_half(got_pt[:, chunk : 2 * chunk])
    got_sum = by_half(incoming[:, :chunk, :], (HD,))

    def fresh_chunk(member, tail=()):
        shaped = member.reshape((rows_dev, step_count, 2, half_heads) + tail)
        shaped = jnp.moveaxis(shaped, 2, 0).reshape((2, half_units) + tail)
        return lax.dynamic_slice_in_dim(shaped, ctx_index * chunk, chunk, 1)

    fresh_peak = fresh_chunk(fresh_stats[0])
    fresh_total = fresh_chunk(fresh_stats[1])
    fresh_sum = fresh_chunk(fresh_stats[2], (HD,))

    top = jnp.maximum(jnp.max(got_peak, axis=1), fresh_peak)
    factor = jnp.exp(got_peak - top[:, None])
    fresh_factor = jnp.exp(fresh_peak - top)
    denom = jnp.sum(factor * got_total, axis=1) + fresh_factor * fresh_total
    numer = jnp.sum(factor[..., None] * got_sum, axis=1) + fresh_factor[..., None] * fresh_sum
    result = (numer / denom[..., None]).astype(jnp.bfloat16)
    whole = lax.all_gather(result, "ctx", axis=0, tiled=False)
    whole = jnp.swapaxes(whole, 0, 1).reshape(2, rows_dev, step_count, half_heads, HD)
    whole = jnp.moveaxis(whole, 0, 2)
    return whole.reshape(rows_dev, step_count, H * HD)


def solution(mesh):
    in_specs = (
        P("row", None, None),
        P("row"),
        P(None, ("ctx", "row"), None),
        P(None, ("ctx", "row"), None),
        P(("ctx", "row"), None, None),
        P(("ctx", "row"), None, None),
        P("row", None),
        P("row"),
        P("row", None, None),
        P("row", None, None),
    )
    out_specs = P("row", None, None)
    return jax.shard_map(
        per_device, mesh=mesh, in_specs=in_specs, out_specs=out_specs, check_vma=False
    )
```

```python
import math

import jax
import jax.numpy as jnp
from jax import lax
from jax.sharding import PartitionSpec as P

H = 32
KVH = 4
HD = 128
LANES = 128


MASKED_SCORE = -1e30


def block_stats(scores, valid_mask, values, einsum_form):
    block_peak = jnp.max(jnp.where(valid_mask, scores, MASKED_SCORE), axis=-1)
    weights = jnp.where(valid_mask, jnp.exp(scores - block_peak[..., None]), 0.0).astype(
        jnp.bfloat16
    )
    block_total = jnp.sum(weights.astype(jnp.float32), axis=-1)
    block_sum = jnp.einsum(einsum_form, weights, values, preferred_element_type=jnp.float32)
    return (block_peak, block_total, block_sum)


def combine_pair(earlier, later):
    highest = jnp.maximum(earlier[0], later[0])
    left_factor = jnp.exp(earlier[0] - highest)
    right_factor = jnp.exp(later[0] - highest)
    totals = left_factor * earlier[1] + right_factor * later[1]
    sums = left_factor[..., None] * earlier[2] + right_factor[..., None] * later[2]
    return (highest, totals, sums)


def per_device(
    queries,
    prefix_id,
    prefix_keys,
    prefix_values,
    pool_keys,
    pool_values,
    page_table,
    suffix_len,
    new_keys,
    new_values,
):
    rows_dev, step_count, feature_width = queries.shape
    groups = H // KVH
    score_scale = 1.0 / math.sqrt(HD)
    row_count = lax.axis_size("row")
    ctx_count = lax.axis_size("ctx")
    row_index = lax.axis_index("row")
    ctx_index = lax.axis_index("ctx")
    flat_index = ctx_index * row_count + row_index
    own_query = queries.reshape(rows_dev, step_count, KVH, groups, HD)

    slot_count, page_len, kv_width = pool_keys.shape
    slot_ids = flat_index * slot_count + jnp.arange(slot_count, dtype=jnp.int32)
    slot_match = page_table[:, :, None] == slot_ids[None, None, :]
    entry_pos = jnp.arange(page_table.shape[1], dtype=jnp.int32)
    page_of = jnp.sum(jnp.where(slot_match, entry_pos[None, :, None], 0), axis=1)
    owned = jnp.any(slot_match, axis=1)
    token_pos = (
        page_of[:, :, None] * page_len + jnp.arange(page_len, dtype=jnp.int32)[None, None, :]
    )
    live_mask = owned[:, :, None] & (token_pos < suffix_len[:, None, None])
    live_mask = live_mask.reshape(rows_dev, 1, 1, 1, slot_count * page_len)
    flat_keys = pool_keys.reshape(slot_count * page_len, KVH, HD)
    flat_values = pool_values.reshape(slot_count * page_len, KVH, HD)
    suffix_scores = (
        jnp.einsum("rskgd,tkd->rskgt", own_query, flat_keys, preferred_element_type=jnp.float32)
        * score_scale
    )
    suffix_stats = block_stats(suffix_scores, live_mask, flat_values, "rskgt,tkd->rskgd")

    fresh_keys = new_keys.reshape(rows_dev, step_count, KVH, HD)
    fresh_values = new_values.reshape(rows_dev, step_count, KVH, HD)
    fresh_scores = (
        jnp.einsum("rskgd,rtkd->rskgt", own_query, fresh_keys, preferred_element_type=jnp.float32)
        * score_scale
    )
    causal = jnp.arange(step_count)[None, :] <= jnp.arange(step_count)[:, None]
    causal = causal.reshape(1, step_count, 1, 1, step_count)
    fresh_stats = block_stats(fresh_scores, causal, fresh_values, "rskgt,rtkd->rskgd")

    core_bit = ctx_index % 2
    half_kv = KVH // 2
    half_heads = H // 2
    own_half_query = lax.dynamic_slice_in_dim(own_query, core_bit * half_kv, half_kv, 2)
    query_rows = rows_dev * step_count * half_heads * HD // LANES
    id_rows = -(-rows_dev // 16) * 16
    id_block = jnp.zeros((id_rows, LANES), jnp.bfloat16)
    id_block = id_block.at[:rows_dev, :].set(
        jnp.broadcast_to(prefix_id.astype(jnp.bfloat16)[:, None], (rows_dev, LANES))
    )
    packed = jnp.concatenate([own_half_query.reshape(query_rows, LANES), id_block], axis=0)
    fanned = jnp.broadcast_to(packed[None], (row_count,) + packed.shape)
    gathered = lax.all_to_all(fanned, "row", split_axis=0, concat_axis=0, tiled=True)
    total_rows = row_count * rows_dev
    half_query = gathered[:, :query_rows, :].reshape(
        total_rows, step_count, half_kv, groups, HD
    )
    every_prefix = gathered[:, query_rows : query_rows + rows_dev, 0].reshape(total_rows)
    every_prefix = every_prefix.astype(jnp.int32)

    swap = [(c, c ^ 1) for c in range(ctx_count)]
    span_len = prefix_keys.shape[1]
    prefix_count = prefix_keys.shape[0]
    kv_both = jnp.stack(
        [
            prefix_keys.reshape(prefix_count, span_len, KVH, HD),
            prefix_values.reshape(prefix_count, span_len, KVH, HD),
        ]
    )
    own_kv = lax.dynamic_slice_in_dim(kv_both, core_bit * half_kv, half_kv, 3)
    given_kv = lax.dynamic_slice_in_dim(kv_both, (1 - core_bit) * half_kv, half_kv, 3)
    partner_kv = lax.ppermute(given_kv, "ctx", swap)


    def prefix_block(kv):
        row_keys = jnp.take(kv[0], every_prefix, axis=0)
        row_values = jnp.take(kv[1], every_prefix, axis=0)
        scores = (
            jnp.einsum(
                "rskgd,rtkd->rskgt", half_query, row_keys, preferred_element_type=jnp.float32
            )
            * score_scale
        )
        always = jnp.ones((1, 1, 1, 1, span_len), dtype=bool)
        return block_stats(scores, always, row_values, "rskgt,rtkd->rskgd")

    prefix_stats = combine_pair(prefix_block(own_kv), prefix_block(partner_kv))

    def head_half(member, at):
        return lax.dynamic_slice_in_dim(member, at * half_kv, half_kv, 2)

    suffix_packed = jnp.concatenate(
        [suffix_stats[2], suffix_stats[0][..., None], suffix_stats[1][..., None]], axis=-1
    )
    suffix_moved = lax.ppermute(head_half(suffix_packed, 1 - core_bit), "ctx", swap)
    suffix_partner = (suffix_moved[..., HD], suffix_moved[..., HD + 1], suffix_moved[..., :HD])
    suffix_kept = tuple(head_half(member, core_bit) for member in suffix_stats)
    suffix_half = combine_pair(suffix_kept, suffix_partner)

    row_start = row_index * rows_dev
    own_prefix = tuple(
        lax.dynamic_slice_in_dim(member, row_start, rows_dev, 0) for member in prefix_stats
    )
    own_merged = combine_pair(own_prefix, suffix_half)
    peak_all, total_all, sum_all = tuple(
        lax.dynamic_update_slice_in_dim(whole_arr, piece_arr, row_start, 0)
        for whole_arr, piece_arr in zip(prefix_stats, own_merged)
    )

    half_units = rows_dev * step_count * half_heads
    chunk = half_units // ctx_count
    pt_rows = -(-2 * chunk // LANES)
    dests = ctx_count * row_count

    def by_dest(member, tail=()):
        shaped = member.reshape((row_count, ctx_count, chunk) + tail)
        return jnp.swapaxes(shaped, 0, 1).reshape((dests, chunk) + tail)

    pt = jnp.concatenate([by_dest(peak_all), by_dest(total_all)], axis=-1)
    pt = jnp.pad(pt, ((0, 0), (0, pt_rows * LANES - 2 * chunk)))
    outgoing = jnp.concatenate(
        [by_dest(sum_all, (HD,)), pt.reshape(dests, pt_rows, LANES)], axis=1
    )
    incoming = lax.all_to_all(
        outgoing.reshape(dests, 1, (chunk + pt_rows) * LANES),
        ("ctx", "row"),
        split_axis=0,
        concat_axis=0,
        tiled=True,
    )
    incoming = incoming.reshape(dests, chunk + pt_rows, LANES)
    got_pt = incoming[:, chunk:, :].reshape(dests, pt_rows * LANES)
    pairs = ctx_count // 2

    def by_half(member, tail=()):
        shaped = member.reshape((pairs, 2, row_count, chunk) + tail)
        return jnp.swapaxes(shaped, 0, 1).reshape((2, pairs * row_count, chunk) + tail)

    got_peak = by_half(got_pt[:, :chunk])
    got_total = by_half(got_pt[:, chunk : 2 * chunk])
    got_sum = by_half(incoming[:, :chunk, :], (HD,))

    def fresh_chunk(member, tail=()):
        shaped = member.reshape((rows_dev, step_count, 2, half_heads) + tail)
        shaped = jnp.moveaxis(shaped, 2, 0).reshape((2, half_units) + tail)
        return lax.dynamic_slice_in_dim(shaped, ctx_index * chunk, chunk, 1)

    fresh_peak = fresh_chunk(fresh_stats[0])
    fresh_total = fresh_chunk(fresh_stats[1])
    fresh_sum = fresh_chunk(fresh_stats[2], (HD,))

    top = jnp.maximum(jnp.max(got_peak, axis=1), fresh_peak)
    factor = jnp.exp(got_peak - top[:, None])
    fresh_factor = jnp.exp(fresh_peak - top)
    denom = jnp.sum(factor * got_total, axis=1) + fresh_factor * fresh_total
    numer = jnp.sum(factor[..., None] * got_sum, axis=1) + fresh_factor[..., None] * fresh_sum
    result = (numer / denom[..., None]).astype(jnp.bfloat16)
    whole = lax.all_gather(result, "ctx", axis=0, tiled=False)
    whole = jnp.swapaxes(whole, 0, 1).reshape(2, rows_dev, step_count, half_heads, HD)
    whole = jnp.moveaxis(whole, 0, 2)
    return whole.reshape(rows_dev, step_count, H * HD)


def solution(mesh):
    in_specs = (
        P("row", None, None),
        P("row"),
        P(None, ("ctx", "row"), None),
        P(None, ("ctx", "row"), None),
        P(("ctx", "row"), None, None),
        P(("ctx", "row"), None, None),
        P("row", None),
        P("row"),
        P("row", None, None),
        P("row", None, None),
    )
    out_specs = P("row", None, None)
    return jax.shard_map(
        per_device, mesh=mesh, in_specs=in_specs, out_specs=out_specs, check_vma=False
    )
```

```python
import math

import jax
import jax.numpy as jnp
from jax import lax
from jax.sharding import PartitionSpec as P

H = 32
KVH = 4
HD = 128
LANES = 128


MASKED_SCORE = -1e30


def block_stats(scores, valid_mask, values, einsum_form):
    block_peak = jnp.max(jnp.where(valid_mask, scores, MASKED_SCORE), axis=-1)
    weights = jnp.where(valid_mask, jnp.exp(scores - block_peak[..., None]), 0.0).astype(
        jnp.bfloat16
    )
    block_total = jnp.sum(weights.astype(jnp.float32), axis=-1)
    block_sum = jnp.einsum(einsum_form, weights, values, preferred_element_type=jnp.float32)
    return (block_peak, block_total, block_sum)


def combine_pair(earlier, later):
    highest = jnp.maximum(earlier[0], later[0])
    left_factor = jnp.exp(earlier[0] - highest)
    right_factor = jnp.exp(later[0] - highest)
    totals = left_factor * earlier[1] + right_factor * later[1]
    sums = left_factor[..., None] * earlier[2] + right_factor[..., None] * later[2]
    return (highest, totals, sums)


def per_device(
    queries,
    prefix_id,
    prefix_keys,
    prefix_values,
    pool_keys,
    pool_values,
    page_table,
    suffix_len,
    new_keys,
    new_values,
):
    rows_dev, step_count, feature_width = queries.shape
    groups = H // KVH
    score_scale = 1.0 / math.sqrt(HD)
    row_count = lax.axis_size("row")
    ctx_count = lax.axis_size("ctx")
    row_index = lax.axis_index("row")
    ctx_index = lax.axis_index("ctx")
    flat_index = ctx_index * row_count + row_index
    own_query = queries.reshape(rows_dev, step_count, KVH, groups, HD)

    slot_count, page_len, kv_width = pool_keys.shape
    slot_ids = flat_index * slot_count + jnp.arange(slot_count, dtype=jnp.int32)
    slot_match = page_table[:, :, None] == slot_ids[None, None, :]
    entry_pos = jnp.arange(page_table.shape[1], dtype=jnp.int32)
    page_of = jnp.sum(jnp.where(slot_match, entry_pos[None, :, None], 0), axis=1)
    owned = jnp.any(slot_match, axis=1)
    token_pos = (
        page_of[:, :, None] * page_len + jnp.arange(page_len, dtype=jnp.int32)[None, None, :]
    )
    live_mask = owned[:, :, None] & (token_pos < suffix_len[:, None, None])
    live_mask = live_mask.reshape(rows_dev, 1, 1, 1, slot_count * page_len)
    flat_keys = pool_keys.reshape(slot_count * page_len, kv_width)
    flat_values = pool_values.reshape(slot_count * page_len, kv_width)
    head_eye = (jnp.arange(KVH)[:, None] == jnp.arange(KVH)[None, :]).reshape(
        1, 1, KVH, 1, KVH, 1
    )
    wide_query = jnp.where(head_eye, own_query[:, :, :, :, None, :], 0).reshape(
        rows_dev, step_count, KVH, groups, kv_width
    )
    suffix_scores = (
        jnp.einsum("rskgw,tw->rskgt", wide_query, flat_keys, preferred_element_type=jnp.float32)
        * score_scale
    )
    wide_stats = block_stats(suffix_scores, live_mask, flat_values, "rskgt,tw->rskgw")
    wide_sum = wide_stats[2].reshape(rows_dev, step_count, KVH, groups, KVH, HD)
    suffix_stats = (
        wide_stats[0],
        wide_stats[1],
        jnp.sum(jnp.where(head_eye, wide_sum, 0.0), axis=4),
    )

    fresh_keys = new_keys.reshape(rows_dev, step_count, KVH, HD)
    fresh_values = new_values.reshape(rows_dev, step_count, KVH, HD)
    fresh_scores = (
        jnp.einsum("rskgd,rtkd->rskgt", own_query, fresh_keys, preferred_element_type=jnp.float32)
        * score_scale
    )
    causal = jnp.arange(step_count)[None, :] <= jnp.arange(step_count)[:, None]
    causal = causal.reshape(1, step_count, 1, 1, step_count)
    fresh_stats = block_stats(fresh_scores, causal, fresh_values, "rskgt,rtkd->rskgd")

    core_bit = ctx_index % 2
    half_kv = KVH // 2
    half_heads = H // 2
    own_half_query = lax.dynamic_slice_in_dim(own_query, core_bit * half_kv, half_kv, 2)
    query_rows = rows_dev * step_count * half_heads * HD // LANES
    id_rows = -(-rows_dev // 16) * 16
    id_block = jnp.zeros((id_rows, LANES), jnp.bfloat16)
    id_block = id_block.at[:rows_dev, :].set(
        jnp.broadcast_to(prefix_id.astype(jnp.bfloat16)[:, None], (rows_dev, LANES))
    )
    packed = jnp.concatenate([own_half_query.reshape(query_rows, LANES), id_block], axis=0)
    fanned = jnp.broadcast_to(packed[None], (row_count,) + packed.shape)
    gathered = lax.all_to_all(fanned, "row", split_axis=0, concat_axis=0, tiled=True)
    total_rows = row_count * rows_dev
    half_query = gathered[:, :query_rows, :].reshape(
        total_rows, step_count, half_kv, groups, HD
    )
    every_prefix = gathered[:, query_rows : query_rows + rows_dev, 0].reshape(total_rows)
    every_prefix = every_prefix.astype(jnp.int32)

    swap = [(c, c ^ 1) for c in range(ctx_count)]
    span_len = prefix_keys.shape[1]
    prefix_count = prefix_keys.shape[0]
    kv_both = jnp.stack(
        [
            prefix_keys.reshape(prefix_count, span_len, KVH, HD),
            prefix_values.reshape(prefix_count, span_len, KVH, HD),
        ]
    )
    own_kv = lax.dynamic_slice_in_dim(kv_both, core_bit * half_kv, half_kv, 3)
    given_kv = lax.dynamic_slice_in_dim(kv_both, (1 - core_bit) * half_kv, half_kv, 3)
    partner_kv = lax.ppermute(given_kv, "ctx", swap)


    def prefix_block(kv):
        row_keys = jnp.take(kv[0], every_prefix, axis=0)
        row_values = jnp.take(kv[1], every_prefix, axis=0)
        scores = (
            jnp.einsum(
                "rskgd,rtkd->rskgt", half_query, row_keys, preferred_element_type=jnp.float32
            )
            * score_scale
        )
        always = jnp.ones((1, 1, 1, 1, span_len), dtype=bool)
        return block_stats(scores, always, row_values, "rskgt,rtkd->rskgd")

    prefix_stats = combine_pair(prefix_block(own_kv), prefix_block(partner_kv))

    def head_half(member, at):
        return lax.dynamic_slice_in_dim(member, at * half_kv, half_kv, 2)

    suffix_packed = jnp.concatenate(
        [suffix_stats[2], suffix_stats[0][..., None], suffix_stats[1][..., None]], axis=-1
    )
    suffix_moved = lax.ppermute(head_half(suffix_packed, 1 - core_bit), "ctx", swap)
    suffix_partner = (suffix_moved[..., HD], suffix_moved[..., HD + 1], suffix_moved[..., :HD])
    suffix_kept = tuple(head_half(member, core_bit) for member in suffix_stats)
    suffix_half = combine_pair(suffix_kept, suffix_partner)

    row_start = row_index * rows_dev
    own_prefix = tuple(
        lax.dynamic_slice_in_dim(member, row_start, rows_dev, 0) for member in prefix_stats
    )
    own_merged = combine_pair(own_prefix, suffix_half)
    peak_all, total_all, sum_all = tuple(
        lax.dynamic_update_slice_in_dim(whole_arr, piece_arr, row_start, 0)
        for whole_arr, piece_arr in zip(prefix_stats, own_merged)
    )

    half_units = rows_dev * step_count * half_heads
    chunk = half_units // ctx_count
    pt_rows = -(-2 * chunk // LANES)
    dests = ctx_count * row_count

    def by_dest(member, tail=()):
        shaped = member.reshape((row_count, ctx_count, chunk) + tail)
        return jnp.swapaxes(shaped, 0, 1).reshape((dests, chunk) + tail)

    pt = jnp.concatenate([by_dest(peak_all), by_dest(total_all)], axis=-1)
    pt = jnp.pad(pt, ((0, 0), (0, pt_rows * LANES - 2 * chunk)))
    outgoing = jnp.concatenate(
        [by_dest(sum_all, (HD,)), pt.reshape(dests, pt_rows, LANES)], axis=1
    )
    incoming = lax.all_to_all(
        outgoing.reshape(dests, 1, (chunk + pt_rows) * LANES),
        ("ctx", "row"),
        split_axis=0,
        concat_axis=0,
        tiled=True,
    )
    incoming = incoming.reshape(dests, chunk + pt_rows, LANES)
    got_pt = incoming[:, chunk:, :].reshape(dests, pt_rows * LANES)
    pairs = ctx_count // 2

    def by_half(member, tail=()):
        shaped = member.reshape((pairs, 2, row_count, chunk) + tail)
        return jnp.swapaxes(shaped, 0, 1).reshape((2, pairs * row_count, chunk) + tail)

    got_peak = by_half(got_pt[:, :chunk])
    got_total = by_half(got_pt[:, chunk : 2 * chunk])
    got_sum = by_half(incoming[:, :chunk, :], (HD,))

    def fresh_chunk(member, tail=()):
        shaped = member.reshape((rows_dev, step_count, 2, half_heads) + tail)
        shaped = jnp.moveaxis(shaped, 2, 0).reshape((2, half_units) + tail)
        return lax.dynamic_slice_in_dim(shaped, ctx_index * chunk, chunk, 1)

    fresh_peak = fresh_chunk(fresh_stats[0])
    fresh_total = fresh_chunk(fresh_stats[1])
    fresh_sum = fresh_chunk(fresh_stats[2], (HD,))

    top = jnp.maximum(jnp.max(got_peak, axis=1), fresh_peak)
    factor = jnp.exp(got_peak - top[:, None])
    fresh_factor = jnp.exp(fresh_peak - top)
    denom = jnp.sum(factor * got_total, axis=1) + fresh_factor * fresh_total
    numer = jnp.sum(factor[..., None] * got_sum, axis=1) + fresh_factor[..., None] * fresh_sum
    result = (numer / denom[..., None]).astype(jnp.bfloat16)
    whole = lax.all_gather(result, "ctx", axis=0, tiled=False)
    whole = jnp.swapaxes(whole, 0, 1).reshape(2, rows_dev, step_count, half_heads, HD)
    whole = jnp.moveaxis(whole, 0, 2)
    return whole.reshape(rows_dev, step_count, H * HD)


def solution(mesh):
    in_specs = (
        P("row", None, None),
        P("row"),
        P(None, ("ctx", "row"), None),
        P(None, ("ctx", "row"), None),
        P(("ctx", "row"), None, None),
        P(("ctx", "row"), None, None),
        P("row", None),
        P("row"),
        P("row", None, None),
        P("row", None, None),
    )
    out_specs = P("row", None, None)
    return jax.shard_map(
        per_device, mesh=mesh, in_specs=in_specs, out_specs=out_specs, check_vma=False
    )
```

```python
import math

import jax
import jax.numpy as jnp
from jax import lax
from jax.sharding import PartitionSpec as P

H = 32
KVH = 4
HD = 128
LANES = 128


MASKED_SCORE = -1e30


def block_stats(scores, valid_mask, values, einsum_form):
    block_peak = jnp.max(jnp.where(valid_mask, scores, MASKED_SCORE), axis=-1)
    weights = jnp.where(valid_mask, jnp.exp(scores - block_peak[..., None]), 0.0).astype(
        jnp.bfloat16
    )
    block_total = jnp.sum(weights.astype(jnp.float32), axis=-1)
    block_sum = jnp.einsum(einsum_form, weights, values, preferred_element_type=jnp.float32)
    return (block_peak, block_total, block_sum)


def combine_pair(earlier, later):
    highest = jnp.maximum(earlier[0], later[0])
    left_factor = jnp.exp(earlier[0] - highest)
    right_factor = jnp.exp(later[0] - highest)
    totals = left_factor * earlier[1] + right_factor * later[1]
    sums = left_factor[..., None] * earlier[2] + right_factor[..., None] * later[2]
    return (highest, totals, sums)


def per_device(
    queries,
    prefix_id,
    prefix_keys,
    prefix_values,
    pool_keys,
    pool_values,
    page_table,
    suffix_len,
    new_keys,
    new_values,
):
    rows_dev, step_count, feature_width = queries.shape
    groups = H // KVH
    score_scale = 1.0 / math.sqrt(HD)
    row_count = lax.axis_size("row")
    ctx_count = lax.axis_size("ctx")
    row_index = lax.axis_index("row")
    ctx_index = lax.axis_index("ctx")
    flat_index = ctx_index * row_count + row_index
    own_query = queries.reshape(rows_dev, step_count, KVH, groups, HD)

    slot_count, page_len, kv_width = pool_keys.shape
    slot_ids = flat_index * slot_count + jnp.arange(slot_count, dtype=jnp.int32)
    slot_match = page_table[:, :, None] == slot_ids[None, None, :]
    entry_pos = jnp.arange(page_table.shape[1], dtype=jnp.int32)
    page_of = jnp.sum(jnp.where(slot_match, entry_pos[None, :, None], 0), axis=1)
    owned = jnp.any(slot_match, axis=1)
    token_pos = (
        page_of[:, :, None] * page_len + jnp.arange(page_len, dtype=jnp.int32)[None, None, :]
    )
    live_mask = owned[:, :, None] & (token_pos < suffix_len[:, None, None])
    live_mask = live_mask.reshape(rows_dev, 1, 1, 1, slot_count * page_len)
    flat_keys = pool_keys.reshape(slot_count * page_len, kv_width)
    flat_values = pool_values.reshape(slot_count * page_len, KVH, HD)
    head_eye = (jnp.arange(KVH)[:, None] == jnp.arange(KVH)[None, :]).reshape(
        1, 1, KVH, 1, KVH, 1
    )
    wide_query = jnp.where(head_eye, own_query[:, :, :, :, None, :], 0).reshape(
        rows_dev, step_count, KVH, groups, kv_width
    )
    suffix_scores = (
        jnp.einsum("rskgw,tw->rskgt", wide_query, flat_keys, preferred_element_type=jnp.float32)
        * score_scale
    )
    suffix_stats = block_stats(suffix_scores, live_mask, flat_values, "rskgt,tkd->rskgd")

    fresh_keys = new_keys.reshape(rows_dev, step_count, KVH, HD)
    fresh_values = new_values.reshape(rows_dev, step_count, KVH, HD)
    fresh_scores = (
        jnp.einsum("rskgd,rtkd->rskgt", own_query, fresh_keys, preferred_element_type=jnp.float32)
        * score_scale
    )
    causal = jnp.arange(step_count)[None, :] <= jnp.arange(step_count)[:, None]
    causal = causal.reshape(1, step_count, 1, 1, step_count)
    fresh_stats = block_stats(fresh_scores, causal, fresh_values, "rskgt,rtkd->rskgd")

    core_bit = ctx_index % 2
    half_kv = KVH // 2
    half_heads = H // 2
    own_half_query = lax.dynamic_slice_in_dim(own_query, core_bit * half_kv, half_kv, 2)
    query_rows = rows_dev * step_count * half_heads * HD // LANES
    id_rows = -(-rows_dev // 16) * 16
    id_block = jnp.zeros((id_rows, LANES), jnp.bfloat16)
    id_block = id_block.at[:rows_dev, :].set(
        jnp.broadcast_to(prefix_id.astype(jnp.bfloat16)[:, None], (rows_dev, LANES))
    )
    packed = jnp.concatenate([own_half_query.reshape(query_rows, LANES), id_block], axis=0)
    fanned = jnp.broadcast_to(packed[None], (row_count,) + packed.shape)
    gathered = lax.all_to_all(fanned, "row", split_axis=0, concat_axis=0, tiled=True)
    total_rows = row_count * rows_dev
    half_query = gathered[:, :query_rows, :].reshape(
        total_rows, step_count, half_kv, groups, HD
    )
    every_prefix = gathered[:, query_rows : query_rows + rows_dev, 0].reshape(total_rows)
    every_prefix = every_prefix.astype(jnp.int32)

    swap = [(c, c ^ 1) for c in range(ctx_count)]
    span_len = prefix_keys.shape[1]
    prefix_count = prefix_keys.shape[0]
    kv_both = jnp.stack(
        [
            prefix_keys.reshape(prefix_count, span_len, KVH, HD),
            prefix_values.reshape(prefix_count, span_len, KVH, HD),
        ]
    )
    own_kv = lax.dynamic_slice_in_dim(kv_both, core_bit * half_kv, half_kv, 3)
    given_kv = lax.dynamic_slice_in_dim(kv_both, (1 - core_bit) * half_kv, half_kv, 3)
    partner_kv = lax.ppermute(given_kv, "ctx", swap)


    def prefix_block(kv):
        row_keys = jnp.take(kv[0], every_prefix, axis=0)
        row_values = jnp.take(kv[1], every_prefix, axis=0)
        scores = (
            jnp.einsum(
                "rskgd,rtkd->rskgt", half_query, row_keys, preferred_element_type=jnp.float32
            )
            * score_scale
        )
        always = jnp.ones((1, 1, 1, 1, span_len), dtype=bool)
        return block_stats(scores, always, row_values, "rskgt,rtkd->rskgd")

    prefix_stats = combine_pair(prefix_block(own_kv), prefix_block(partner_kv))

    def head_half(member, at):
        return lax.dynamic_slice_in_dim(member, at * half_kv, half_kv, 2)

    suffix_packed = jnp.concatenate(
        [suffix_stats[2], suffix_stats[0][..., None], suffix_stats[1][..., None]], axis=-1
    )
    suffix_moved = lax.ppermute(head_half(suffix_packed, 1 - core_bit), "ctx", swap)
    suffix_partner = (suffix_moved[..., HD], suffix_moved[..., HD + 1], suffix_moved[..., :HD])
    suffix_kept = tuple(head_half(member, core_bit) for member in suffix_stats)
    suffix_half = combine_pair(suffix_kept, suffix_partner)

    row_start = row_index * rows_dev
    own_prefix = tuple(
        lax.dynamic_slice_in_dim(member, row_start, rows_dev, 0) for member in prefix_stats
    )
    own_merged = combine_pair(own_prefix, suffix_half)
    peak_all, total_all, sum_all = tuple(
        lax.dynamic_update_slice_in_dim(whole_arr, piece_arr, row_start, 0)
        for whole_arr, piece_arr in zip(prefix_stats, own_merged)
    )

    half_units = rows_dev * step_count * half_heads
    chunk = half_units // ctx_count
    pt_rows = -(-2 * chunk // LANES)
    dests = ctx_count * row_count

    def by_dest(member, tail=()):
        shaped = member.reshape((row_count, ctx_count, chunk) + tail)
        return jnp.swapaxes(shaped, 0, 1).reshape((dests, chunk) + tail)

    pt = jnp.concatenate([by_dest(peak_all), by_dest(total_all)], axis=-1)
    pt = jnp.pad(pt, ((0, 0), (0, pt_rows * LANES - 2 * chunk)))
    outgoing = jnp.concatenate(
        [by_dest(sum_all, (HD,)), pt.reshape(dests, pt_rows, LANES)], axis=1
    )
    incoming = lax.all_to_all(
        outgoing.reshape(dests, 1, (chunk + pt_rows) * LANES),
        ("ctx", "row"),
        split_axis=0,
        concat_axis=0,
        tiled=True,
    )
    incoming = incoming.reshape(dests, chunk + pt_rows, LANES)
    got_pt = incoming[:, chunk:, :].reshape(dests, pt_rows * LANES)
    pairs = ctx_count // 2

    def by_half(member, tail=()):
        shaped = member.reshape((pairs, 2, row_count, chunk) + tail)
        return jnp.swapaxes(shaped, 0, 1).reshape((2, pairs * row_count, chunk) + tail)

    got_peak = by_half(got_pt[:, :chunk])
    got_total = by_half(got_pt[:, chunk : 2 * chunk])
    got_sum = by_half(incoming[:, :chunk, :], (HD,))

    def fresh_chunk(member, tail=()):
        shaped = member.reshape((rows_dev, step_count, 2, half_heads) + tail)
        shaped = jnp.moveaxis(shaped, 2, 0).reshape((2, half_units) + tail)
        return lax.dynamic_slice_in_dim(shaped, ctx_index * chunk, chunk, 1)

    fresh_peak = fresh_chunk(fresh_stats[0])
    fresh_total = fresh_chunk(fresh_stats[1])
    fresh_sum = fresh_chunk(fresh_stats[2], (HD,))

    top = jnp.maximum(jnp.max(got_peak, axis=1), fresh_peak)
    factor = jnp.exp(got_peak - top[:, None])
    fresh_factor = jnp.exp(fresh_peak - top)
    denom = jnp.sum(factor * got_total, axis=1) + fresh_factor * fresh_total
    numer = jnp.sum(factor[..., None] * got_sum, axis=1) + fresh_factor[..., None] * fresh_sum
    result = (numer / denom[..., None]).astype(jnp.bfloat16)
    whole = lax.all_gather(result, "ctx", axis=0, tiled=False)
    whole = jnp.swapaxes(whole, 0, 1).reshape(2, rows_dev, step_count, half_heads, HD)
    whole = jnp.moveaxis(whole, 0, 2)
    return whole.reshape(rows_dev, step_count, H * HD)


def solution(mesh):
    in_specs = (
        P("row", None, None),
        P("row"),
        P(None, ("ctx", "row"), None),
        P(None, ("ctx", "row"), None),
        P(("ctx", "row"), None, None),
        P(("ctx", "row"), None, None),
        P("row", None),
        P("row"),
        P("row", None, None),
        P("row", None, None),
    )
    out_specs = P("row", None, None)
    return jax.shard_map(
        per_device, mesh=mesh, in_specs=in_specs, out_specs=out_specs, check_vma=False
    )
```

```python
import math

import jax
import jax.numpy as jnp
from jax import lax
from jax.sharding import PartitionSpec as P

H = 32
KVH = 4
HD = 128
LANES = 128


MASKED_SCORE = -1e30


def block_stats(scores, valid_mask, values, einsum_form):
    block_peak = jnp.max(jnp.where(valid_mask, scores, MASKED_SCORE), axis=-1)
    weights = jnp.where(valid_mask, jnp.exp(scores - block_peak[..., None]), 0.0).astype(
        jnp.bfloat16
    )
    block_total = jnp.sum(weights.astype(jnp.float32), axis=-1)
    block_sum = jnp.einsum(einsum_form, weights, values, preferred_element_type=jnp.float32)
    return (block_peak, block_total, block_sum)


def combine_pair(earlier, later):
    highest = jnp.maximum(earlier[0], later[0])
    left_factor = jnp.exp(earlier[0] - highest)
    right_factor = jnp.exp(later[0] - highest)
    totals = left_factor * earlier[1] + right_factor * later[1]
    sums = left_factor[..., None] * earlier[2] + right_factor[..., None] * later[2]
    return (highest, totals, sums)


def per_device(
    queries,
    prefix_id,
    prefix_keys,
    prefix_values,
    pool_keys,
    pool_values,
    page_table,
    suffix_len,
    new_keys,
    new_values,
):
    rows_dev, step_count, feature_width = queries.shape
    groups = H // KVH
    score_scale = 1.0 / math.sqrt(HD)
    row_count = lax.axis_size("row")
    ctx_count = lax.axis_size("ctx")
    row_index = lax.axis_index("row")
    ctx_index = lax.axis_index("ctx")
    flat_index = ctx_index * row_count + row_index
    own_query = queries.reshape(rows_dev, step_count, KVH, groups, HD)

    slot_count, page_len, kv_width = pool_keys.shape
    slot_ids = flat_index * slot_count + jnp.arange(slot_count, dtype=jnp.int32)
    slot_match = page_table[:, :, None] == slot_ids[None, None, :]
    entry_pos = jnp.arange(page_table.shape[1], dtype=jnp.int32)
    page_of = jnp.sum(jnp.where(slot_match, entry_pos[None, :, None], 0), axis=1)
    owned = jnp.any(slot_match, axis=1)
    token_pos = (
        page_of[:, :, None] * page_len + jnp.arange(page_len, dtype=jnp.int32)[None, None, :]
    )
    live_mask = owned[:, :, None] & (token_pos < suffix_len[:, None, None])
    live_mask = live_mask.reshape(rows_dev, 1, 1, 1, slot_count * page_len)
    flat_keys = pool_keys.reshape(slot_count * page_len, kv_width)
    flat_values = pool_values.reshape(slot_count * page_len, KVH, HD)
    head_eye = (jnp.arange(KVH)[:, None] == jnp.arange(KVH)[None, :]).reshape(
        1, 1, KVH, 1, KVH, 1
    )
    wide_query = jnp.where(head_eye, own_query[:, :, :, :, None, :], 0).reshape(
        rows_dev, step_count, KVH, groups, kv_width
    )
    suffix_scores = (
        jnp.einsum("rskgw,tw->rskgt", wide_query, flat_keys, preferred_element_type=jnp.float32)
        * score_scale
    )
    suffix_stats = block_stats(suffix_scores, live_mask, flat_values, "rskgt,tkd->rskgd")

    fresh_keys = new_keys.reshape(rows_dev, step_count, KVH, HD)
    fresh_values = new_values.reshape(rows_dev, step_count, KVH, HD)
    fresh_scores = (
        jnp.einsum("rskgd,rtkd->rskgt", own_query, fresh_keys, preferred_element_type=jnp.float32)
        * score_scale
    )
    causal = jnp.arange(step_count)[None, :] <= jnp.arange(step_count)[:, None]
    causal = causal.reshape(1, step_count, 1, 1, step_count)
    fresh_stats = block_stats(fresh_scores, causal, fresh_values, "rskgt,rtkd->rskgd")

    core_bit = ctx_index % 2
    half_kv = KVH // 2
    half_heads = H // 2
    own_half_query = lax.dynamic_slice_in_dim(own_query, core_bit * half_kv, half_kv, 2)
    query_rows = rows_dev * step_count * half_heads * HD // LANES
    id_rows = -(-rows_dev // 16) * 16
    id_block = jnp.zeros((id_rows, LANES), jnp.bfloat16)
    id_block = id_block.at[:rows_dev, :].set(
        jnp.broadcast_to(prefix_id.astype(jnp.bfloat16)[:, None], (rows_dev, LANES))
    )
    packed = jnp.concatenate([own_half_query.reshape(query_rows, LANES), id_block], axis=0)
    fanned = jnp.broadcast_to(packed[None], (row_count,) + packed.shape)
    gathered = lax.all_to_all(fanned, "row", split_axis=0, concat_axis=0, tiled=True)
    total_rows = row_count * rows_dev
    half_query = gathered[:, :query_rows, :].reshape(
        total_rows, step_count, half_kv, groups, HD
    )
    every_prefix = gathered[:, query_rows : query_rows + rows_dev, 0].reshape(total_rows)
    every_prefix = every_prefix.astype(jnp.int32)

    swap = [(c, c ^ 1) for c in range(ctx_count)]
    span_len = prefix_keys.shape[1]
    prefix_count = prefix_keys.shape[0]
    kv_both = jnp.stack(
        [
            prefix_keys.reshape(prefix_count, span_len, KVH, HD),
            prefix_values.reshape(prefix_count, span_len, KVH, HD),
        ]
    )
    own_kv = lax.dynamic_slice_in_dim(kv_both, core_bit * half_kv, half_kv, 3)
    given_kv = lax.dynamic_slice_in_dim(kv_both, (1 - core_bit) * half_kv, half_kv, 3)
    partner_kv = lax.ppermute(given_kv, "ctx", swap)


    def prefix_block(kv):
        row_kv = jnp.take(kv, every_prefix, axis=1)
        row_keys, row_values = row_kv[0], row_kv[1]
        scores = (
            jnp.einsum(
                "rskgd,rtkd->rskgt", half_query, row_keys, preferred_element_type=jnp.float32
            )
            * score_scale
        )
        always = jnp.ones((1, 1, 1, 1, span_len), dtype=bool)
        return block_stats(scores, always, row_values, "rskgt,rtkd->rskgd")

    prefix_stats = combine_pair(prefix_block(own_kv), prefix_block(partner_kv))

    def head_half(member, at):
        return lax.dynamic_slice_in_dim(member, at * half_kv, half_kv, 2)

    suffix_packed = jnp.concatenate(
        [suffix_stats[2], suffix_stats[0][..., None], suffix_stats[1][..., None]], axis=-1
    )
    suffix_moved = lax.ppermute(head_half(suffix_packed, 1 - core_bit), "ctx", swap)
    suffix_partner = (suffix_moved[..., HD], suffix_moved[..., HD + 1], suffix_moved[..., :HD])
    suffix_kept = tuple(head_half(member, core_bit) for member in suffix_stats)
    suffix_half = combine_pair(suffix_kept, suffix_partner)

    row_start = row_index * rows_dev
    own_prefix = tuple(
        lax.dynamic_slice_in_dim(member, row_start, rows_dev, 0) for member in prefix_stats
    )
    own_merged = combine_pair(own_prefix, suffix_half)
    peak_all, total_all, sum_all = tuple(
        lax.dynamic_update_slice_in_dim(whole_arr, piece_arr, row_start, 0)
        for whole_arr, piece_arr in zip(prefix_stats, own_merged)
    )

    half_units = rows_dev * step_count * half_heads
    chunk = half_units // ctx_count
    pt_rows = -(-2 * chunk // LANES)
    dests = ctx_count * row_count

    def by_dest(member, tail=()):
        shaped = member.reshape((row_count, ctx_count, chunk) + tail)
        return jnp.swapaxes(shaped, 0, 1).reshape((dests, chunk) + tail)

    pt = jnp.concatenate([by_dest(peak_all), by_dest(total_all)], axis=-1)
    pt = jnp.pad(pt, ((0, 0), (0, pt_rows * LANES - 2 * chunk)))
    outgoing = jnp.concatenate(
        [by_dest(sum_all, (HD,)), pt.reshape(dests, pt_rows, LANES)], axis=1
    )
    incoming = lax.all_to_all(
        outgoing.reshape(dests, 1, (chunk + pt_rows) * LANES),
        ("ctx", "row"),
        split_axis=0,
        concat_axis=0,
        tiled=True,
    )
    incoming = incoming.reshape(dests, chunk + pt_rows, LANES)
    got_pt = incoming[:, chunk:, :].reshape(dests, pt_rows * LANES)
    pairs = ctx_count // 2

    def by_half(member, tail=()):
        shaped = member.reshape((pairs, 2, row_count, chunk) + tail)
        return jnp.swapaxes(shaped, 0, 1).reshape((2, pairs * row_count, chunk) + tail)

    got_peak = by_half(got_pt[:, :chunk])
    got_total = by_half(got_pt[:, chunk : 2 * chunk])
    got_sum = by_half(incoming[:, :chunk, :], (HD,))

    def fresh_chunk(member, tail=()):
        shaped = member.reshape((rows_dev, step_count, 2, half_heads) + tail)
        shaped = jnp.moveaxis(shaped, 2, 0).reshape((2, half_units) + tail)
        return lax.dynamic_slice_in_dim(shaped, ctx_index * chunk, chunk, 1)

    fresh_peak = fresh_chunk(fresh_stats[0])
    fresh_total = fresh_chunk(fresh_stats[1])
    fresh_sum = fresh_chunk(fresh_stats[2], (HD,))

    top = jnp.maximum(jnp.max(got_peak, axis=1), fresh_peak)
    factor = jnp.exp(got_peak - top[:, None])
    fresh_factor = jnp.exp(fresh_peak - top)
    denom = jnp.sum(factor * got_total, axis=1) + fresh_factor * fresh_total
    numer = jnp.sum(factor[..., None] * got_sum, axis=1) + fresh_factor[..., None] * fresh_sum
    result = (numer / denom[..., None]).astype(jnp.bfloat16)
    whole = lax.all_gather(result, "ctx", axis=0, tiled=False)
    whole = jnp.swapaxes(whole, 0, 1).reshape(2, rows_dev, step_count, half_heads, HD)
    whole = jnp.moveaxis(whole, 0, 2)
    return whole.reshape(rows_dev, step_count, H * HD)


def solution(mesh):
    in_specs = (
        P("row", None, None),
        P("row"),
        P(None, ("ctx", "row"), None),
        P(None, ("ctx", "row"), None),
        P(("ctx", "row"), None, None),
        P(("ctx", "row"), None, None),
        P("row", None),
        P("row"),
        P("row", None, None),
        P("row", None, None),
    )
    out_specs = P("row", None, None)
    return jax.shard_map(
        per_device, mesh=mesh, in_specs=in_specs, out_specs=out_specs, check_vma=False
    )
```

```python
import math

import jax
import jax.numpy as jnp
from jax import lax
from jax.sharding import PartitionSpec as P

H = 32
KVH = 4
HD = 128
LANES = 128


MASKED_SCORE = -1e30


def block_stats(scores, valid_mask, values, einsum_form):
    block_peak = jnp.max(jnp.where(valid_mask, scores, MASKED_SCORE), axis=-1)
    weights = jnp.where(valid_mask, jnp.exp(scores - block_peak[..., None]), 0.0).astype(
        jnp.bfloat16
    )
    block_total = jnp.sum(weights.astype(jnp.float32), axis=-1)
    block_sum = jnp.einsum(einsum_form, weights, values, preferred_element_type=jnp.float32)
    return (block_peak, block_total, block_sum)


def combine_pair(earlier, later):
    highest = jnp.maximum(earlier[0], later[0])
    left_factor = jnp.exp(earlier[0] - highest)
    right_factor = jnp.exp(later[0] - highest)
    totals = left_factor * earlier[1] + right_factor * later[1]
    sums = left_factor[..., None] * earlier[2] + right_factor[..., None] * later[2]
    return (highest, totals, sums)


def per_device(
    queries,
    prefix_id,
    prefix_keys,
    prefix_values,
    pool_keys,
    pool_values,
    page_table,
    suffix_len,
    new_keys,
    new_values,
):
    rows_dev, step_count, feature_width = queries.shape
    groups = H // KVH
    score_scale = 1.0 / math.sqrt(HD)
    row_count = lax.axis_size("row")
    ctx_count = lax.axis_size("ctx")
    row_index = lax.axis_index("row")
    ctx_index = lax.axis_index("ctx")
    flat_index = ctx_index * row_count + row_index
    own_query = queries.reshape(rows_dev, step_count, KVH, groups, HD)

    slot_count, page_len, kv_width = pool_keys.shape
    slot_ids = flat_index * slot_count + jnp.arange(slot_count, dtype=jnp.int32)
    slot_match = page_table[:, :, None] == slot_ids[None, None, :]
    entry_pos = jnp.arange(page_table.shape[1], dtype=jnp.int32)
    page_of = jnp.sum(jnp.where(slot_match, entry_pos[None, :, None], 0), axis=1)
    owned = jnp.any(slot_match, axis=1)
    token_pos = (
        page_of[:, :, None] * page_len + jnp.arange(page_len, dtype=jnp.int32)[None, None, :]
    )
    live_mask = owned[:, :, None] & (token_pos < suffix_len[:, None, None])
    live_mask = live_mask.reshape(rows_dev, 1, 1, 1, slot_count * page_len)
    flat_keys = pool_keys.reshape(slot_count * page_len, kv_width)
    flat_values = pool_values.reshape(slot_count * page_len, KVH, HD)
    head_eye = (jnp.arange(KVH)[:, None] == jnp.arange(KVH)[None, :]).reshape(
        1, 1, KVH, 1, KVH, 1
    )
    wide_query = jnp.where(head_eye, own_query[:, :, :, :, None, :], 0).reshape(
        rows_dev, step_count, KVH, groups, kv_width
    )
    suffix_scores = (
        jnp.einsum("rskgw,tw->rskgt", wide_query, flat_keys, preferred_element_type=jnp.float32)
        * score_scale
    )
    suffix_stats = block_stats(suffix_scores, live_mask, flat_values, "rskgt,tkd->rskgd")

    fresh_keys = new_keys.reshape(rows_dev, step_count, KVH, HD)
    fresh_values = new_values.reshape(rows_dev, step_count, KVH, HD)
    fresh_scores = (
        jnp.einsum("rskgd,rtkd->rskgt", own_query, fresh_keys, preferred_element_type=jnp.float32)
        * score_scale
    )
    causal = jnp.arange(step_count)[None, :] <= jnp.arange(step_count)[:, None]
    causal = causal.reshape(1, step_count, 1, 1, step_count)
    fresh_stats = block_stats(fresh_scores, causal, fresh_values, "rskgt,rtkd->rskgd")

    core_bit = ctx_index % 2
    half_kv = KVH // 2
    half_heads = H // 2
    own_half_query = lax.dynamic_slice_in_dim(own_query, core_bit * half_kv, half_kv, 2)
    query_rows = rows_dev * step_count * half_heads * HD // LANES
    id_rows = -(-rows_dev // 16) * 16
    id_block = jnp.zeros((id_rows, LANES), jnp.bfloat16)
    id_block = id_block.at[:rows_dev, :].set(
        jnp.broadcast_to(prefix_id.astype(jnp.bfloat16)[:, None], (rows_dev, LANES))
    )
    packed = jnp.concatenate([own_half_query.reshape(query_rows, LANES), id_block], axis=0)
    fanned = jnp.broadcast_to(packed[None], (row_count,) + packed.shape)
    gathered = lax.all_to_all(fanned, "row", split_axis=0, concat_axis=0, tiled=True)
    total_rows = row_count * rows_dev
    half_query = gathered[:, :query_rows, :].reshape(
        total_rows, step_count, half_kv, groups, HD
    )
    every_prefix = gathered[:, query_rows : query_rows + rows_dev, 0].reshape(total_rows)
    every_prefix = every_prefix.astype(jnp.int32)

    swap = [(c, c ^ 1) for c in range(ctx_count)]
    span_len = prefix_keys.shape[1]
    prefix_count = prefix_keys.shape[0]
    lane_half = half_kv * HD

    def lane_half_of(member, at):
        return lax.dynamic_slice_in_dim(member, at * lane_half, lane_half, 2)

    own_kv = jnp.stack(
        [lane_half_of(prefix_keys, core_bit), lane_half_of(prefix_values, core_bit)]
    )
    given_kv = jnp.stack(
        [lane_half_of(prefix_keys, 1 - core_bit), lane_half_of(prefix_values, 1 - core_bit)]
    )
    partner_kv = lax.ppermute(given_kv, "ctx", swap)


    def prefix_block(kv):
        row_kv = jnp.take(kv, every_prefix, axis=1).reshape(
            2, total_rows, span_len, half_kv, HD
        )
        row_keys, row_values = row_kv[0], row_kv[1]
        scores = (
            jnp.einsum(
                "rskgd,rtkd->rskgt", half_query, row_keys, preferred_element_type=jnp.float32
            )
            * score_scale
        )
        always = jnp.ones((1, 1, 1, 1, span_len), dtype=bool)
        return block_stats(scores, always, row_values, "rskgt,rtkd->rskgd")

    prefix_stats = combine_pair(prefix_block(own_kv), prefix_block(partner_kv))

    def head_half(member, at):
        return lax.dynamic_slice_in_dim(member, at * half_kv, half_kv, 2)

    suffix_packed = jnp.concatenate(
        [suffix_stats[2], suffix_stats[0][..., None], suffix_stats[1][..., None]], axis=-1
    )
    suffix_moved = lax.ppermute(head_half(suffix_packed, 1 - core_bit), "ctx", swap)
    suffix_partner = (suffix_moved[..., HD], suffix_moved[..., HD + 1], suffix_moved[..., :HD])
    suffix_kept = tuple(head_half(member, core_bit) for member in suffix_stats)
    suffix_half = combine_pair(suffix_kept, suffix_partner)

    row_start = row_index * rows_dev
    own_prefix = tuple(
        lax.dynamic_slice_in_dim(member, row_start, rows_dev, 0) for member in prefix_stats
    )
    own_merged = combine_pair(own_prefix, suffix_half)
    peak_all, total_all, sum_all = tuple(
        lax.dynamic_update_slice_in_dim(whole_arr, piece_arr, row_start, 0)
        for whole_arr, piece_arr in zip(prefix_stats, own_merged)
    )

    half_units = rows_dev * step_count * half_heads
    chunk = half_units // ctx_count
    pt_rows = -(-2 * chunk // LANES)
    dests = ctx_count * row_count

    def by_dest(member, tail=()):
        shaped = member.reshape((row_count, ctx_count, chunk) + tail)
        return jnp.swapaxes(shaped, 0, 1).reshape((dests, chunk) + tail)

    pt = jnp.concatenate([by_dest(peak_all), by_dest(total_all)], axis=-1)
    pt = jnp.pad(pt, ((0, 0), (0, pt_rows * LANES - 2 * chunk)))
    outgoing = jnp.concatenate(
        [by_dest(sum_all, (HD,)), pt.reshape(dests, pt_rows, LANES)], axis=1
    )
    incoming = lax.all_to_all(
        outgoing.reshape(dests, 1, (chunk + pt_rows) * LANES),
        ("ctx", "row"),
        split_axis=0,
        concat_axis=0,
        tiled=True,
    )
    incoming = incoming.reshape(dests, chunk + pt_rows, LANES)
    got_pt = incoming[:, chunk:, :].reshape(dests, pt_rows * LANES)
    pairs = ctx_count // 2

    def by_half(member, tail=()):
        shaped = member.reshape((pairs, 2, row_count, chunk) + tail)
        return jnp.swapaxes(shaped, 0, 1).reshape((2, pairs * row_count, chunk) + tail)

    got_peak = by_half(got_pt[:, :chunk])
    got_total = by_half(got_pt[:, chunk : 2 * chunk])
    got_sum = by_half(incoming[:, :chunk, :], (HD,))

    def fresh_chunk(member, tail=()):
        shaped = member.reshape((rows_dev, step_count, 2, half_heads) + tail)
        shaped = jnp.moveaxis(shaped, 2, 0).reshape((2, half_units) + tail)
        return lax.dynamic_slice_in_dim(shaped, ctx_index * chunk, chunk, 1)

    fresh_peak = fresh_chunk(fresh_stats[0])
    fresh_total = fresh_chunk(fresh_stats[1])
    fresh_sum = fresh_chunk(fresh_stats[2], (HD,))

    top = jnp.maximum(jnp.max(got_peak, axis=1), fresh_peak)
    factor = jnp.exp(got_peak - top[:, None])
    fresh_factor = jnp.exp(fresh_peak - top)
    denom = jnp.sum(factor * got_total, axis=1) + fresh_factor * fresh_total
    numer = jnp.sum(factor[..., None] * got_sum, axis=1) + fresh_factor[..., None] * fresh_sum
    result = (numer / denom[..., None]).astype(jnp.bfloat16)
    whole = lax.all_gather(result, "ctx", axis=0, tiled=False)
    whole = jnp.swapaxes(whole, 0, 1).reshape(2, rows_dev, step_count, half_heads, HD)
    whole = jnp.moveaxis(whole, 0, 2)
    return whole.reshape(rows_dev, step_count, H * HD)


def solution(mesh):
    in_specs = (
        P("row", None, None),
        P("row"),
        P(None, ("ctx", "row"), None),
        P(None, ("ctx", "row"), None),
        P(("ctx", "row"), None, None),
        P(("ctx", "row"), None, None),
        P("row", None),
        P("row"),
        P("row", None, None),
        P("row", None, None),
    )
    out_specs = P("row", None, None)
    return jax.shard_map(
        per_device, mesh=mesh, in_specs=in_specs, out_specs=out_specs, check_vma=False
    )
```

```python
import math

import jax
import jax.numpy as jnp
from jax import lax
from jax.sharding import PartitionSpec as P

H = 32
KVH = 4
HD = 128
LANES = 128


MASKED_SCORE = -1e30


def block_stats(scores, valid_mask, values, einsum_form):
    block_peak = jnp.max(jnp.where(valid_mask, scores, MASKED_SCORE), axis=-1)
    weights = jnp.where(valid_mask, jnp.exp(scores - block_peak[..., None]), 0.0).astype(
        jnp.bfloat16
    )
    block_total = jnp.sum(weights.astype(jnp.float32), axis=-1)
    block_sum = jnp.einsum(einsum_form, weights, values, preferred_element_type=jnp.float32)
    return (block_peak, block_total, block_sum)


def combine_pair(earlier, later):
    highest = jnp.maximum(earlier[0], later[0])
    left_factor = jnp.exp(earlier[0] - highest)
    right_factor = jnp.exp(later[0] - highest)
    totals = left_factor * earlier[1] + right_factor * later[1]
    sums = left_factor[..., None] * earlier[2] + right_factor[..., None] * later[2]
    return (highest, totals, sums)


def per_device(
    queries,
    prefix_id,
    prefix_keys,
    prefix_values,
    pool_keys,
    pool_values,
    page_table,
    suffix_len,
    new_keys,
    new_values,
):
    rows_dev, step_count, feature_width = queries.shape
    groups = H // KVH
    score_scale = 1.0 / math.sqrt(HD)
    row_count = lax.axis_size("row")
    ctx_count = lax.axis_size("ctx")
    row_index = lax.axis_index("row")
    ctx_index = lax.axis_index("ctx")
    flat_index = ctx_index * row_count + row_index
    own_query = queries.reshape(rows_dev, step_count, KVH, groups, HD)

    slot_count, page_len, kv_width = pool_keys.shape
    slot_ids = flat_index * slot_count + jnp.arange(slot_count, dtype=jnp.int32)
    slot_match = page_table[:, :, None] == slot_ids[None, None, :]
    entry_pos = jnp.arange(page_table.shape[1], dtype=jnp.int32)
    page_of = jnp.sum(jnp.where(slot_match, entry_pos[None, :, None], 0), axis=1)
    owned = jnp.any(slot_match, axis=1)
    token_pos = (
        page_of[:, :, None] * page_len + jnp.arange(page_len, dtype=jnp.int32)[None, None, :]
    )
    live_mask = owned[:, :, None] & (token_pos < suffix_len[:, None, None])
    live_mask = live_mask.reshape(rows_dev, 1, 1, 1, slot_count * page_len)
    flat_keys = pool_keys.reshape(slot_count * page_len, kv_width)
    flat_values = pool_values.reshape(slot_count * page_len, KVH, HD)
    head_eye = (jnp.arange(KVH)[:, None] == jnp.arange(KVH)[None, :]).reshape(
        1, 1, KVH, 1, KVH, 1
    )
    wide_query = jnp.where(head_eye, own_query[:, :, :, :, None, :], 0).reshape(
        rows_dev, step_count, KVH, groups, kv_width
    )
    suffix_scores = (
        jnp.einsum("rskgw,tw->rskgt", wide_query, flat_keys, preferred_element_type=jnp.float32)
        * score_scale
    )
    suffix_stats = block_stats(suffix_scores, live_mask, flat_values, "rskgt,tkd->rskgd")

    fresh_keys = new_keys.reshape(rows_dev, step_count, KVH, HD)
    fresh_values = new_values.reshape(rows_dev, step_count, KVH, HD)
    fresh_scores = (
        jnp.einsum("rskgd,rtkd->rskgt", own_query, fresh_keys, preferred_element_type=jnp.float32)
        * score_scale
    )
    causal = jnp.arange(step_count)[None, :] <= jnp.arange(step_count)[:, None]
    causal = causal.reshape(1, step_count, 1, 1, step_count)
    fresh_stats = block_stats(fresh_scores, causal, fresh_values, "rskgt,rtkd->rskgd")

    core_bit = ctx_index % 2
    half_kv = KVH // 2
    half_heads = H // 2
    own_half_query = lax.dynamic_slice_in_dim(own_query, core_bit * half_kv, half_kv, 2)
    query_rows = rows_dev * step_count * half_heads * HD // LANES
    id_rows = -(-rows_dev // 16) * 16
    id_block = jnp.zeros((id_rows, LANES), jnp.bfloat16)
    id_block = id_block.at[:rows_dev, :].set(
        jnp.broadcast_to(prefix_id.astype(jnp.bfloat16)[:, None], (rows_dev, LANES))
    )
    packed = jnp.concatenate([own_half_query.reshape(query_rows, LANES), id_block], axis=0)
    fanned = jnp.broadcast_to(packed[None], (row_count,) + packed.shape)
    gathered = lax.all_to_all(fanned, "row", split_axis=0, concat_axis=0, tiled=True)
    total_rows = row_count * rows_dev
    half_query = gathered[:, :query_rows, :].reshape(
        total_rows, step_count, half_kv, groups, HD
    )
    every_prefix = gathered[:, query_rows : query_rows + rows_dev, 0].reshape(total_rows)
    every_prefix = every_prefix.astype(jnp.int32)

    swap = [(c, c ^ 1) for c in range(ctx_count)]
    span_len = prefix_keys.shape[1]
    prefix_count = prefix_keys.shape[0]
    kv_both = jnp.stack(
        [
            prefix_keys.reshape(prefix_count, span_len, KVH, HD),
            prefix_values.reshape(prefix_count, span_len, KVH, HD),
        ]
    )
    own_kv = lax.dynamic_slice_in_dim(kv_both, core_bit * half_kv, half_kv, 3)
    given_kv = lax.dynamic_slice_in_dim(kv_both, (1 - core_bit) * half_kv, half_kv, 3)
    partner_kv = lax.ppermute(given_kv, "ctx", swap)


    def prefix_block(kv):
        row_kv = jnp.take(kv, every_prefix, axis=1)
        row_keys, row_values = row_kv[0], row_kv[1]
        scores = (
            jnp.einsum(
                "rskgd,rtkd->rskgt", half_query, row_keys, preferred_element_type=jnp.float32
            )
            * score_scale
        )
        always = jnp.ones((1, 1, 1, 1, span_len), dtype=bool)
        return block_stats(scores, always, row_values, "rskgt,rtkd->rskgd")

    prefix_stats = combine_pair(prefix_block(own_kv), prefix_block(partner_kv))

    def head_half(member, at):
        return lax.dynamic_slice_in_dim(member, at * half_kv, half_kv, 2)

    suffix_packed = jnp.concatenate(
        [suffix_stats[2], suffix_stats[0][..., None], suffix_stats[1][..., None]], axis=-1
    )
    suffix_moved = lax.ppermute(head_half(suffix_packed, 1 - core_bit), "ctx", swap)
    suffix_partner = (suffix_moved[..., HD], suffix_moved[..., HD + 1], suffix_moved[..., :HD])
    suffix_kept = tuple(head_half(member, core_bit) for member in suffix_stats)
    suffix_half = combine_pair(suffix_kept, suffix_partner)

    row_start = row_index * rows_dev
    own_prefix = tuple(
        lax.dynamic_slice_in_dim(member, row_start, rows_dev, 0) for member in prefix_stats
    )
    own_merged = combine_pair(own_prefix, suffix_half)
    peak_all, total_all, sum_all = tuple(
        lax.dynamic_update_slice_in_dim(whole_arr, piece_arr, row_start, 0)
        for whole_arr, piece_arr in zip(prefix_stats, own_merged)
    )

    half_units = rows_dev * step_count * half_heads
    chunk = half_units // ctx_count
    pt_rows = -(-2 * chunk // LANES)
    dests = ctx_count * row_count

    def by_dest(member, tail=()):
        return member.reshape((dests, chunk) + tail)

    pt = jnp.concatenate([by_dest(peak_all), by_dest(total_all)], axis=-1)
    pt = jnp.pad(pt, ((0, 0), (0, pt_rows * LANES - 2 * chunk)))
    outgoing = jnp.concatenate(
        [by_dest(sum_all, (HD,)), pt.reshape(dests, pt_rows, LANES)], axis=1
    )
    incoming = lax.all_to_all(
        outgoing.reshape(dests, 1, (chunk + pt_rows) * LANES),
        ("row", "ctx"),
        split_axis=0,
        concat_axis=0,
        tiled=True,
    )
    incoming = incoming.reshape(dests, chunk + pt_rows, LANES)
    got_pt = incoming[:, chunk:, :].reshape(dests, pt_rows * LANES)
    pairs = ctx_count // 2

    def by_half(member, tail=()):
        shaped = member.reshape((row_count, pairs, 2, chunk) + tail)
        return jnp.moveaxis(shaped, 2, 0).reshape((2, row_count * pairs, chunk) + tail)

    got_peak = by_half(got_pt[:, :chunk])
    got_total = by_half(got_pt[:, chunk : 2 * chunk])
    got_sum = by_half(incoming[:, :chunk, :], (HD,))

    def fresh_chunk(member, tail=()):
        shaped = member.reshape((rows_dev, step_count, 2, half_heads) + tail)
        shaped = jnp.moveaxis(shaped, 2, 0).reshape((2, half_units) + tail)
        return lax.dynamic_slice_in_dim(shaped, ctx_index * chunk, chunk, 1)

    fresh_peak = fresh_chunk(fresh_stats[0])
    fresh_total = fresh_chunk(fresh_stats[1])
    fresh_sum = fresh_chunk(fresh_stats[2], (HD,))

    top = jnp.maximum(jnp.max(got_peak, axis=1), fresh_peak)
    factor = jnp.exp(got_peak - top[:, None])
    fresh_factor = jnp.exp(fresh_peak - top)
    denom = jnp.sum(factor * got_total, axis=1) + fresh_factor * fresh_total
    numer = jnp.sum(factor[..., None] * got_sum, axis=1) + fresh_factor[..., None] * fresh_sum
    result = (numer / denom[..., None]).astype(jnp.bfloat16)
    whole = lax.all_gather(result, "ctx", axis=0, tiled=False)
    whole = jnp.swapaxes(whole, 0, 1).reshape(2, rows_dev, step_count, half_heads, HD)
    whole = jnp.moveaxis(whole, 0, 2)
    return whole.reshape(rows_dev, step_count, H * HD)


def solution(mesh):
    in_specs = (
        P("row", None, None),
        P("row"),
        P(None, ("ctx", "row"), None),
        P(None, ("ctx", "row"), None),
        P(("ctx", "row"), None, None),
        P(("ctx", "row"), None, None),
        P("row", None),
        P("row"),
        P("row", None, None),
        P("row", None, None),
    )
    out_specs = P("row", None, None)
    return jax.shard_map(
        per_device, mesh=mesh, in_specs=in_specs, out_specs=out_specs, check_vma=False
    )
```

```python
import math

import jax
import jax.numpy as jnp
from jax import lax
from jax.sharding import PartitionSpec as P

H = 32
KVH = 4
HD = 128
LANES = 128


MASKED_SCORE = -1e30


def block_stats(scores, valid_mask, values, einsum_form):
    block_peak = jnp.max(jnp.where(valid_mask, scores, MASKED_SCORE), axis=-1)
    weights = jnp.where(valid_mask, jnp.exp(scores - block_peak[..., None]), 0.0).astype(
        jnp.bfloat16
    )
    block_total = jnp.sum(weights.astype(jnp.float32), axis=-1)
    block_sum = jnp.einsum(einsum_form, weights, values, preferred_element_type=jnp.float32)
    return (block_peak, block_total, block_sum)


def combine_pair(earlier, later):
    highest = jnp.maximum(earlier[0], later[0])
    left_factor = jnp.exp(earlier[0] - highest)
    right_factor = jnp.exp(later[0] - highest)
    totals = left_factor * earlier[1] + right_factor * later[1]
    sums = left_factor[..., None] * earlier[2] + right_factor[..., None] * later[2]
    return (highest, totals, sums)


def per_device(
    queries,
    prefix_id,
    prefix_keys,
    prefix_values,
    pool_keys,
    pool_values,
    page_table,
    suffix_len,
    new_keys,
    new_values,
):
    rows_dev, step_count, feature_width = queries.shape
    groups = H // KVH
    score_scale = 1.0 / math.sqrt(HD)
    row_count = lax.axis_size("row")
    ctx_count = lax.axis_size("ctx")
    row_index = lax.axis_index("row")
    ctx_index = lax.axis_index("ctx")
    flat_index = ctx_index * row_count + row_index
    own_query = queries.reshape(rows_dev, step_count, KVH, groups, HD)

    slot_count, page_len, kv_width = pool_keys.shape
    slot_ids = flat_index * slot_count + jnp.arange(slot_count, dtype=jnp.int32)
    slot_match = page_table[:, :, None] == slot_ids[None, None, :]
    entry_pos = jnp.arange(page_table.shape[1], dtype=jnp.int32)
    page_of = jnp.sum(jnp.where(slot_match, entry_pos[None, :, None], 0), axis=1)
    owned = jnp.any(slot_match, axis=1)
    token_pos = (
        page_of[:, :, None] * page_len + jnp.arange(page_len, dtype=jnp.int32)[None, None, :]
    )
    live_mask = owned[:, :, None] & (token_pos < suffix_len[:, None, None])
    live_mask = live_mask.reshape(rows_dev, 1, 1, 1, slot_count * page_len)
    flat_keys = pool_keys.reshape(slot_count * page_len, kv_width)
    flat_values = pool_values.reshape(slot_count * page_len, KVH, HD)
    head_eye = (jnp.arange(KVH)[:, None] == jnp.arange(KVH)[None, :]).reshape(
        1, 1, KVH, 1, KVH, 1
    )
    wide_query = jnp.where(head_eye, own_query[:, :, :, :, None, :], 0).reshape(
        rows_dev, step_count, KVH, groups, kv_width
    )
    suffix_scores = (
        jnp.einsum("rskgw,tw->rskgt", wide_query, flat_keys, preferred_element_type=jnp.float32)
        * score_scale
    )
    suffix_stats = block_stats(suffix_scores, live_mask, flat_values, "rskgt,tkd->rskgd")

    fresh_keys = new_keys.reshape(rows_dev, step_count, KVH, HD)
    fresh_values = new_values.reshape(rows_dev, step_count, KVH, HD)
    fresh_scores = (
        jnp.einsum("rskgd,rtkd->rskgt", own_query, fresh_keys, preferred_element_type=jnp.float32)
        * score_scale
    )
    causal = jnp.arange(step_count)[None, :] <= jnp.arange(step_count)[:, None]
    causal = causal.reshape(1, step_count, 1, 1, step_count)
    fresh_stats = block_stats(fresh_scores, causal, fresh_values, "rskgt,rtkd->rskgd")

    core_bit = ctx_index % 2
    half_kv = KVH // 2
    half_heads = H // 2
    own_half_query = lax.dynamic_slice_in_dim(own_query, core_bit * half_kv, half_kv, 2)
    query_rows = rows_dev * step_count * half_heads * HD // LANES
    id_rows = -(-rows_dev // 16) * 16
    id_block = jnp.zeros((id_rows, LANES), jnp.bfloat16)
    id_block = id_block.at[:rows_dev, :].set(
        jnp.broadcast_to(prefix_id.astype(jnp.bfloat16)[:, None], (rows_dev, LANES))
    )
    packed = jnp.concatenate([own_half_query.reshape(query_rows, LANES), id_block], axis=0)
    fanned = jnp.broadcast_to(packed[None], (row_count,) + packed.shape)
    gathered = lax.all_to_all(fanned, "row", split_axis=0, concat_axis=0, tiled=True)
    total_rows = row_count * rows_dev
    half_query = gathered[:, :query_rows, :].reshape(
        total_rows, step_count, half_kv, groups, HD
    )
    every_prefix = gathered[:, query_rows : query_rows + rows_dev, 0].reshape(total_rows)
    every_prefix = every_prefix.astype(jnp.int32)

    swap = [(c, c ^ 1) for c in range(ctx_count)]
    prefix_keys, prefix_values, _ = lax.optimization_barrier(
        (prefix_keys, prefix_values, suffix_stats[0])
    )
    span_len = prefix_keys.shape[1]
    prefix_count = prefix_keys.shape[0]
    kv_both = jnp.stack(
        [
            prefix_keys.reshape(prefix_count, span_len, KVH, HD),
            prefix_values.reshape(prefix_count, span_len, KVH, HD),
        ]
    )
    own_kv = lax.dynamic_slice_in_dim(kv_both, core_bit * half_kv, half_kv, 3)
    given_kv = lax.dynamic_slice_in_dim(kv_both, (1 - core_bit) * half_kv, half_kv, 3)
    partner_kv = lax.ppermute(given_kv, "ctx", swap)


    def prefix_block(kv):
        row_kv = jnp.take(kv, every_prefix, axis=1)
        row_keys, row_values = row_kv[0], row_kv[1]
        scores = (
            jnp.einsum(
                "rskgd,rtkd->rskgt", half_query, row_keys, preferred_element_type=jnp.float32
            )
            * score_scale
        )
        always = jnp.ones((1, 1, 1, 1, span_len), dtype=bool)
        return block_stats(scores, always, row_values, "rskgt,rtkd->rskgd")

    prefix_stats = combine_pair(prefix_block(own_kv), prefix_block(partner_kv))

    def head_half(member, at):
        return lax.dynamic_slice_in_dim(member, at * half_kv, half_kv, 2)

    suffix_packed = jnp.concatenate(
        [suffix_stats[2], suffix_stats[0][..., None], suffix_stats[1][..., None]], axis=-1
    )
    suffix_moved = lax.ppermute(head_half(suffix_packed, 1 - core_bit), "ctx", swap)
    suffix_partner = (suffix_moved[..., HD], suffix_moved[..., HD + 1], suffix_moved[..., :HD])
    suffix_kept = tuple(head_half(member, core_bit) for member in suffix_stats)
    suffix_half = combine_pair(suffix_kept, suffix_partner)

    row_start = row_index * rows_dev
    own_prefix = tuple(
        lax.dynamic_slice_in_dim(member, row_start, rows_dev, 0) for member in prefix_stats
    )
    own_merged = combine_pair(own_prefix, suffix_half)
    peak_all, total_all, sum_all = tuple(
        lax.dynamic_update_slice_in_dim(whole_arr, piece_arr, row_start, 0)
        for whole_arr, piece_arr in zip(prefix_stats, own_merged)
    )

    half_units = rows_dev * step_count * half_heads
    chunk = half_units // ctx_count
    pt_rows = -(-2 * chunk // LANES)
    dests = ctx_count * row_count

    def by_dest(member, tail=()):
        return member.reshape((dests, chunk) + tail)

    pt = jnp.concatenate([by_dest(peak_all), by_dest(total_all)], axis=-1)
    pt = jnp.pad(pt, ((0, 0), (0, pt_rows * LANES - 2 * chunk)))
    outgoing = jnp.concatenate(
        [by_dest(sum_all, (HD,)), pt.reshape(dests, pt_rows, LANES)], axis=1
    )
    incoming = lax.all_to_all(
        outgoing.reshape(dests, 1, (chunk + pt_rows) * LANES),
        ("row", "ctx"),
        split_axis=0,
        concat_axis=0,
        tiled=True,
    )
    incoming = incoming.reshape(dests, chunk + pt_rows, LANES)
    got_pt = incoming[:, chunk:, :].reshape(dests, pt_rows * LANES)
    pairs = ctx_count // 2

    def by_half(member, tail=()):
        shaped = member.reshape((row_count, pairs, 2, chunk) + tail)
        return jnp.moveaxis(shaped, 2, 0).reshape((2, row_count * pairs, chunk) + tail)

    got_peak = by_half(got_pt[:, :chunk])
    got_total = by_half(got_pt[:, chunk : 2 * chunk])
    got_sum = by_half(incoming[:, :chunk, :], (HD,))

    def fresh_chunk(member, tail=()):
        shaped = member.reshape((rows_dev, step_count, 2, half_heads) + tail)
        shaped = jnp.moveaxis(shaped, 2, 0).reshape((2, half_units) + tail)
        return lax.dynamic_slice_in_dim(shaped, ctx_index * chunk, chunk, 1)

    fresh_peak = fresh_chunk(fresh_stats[0])
    fresh_total = fresh_chunk(fresh_stats[1])
    fresh_sum = fresh_chunk(fresh_stats[2], (HD,))

    top = jnp.maximum(jnp.max(got_peak, axis=1), fresh_peak)
    factor = jnp.exp(got_peak - top[:, None])
    fresh_factor = jnp.exp(fresh_peak - top)
    denom = jnp.sum(factor * got_total, axis=1) + fresh_factor * fresh_total
    numer = jnp.sum(factor[..., None] * got_sum, axis=1) + fresh_factor[..., None] * fresh_sum
    result = (numer / denom[..., None]).astype(jnp.bfloat16)
    whole = lax.all_gather(result, "ctx", axis=0, tiled=False)
    whole = jnp.swapaxes(whole, 0, 1).reshape(2, rows_dev, step_count, half_heads, HD)
    whole = jnp.moveaxis(whole, 0, 2)
    return whole.reshape(rows_dev, step_count, H * HD)


def solution(mesh):
    in_specs = (
        P("row", None, None),
        P("row"),
        P(None, ("ctx", "row"), None),
        P(None, ("ctx", "row"), None),
        P(("ctx", "row"), None, None),
        P(("ctx", "row"), None, None),
        P("row", None),
        P("row"),
        P("row", None, None),
        P("row", None, None),
    )
    out_specs = P("row", None, None)
    return jax.shard_map(
        per_device, mesh=mesh, in_specs=in_specs, out_specs=out_specs, check_vma=False
    )
```

```python
import math

import jax
import jax.numpy as jnp
from jax import lax
from jax.sharding import PartitionSpec as P

H = 32
KVH = 4
HD = 128
LANES = 128


MASKED_SCORE = -1e30


def block_stats(scores, valid_mask, values, einsum_form):
    block_peak = jnp.max(jnp.where(valid_mask, scores, MASKED_SCORE), axis=-1)
    weights = jnp.where(valid_mask, jnp.exp(scores - block_peak[..., None]), 0.0).astype(
        jnp.bfloat16
    )
    block_total = jnp.sum(weights.astype(jnp.float32), axis=-1)
    block_sum = jnp.einsum(einsum_form, weights, values, preferred_element_type=jnp.float32)
    return (block_peak, block_total, block_sum)


def combine_pair(earlier, later):
    highest = jnp.maximum(earlier[0], later[0])
    left_factor = jnp.exp(earlier[0] - highest)
    right_factor = jnp.exp(later[0] - highest)
    totals = left_factor * earlier[1] + right_factor * later[1]
    sums = left_factor[..., None] * earlier[2] + right_factor[..., None] * later[2]
    return (highest, totals, sums)


def per_device(
    queries,
    prefix_id,
    prefix_keys,
    prefix_values,
    pool_keys,
    pool_values,
    page_table,
    suffix_len,
    new_keys,
    new_values,
):
    rows_dev, step_count, feature_width = queries.shape
    groups = H // KVH
    score_scale = 1.0 / math.sqrt(HD)
    row_count = lax.axis_size("row")
    ctx_count = lax.axis_size("ctx")
    row_index = lax.axis_index("row")
    ctx_index = lax.axis_index("ctx")
    flat_index = ctx_index * row_count + row_index
    own_query = queries.reshape(rows_dev, step_count, KVH, groups, HD)

    slot_count, page_len, kv_width = pool_keys.shape
    slot_ids = flat_index * slot_count + jnp.arange(slot_count, dtype=jnp.int32)
    slot_match = page_table[:, :, None] == slot_ids[None, None, :]
    entry_pos = jnp.arange(page_table.shape[1], dtype=jnp.int32)
    page_of = jnp.sum(jnp.where(slot_match, entry_pos[None, :, None], 0), axis=1)
    owned = jnp.any(slot_match, axis=1)
    token_pos = (
        page_of[:, :, None] * page_len + jnp.arange(page_len, dtype=jnp.int32)[None, None, :]
    )
    live_mask = owned[:, :, None] & (token_pos < suffix_len[:, None, None])
    live_mask = live_mask.reshape(rows_dev, 1, 1, 1, slot_count * page_len)
    flat_keys = pool_keys.reshape(slot_count * page_len, kv_width)
    flat_values = pool_values.reshape(slot_count * page_len, KVH, HD)
    head_eye = (jnp.arange(KVH)[:, None] == jnp.arange(KVH)[None, :]).reshape(
        1, 1, KVH, 1, KVH, 1
    )
    wide_query = jnp.where(head_eye, own_query[:, :, :, :, None, :], 0).reshape(
        rows_dev, step_count, KVH, groups, kv_width
    )
    suffix_scores = (
        jnp.einsum("rskgw,tw->rskgt", wide_query, flat_keys, preferred_element_type=jnp.float32)
        * score_scale
    )
    suffix_stats = block_stats(suffix_scores, live_mask, flat_values, "rskgt,tkd->rskgd")

    fresh_keys = new_keys.reshape(rows_dev, step_count, KVH, HD)
    fresh_values = new_values.reshape(rows_dev, step_count, KVH, HD)
    fresh_scores = (
        jnp.einsum("rskgd,rtkd->rskgt", own_query, fresh_keys, preferred_element_type=jnp.float32)
        * score_scale
    )
    causal = jnp.arange(step_count)[None, :] <= jnp.arange(step_count)[:, None]
    causal = causal.reshape(1, step_count, 1, 1, step_count)
    fresh_stats = block_stats(fresh_scores, causal, fresh_values, "rskgt,rtkd->rskgd")

    core_bit = ctx_index % 2
    half_kv = KVH // 2
    half_heads = H // 2
    own_half_query = lax.dynamic_slice_in_dim(own_query, core_bit * half_kv, half_kv, 2)
    query_rows = rows_dev * step_count * half_heads * HD // LANES
    id_rows = -(-rows_dev // 16) * 16
    id_block = jnp.zeros((id_rows, LANES), jnp.bfloat16)
    id_block = id_block.at[:rows_dev, :].set(
        jnp.broadcast_to(prefix_id.astype(jnp.bfloat16)[:, None], (rows_dev, LANES))
    )
    packed = jnp.concatenate([own_half_query.reshape(query_rows, LANES), id_block], axis=0)
    fanned = jnp.broadcast_to(packed[None], (row_count,) + packed.shape)
    gathered = lax.all_to_all(fanned, "row", split_axis=0, concat_axis=0, tiled=True)
    total_rows = row_count * rows_dev
    half_query = gathered[:, :query_rows, :].reshape(
        total_rows, step_count, half_kv, groups, HD
    )
    every_prefix = gathered[:, query_rows : query_rows + rows_dev, 0].reshape(total_rows)
    every_prefix = every_prefix.astype(jnp.int32)

    swap = [(c, c ^ 1) for c in range(ctx_count)]
    span_len = prefix_keys.shape[1]
    prefix_count = prefix_keys.shape[0]
    kv_both = jnp.stack(
        [
            prefix_keys.reshape(prefix_count, span_len, KVH, HD),
            prefix_values.reshape(prefix_count, span_len, KVH, HD),
        ]
    )
    own_kv = lax.dynamic_slice_in_dim(kv_both, core_bit * half_kv, half_kv, 3)
    given_kv = lax.dynamic_slice_in_dim(kv_both, (1 - core_bit) * half_kv, half_kv, 3)
    partner_kv = lax.ppermute(given_kv, "ctx", swap)


    def prefix_block(kv):
        row_kv = jnp.take(kv, every_prefix, axis=1)
        row_keys, row_values = row_kv[0], row_kv[1]
        scores = (
            jnp.einsum(
                "rskgd,rtkd->rskgt", half_query, row_keys, preferred_element_type=jnp.float32
            )
            * score_scale
        )
        always = jnp.ones((1, 1, 1, 1, span_len), dtype=bool)
        return block_stats(scores, always, row_values, "rskgt,rtkd->rskgd")

    prefix_stats = combine_pair(prefix_block(own_kv), prefix_block(partner_kv))

    def head_half(member, at):
        return lax.dynamic_slice_in_dim(member, at * half_kv, half_kv, 2)

    suffix_packed = jnp.concatenate(
        [suffix_stats[2], suffix_stats[0][..., None], suffix_stats[1][..., None]], axis=-1
    )
    suffix_moved = lax.ppermute(head_half(suffix_packed, 1 - core_bit), "ctx", swap)
    suffix_partner = (suffix_moved[..., HD], suffix_moved[..., HD + 1], suffix_moved[..., :HD])
    suffix_kept = tuple(head_half(member, core_bit) for member in suffix_stats)
    suffix_half = combine_pair(suffix_kept, suffix_partner)

    own_row = (jnp.arange(total_rows, dtype=jnp.int32) // rows_dev) == row_index

    def over_rows(member, empty):
        tiled = jnp.tile(member, (row_count,) + (1,) * (member.ndim - 1))
        mask = own_row.reshape((total_rows,) + (1,) * (member.ndim - 1))
        return jnp.where(mask, tiled, empty)

    suffix_rows = (
        over_rows(suffix_half[0], MASKED_SCORE),
        over_rows(suffix_half[1], 0.0),
        over_rows(suffix_half[2], 0.0),
    )
    peak_all, total_all, sum_all = combine_pair(prefix_stats, suffix_rows)

    half_units = rows_dev * step_count * half_heads
    chunk = half_units // ctx_count
    pt_rows = -(-2 * chunk // LANES)
    dests = ctx_count * row_count

    def by_dest(member, tail=()):
        return member.reshape((dests, chunk) + tail)

    pt = jnp.concatenate([by_dest(peak_all), by_dest(total_all)], axis=-1)
    pt = jnp.pad(pt, ((0, 0), (0, pt_rows * LANES - 2 * chunk)))
    outgoing = jnp.concatenate(
        [by_dest(sum_all, (HD,)), pt.reshape(dests, pt_rows, LANES)], axis=1
    )
    incoming = lax.all_to_all(
        outgoing.reshape(dests, 1, (chunk + pt_rows) * LANES),
        ("row", "ctx"),
        split_axis=0,
        concat_axis=0,
        tiled=True,
    )
    incoming = incoming.reshape(dests, chunk + pt_rows, LANES)
    got_pt = incoming[:, chunk:, :].reshape(dests, pt_rows * LANES)
    pairs = ctx_count // 2

    def by_half(member, tail=()):
        shaped = member.reshape((row_count, pairs, 2, chunk) + tail)
        return jnp.moveaxis(shaped, 2, 0).reshape((2, row_count * pairs, chunk) + tail)

    got_peak = by_half(got_pt[:, :chunk])
    got_total = by_half(got_pt[:, chunk : 2 * chunk])
    got_sum = by_half(incoming[:, :chunk, :], (HD,))

    def fresh_chunk(member, tail=()):
        shaped = member.reshape((rows_dev, step_count, 2, half_heads) + tail)
        shaped = jnp.moveaxis(shaped, 2, 0).reshape((2, half_units) + tail)
        return lax.dynamic_slice_in_dim(shaped, ctx_index * chunk, chunk, 1)

    fresh_peak = fresh_chunk(fresh_stats[0])
    fresh_total = fresh_chunk(fresh_stats[1])
    fresh_sum = fresh_chunk(fresh_stats[2], (HD,))

    top = jnp.maximum(jnp.max(got_peak, axis=1), fresh_peak)
    factor = jnp.exp(got_peak - top[:, None])
    fresh_factor = jnp.exp(fresh_peak - top)
    denom = jnp.sum(factor * got_total, axis=1) + fresh_factor * fresh_total
    numer = jnp.sum(factor[..., None] * got_sum, axis=1) + fresh_factor[..., None] * fresh_sum
    result = (numer / denom[..., None]).astype(jnp.bfloat16)
    whole = lax.all_gather(result, "ctx", axis=0, tiled=False)
    whole = jnp.swapaxes(whole, 0, 1).reshape(2, rows_dev, step_count, half_heads, HD)
    whole = jnp.moveaxis(whole, 0, 2)
    return whole.reshape(rows_dev, step_count, H * HD)


def solution(mesh):
    in_specs = (
        P("row", None, None),
        P("row"),
        P(None, ("ctx", "row"), None),
        P(None, ("ctx", "row"), None),
        P(("ctx", "row"), None, None),
        P(("ctx", "row"), None, None),
        P("row", None),
        P("row"),
        P("row", None, None),
        P("row", None, None),
    )
    out_specs = P("row", None, None)
    return jax.shard_map(
        per_device, mesh=mesh, in_specs=in_specs, out_specs=out_specs, check_vma=False
    )
```

```python
import math

import jax
import jax.numpy as jnp
from jax import lax
from jax.sharding import PartitionSpec as P

H = 32
KVH = 4
HD = 128
LANES = 128


MASKED_SCORE = -1e30


def block_stats(scores, valid_mask, values, einsum_form):
    block_peak = jnp.max(jnp.where(valid_mask, scores, MASKED_SCORE), axis=-1)
    weights = jnp.where(valid_mask, jnp.exp(scores - block_peak[..., None]), 0.0).astype(
        jnp.bfloat16
    )
    block_total = jnp.sum(weights.astype(jnp.float32), axis=-1)
    block_sum = jnp.einsum(einsum_form, weights, values, preferred_element_type=jnp.float32)
    return (block_peak, block_total, block_sum)


def combine_pair(earlier, later):
    highest = jnp.maximum(earlier[0], later[0])
    left_factor = jnp.exp(earlier[0] - highest)
    right_factor = jnp.exp(later[0] - highest)
    totals = left_factor * earlier[1] + right_factor * later[1]
    sums = left_factor[..., None] * earlier[2] + right_factor[..., None] * later[2]
    return (highest, totals, sums)


def per_device(
    queries,
    prefix_id,
    prefix_keys,
    prefix_values,
    pool_keys,
    pool_values,
    page_table,
    suffix_len,
    new_keys,
    new_values,
):
    rows_dev, step_count, feature_width = queries.shape
    groups = H // KVH
    score_scale = 1.0 / math.sqrt(HD)
    row_count = lax.axis_size("row")
    ctx_count = lax.axis_size("ctx")
    row_index = lax.axis_index("row")
    ctx_index = lax.axis_index("ctx")
    flat_index = ctx_index * row_count + row_index
    own_query = queries.reshape(rows_dev, step_count, KVH, groups, HD)

    slot_count, page_len, kv_width = pool_keys.shape
    slot_ids = flat_index * slot_count + jnp.arange(slot_count, dtype=jnp.int32)
    slot_match = page_table[:, :, None] == slot_ids[None, None, :]
    entry_pos = jnp.arange(page_table.shape[1], dtype=jnp.int32)
    page_of = jnp.sum(jnp.where(slot_match, entry_pos[None, :, None], 0), axis=1)
    owned = jnp.any(slot_match, axis=1)
    token_pos = (
        page_of[:, :, None] * page_len + jnp.arange(page_len, dtype=jnp.int32)[None, None, :]
    )
    live_mask = owned[:, :, None] & (token_pos < suffix_len[:, None, None])
    live_mask = live_mask.reshape(rows_dev, 1, 1, 1, slot_count * page_len)
    flat_keys = pool_keys.reshape(slot_count * page_len, kv_width)
    flat_values = pool_values.reshape(slot_count * page_len, KVH, HD)
    head_eye = (jnp.arange(KVH)[:, None] == jnp.arange(KVH)[None, :]).reshape(
        1, 1, KVH, 1, KVH, 1
    )
    wide_query = jnp.where(head_eye, own_query[:, :, :, :, None, :], 0).reshape(
        rows_dev, step_count, KVH, groups, kv_width
    )
    suffix_scores = (
        jnp.einsum("rskgw,tw->rskgt", wide_query, flat_keys, preferred_element_type=jnp.float32)
        * score_scale
    )
    suffix_stats = block_stats(suffix_scores, live_mask, flat_values, "rskgt,tkd->rskgd")

    fresh_keys = new_keys.reshape(rows_dev, step_count, KVH, HD)
    fresh_values = new_values.reshape(rows_dev, step_count, KVH, HD)
    fresh_scores = (
        jnp.einsum("rskgd,rtkd->rskgt", own_query, fresh_keys, preferred_element_type=jnp.float32)
        * score_scale
    )
    causal = jnp.arange(step_count)[None, :] <= jnp.arange(step_count)[:, None]
    causal = causal.reshape(1, step_count, 1, 1, step_count)
    fresh_stats = block_stats(fresh_scores, causal, fresh_values, "rskgt,rtkd->rskgd")

    core_bit = ctx_index % 2
    half_kv = KVH // 2
    half_heads = H // 2
    own_half_query = lax.dynamic_slice_in_dim(own_query, core_bit * half_kv, half_kv, 2)
    query_rows = rows_dev * step_count * half_heads * HD // LANES
    id_rows = -(-rows_dev // 16) * 16
    id_block = jnp.zeros((id_rows, LANES), jnp.bfloat16)
    id_block = id_block.at[:rows_dev, :].set(
        jnp.broadcast_to(prefix_id.astype(jnp.bfloat16)[:, None], (rows_dev, LANES))
    )
    packed = jnp.concatenate([own_half_query.reshape(query_rows, LANES), id_block], axis=0)
    fanned = jnp.broadcast_to(packed[None], (row_count,) + packed.shape)
    gathered = lax.all_to_all(fanned, "row", split_axis=0, concat_axis=0, tiled=True)
    total_rows = row_count * rows_dev
    half_query = gathered[:, :query_rows, :].reshape(
        total_rows, step_count, half_kv, groups, HD
    )
    every_prefix = gathered[:, query_rows : query_rows + rows_dev, 0].reshape(total_rows)
    every_prefix = every_prefix.astype(jnp.int32)

    swap = [(c, c ^ 1) for c in range(ctx_count)]
    span_len = prefix_keys.shape[1]
    prefix_count = prefix_keys.shape[0]
    kv_both = jnp.stack(
        [
            prefix_keys.reshape(prefix_count, span_len, KVH, HD),
            prefix_values.reshape(prefix_count, span_len, KVH, HD),
        ]
    )
    own_kv = lax.dynamic_slice_in_dim(kv_both, core_bit * half_kv, half_kv, 3)
    given_kv = lax.dynamic_slice_in_dim(kv_both, (1 - core_bit) * half_kv, half_kv, 3)
    partner_kv = lax.ppermute(given_kv, "ctx", swap)


    chosen = (
        every_prefix[:, None] == jnp.arange(prefix_count, dtype=jnp.int32)[None, :]
    ).reshape(total_rows, 1, 1, 1, prefix_count, 1)

    def prefix_block(kv):
        every_scores = jnp.einsum(
            "rskgd,ptkd->rskgpt", half_query, kv[0], preferred_element_type=jnp.float32
        )
        scores = jnp.sum(jnp.where(chosen, every_scores, 0.0), axis=4) * score_scale
        block_peak = jnp.max(scores, axis=-1)
        weights = jnp.exp(scores - block_peak[..., None]).astype(jnp.bfloat16)
        block_total = jnp.sum(weights.astype(jnp.float32), axis=-1)
        spread = jnp.where(chosen, weights[..., None, :], jnp.zeros((), jnp.bfloat16))
        block_sum = jnp.einsum(
            "rskgpt,ptkd->rskgd", spread, kv[1], preferred_element_type=jnp.float32
        )
        return (block_peak, block_total, block_sum)

    prefix_stats = combine_pair(prefix_block(own_kv), prefix_block(partner_kv))

    def head_half(member, at):
        return lax.dynamic_slice_in_dim(member, at * half_kv, half_kv, 2)

    suffix_packed = jnp.concatenate(
        [suffix_stats[2], suffix_stats[0][..., None], suffix_stats[1][..., None]], axis=-1
    )
    suffix_moved = lax.ppermute(head_half(suffix_packed, 1 - core_bit), "ctx", swap)
    suffix_partner = (suffix_moved[..., HD], suffix_moved[..., HD + 1], suffix_moved[..., :HD])
    suffix_kept = tuple(head_half(member, core_bit) for member in suffix_stats)
    suffix_half = combine_pair(suffix_kept, suffix_partner)

    row_start = row_index * rows_dev
    own_prefix = tuple(
        lax.dynamic_slice_in_dim(member, row_start, rows_dev, 0) for member in prefix_stats
    )
    own_merged = combine_pair(own_prefix, suffix_half)
    peak_all, total_all, sum_all = tuple(
        lax.dynamic_update_slice_in_dim(whole_arr, piece_arr, row_start, 0)
        for whole_arr, piece_arr in zip(prefix_stats, own_merged)
    )

    half_units = rows_dev * step_count * half_heads
    chunk = half_units // ctx_count
    pt_rows = -(-2 * chunk // LANES)
    dests = ctx_count * row_count

    def by_dest(member, tail=()):
        return member.reshape((dests, chunk) + tail)

    pt = jnp.concatenate([by_dest(peak_all), by_dest(total_all)], axis=-1)
    pt = jnp.pad(pt, ((0, 0), (0, pt_rows * LANES - 2 * chunk)))
    outgoing = jnp.concatenate(
        [by_dest(sum_all, (HD,)), pt.reshape(dests, pt_rows, LANES)], axis=1
    )
    incoming = lax.all_to_all(
        outgoing.reshape(dests, 1, (chunk + pt_rows) * LANES),
        ("row", "ctx"),
        split_axis=0,
        concat_axis=0,
        tiled=True,
    )
    incoming = incoming.reshape(dests, chunk + pt_rows, LANES)
    got_pt = incoming[:, chunk:, :].reshape(dests, pt_rows * LANES)
    pairs = ctx_count // 2

    def by_half(member, tail=()):
        shaped = member.reshape((row_count, pairs, 2, chunk) + tail)
        return jnp.moveaxis(shaped, 2, 0).reshape((2, row_count * pairs, chunk) + tail)

    got_peak = by_half(got_pt[:, :chunk])
    got_total = by_half(got_pt[:, chunk : 2 * chunk])
    got_sum = by_half(incoming[:, :chunk, :], (HD,))

    def fresh_chunk(member, tail=()):
        shaped = member.reshape((rows_dev, step_count, 2, half_heads) + tail)
        shaped = jnp.moveaxis(shaped, 2, 0).reshape((2, half_units) + tail)
        return lax.dynamic_slice_in_dim(shaped, ctx_index * chunk, chunk, 1)

    fresh_peak = fresh_chunk(fresh_stats[0])
    fresh_total = fresh_chunk(fresh_stats[1])
    fresh_sum = fresh_chunk(fresh_stats[2], (HD,))

    top = jnp.maximum(jnp.max(got_peak, axis=1), fresh_peak)
    factor = jnp.exp(got_peak - top[:, None])
    fresh_factor = jnp.exp(fresh_peak - top)
    denom = jnp.sum(factor * got_total, axis=1) + fresh_factor * fresh_total
    numer = jnp.sum(factor[..., None] * got_sum, axis=1) + fresh_factor[..., None] * fresh_sum
    result = (numer / denom[..., None]).astype(jnp.bfloat16)
    whole = lax.all_gather(result, "ctx", axis=0, tiled=False)
    whole = jnp.swapaxes(whole, 0, 1).reshape(2, rows_dev, step_count, half_heads, HD)
    whole = jnp.moveaxis(whole, 0, 2)
    return whole.reshape(rows_dev, step_count, H * HD)


def solution(mesh):
    in_specs = (
        P("row", None, None),
        P("row"),
        P(None, ("ctx", "row"), None),
        P(None, ("ctx", "row"), None),
        P(("ctx", "row"), None, None),
        P(("ctx", "row"), None, None),
        P("row", None),
        P("row"),
        P("row", None, None),
        P("row", None, None),
    )
    out_specs = P("row", None, None)
    return jax.shard_map(
        per_device, mesh=mesh, in_specs=in_specs, out_specs=out_specs, check_vma=False
    )
```

```python
import math

import jax
import jax.numpy as jnp
from jax import lax
from jax.sharding import PartitionSpec as P

H = 32
KVH = 4
HD = 128
LANES = 128


MASKED_SCORE = -1e30


def block_stats(scores, valid_mask, values, einsum_form):
    block_peak = jnp.max(jnp.where(valid_mask, scores, MASKED_SCORE), axis=-1)
    weights = jnp.where(valid_mask, jnp.exp(scores - block_peak[..., None]), 0.0).astype(
        jnp.bfloat16
    )
    block_total = jnp.sum(weights.astype(jnp.float32), axis=-1)
    block_sum = jnp.einsum(einsum_form, weights, values, preferred_element_type=jnp.float32)
    return (block_peak, block_total, block_sum)


def combine_pair(earlier, later):
    highest = jnp.maximum(earlier[0], later[0])
    left_factor = jnp.exp(earlier[0] - highest)
    right_factor = jnp.exp(later[0] - highest)
    totals = left_factor * earlier[1] + right_factor * later[1]
    sums = left_factor[..., None] * earlier[2] + right_factor[..., None] * later[2]
    return (highest, totals, sums)


def per_device(
    queries,
    prefix_id,
    prefix_keys,
    prefix_values,
    pool_keys,
    pool_values,
    page_table,
    suffix_len,
    new_keys,
    new_values,
):
    rows_dev, step_count, feature_width = queries.shape
    groups = H // KVH
    score_scale = 1.0 / math.sqrt(HD)
    row_count = lax.axis_size("row")
    ctx_count = lax.axis_size("ctx")
    row_index = lax.axis_index("row")
    ctx_index = lax.axis_index("ctx")
    flat_index = ctx_index * row_count + row_index
    own_query = queries.reshape(rows_dev, step_count, KVH, groups, HD)

    slot_count, page_len, kv_width = pool_keys.shape
    slot_ids = flat_index * slot_count + jnp.arange(slot_count, dtype=jnp.int32)
    slot_match = page_table[:, :, None] == slot_ids[None, None, :]
    entry_pos = jnp.arange(page_table.shape[1], dtype=jnp.int32)
    page_of = jnp.sum(jnp.where(slot_match, entry_pos[None, :, None], 0), axis=1)
    owned = jnp.any(slot_match, axis=1)
    token_pos = (
        page_of[:, :, None] * page_len + jnp.arange(page_len, dtype=jnp.int32)[None, None, :]
    )
    live_mask = owned[:, :, None] & (token_pos < suffix_len[:, None, None])
    live_mask = live_mask.reshape(rows_dev, 1, 1, 1, slot_count * page_len)
    flat_keys = pool_keys.reshape(slot_count * page_len, kv_width)
    flat_values = pool_values.reshape(slot_count * page_len, KVH, HD)
    head_eye = (jnp.arange(KVH)[:, None] == jnp.arange(KVH)[None, :]).reshape(
        1, 1, KVH, 1, KVH, 1
    )
    wide_query = jnp.where(head_eye, own_query[:, :, :, :, None, :], 0).reshape(
        rows_dev, step_count, KVH, groups, kv_width
    )
    suffix_scores = (
        jnp.einsum("rskgw,tw->rskgt", wide_query, flat_keys, preferred_element_type=jnp.float32)
        * score_scale
    )
    suffix_stats = block_stats(suffix_scores, live_mask, flat_values, "rskgt,tkd->rskgd")

    fresh_keys = new_keys.reshape(rows_dev, step_count, KVH, HD)
    fresh_values = new_values.reshape(rows_dev, step_count, KVH, HD)
    fresh_scores = (
        jnp.einsum("rskgd,rtkd->rskgt", own_query, fresh_keys, preferred_element_type=jnp.float32)
        * score_scale
    )
    causal = jnp.arange(step_count)[None, :] <= jnp.arange(step_count)[:, None]
    causal = causal.reshape(1, step_count, 1, 1, step_count)
    fresh_stats = block_stats(fresh_scores, causal, fresh_values, "rskgt,rtkd->rskgd")

    core_bit = ctx_index % 2
    half_kv = KVH // 2
    half_heads = H // 2
    own_half_query = lax.dynamic_slice_in_dim(own_query, core_bit * half_kv, half_kv, 2)
    query_rows = rows_dev * step_count * half_heads * HD // LANES
    id_rows = -(-rows_dev // 16) * 16
    id_block = jnp.zeros((id_rows, LANES), jnp.bfloat16)
    id_block = id_block.at[:rows_dev, :].set(
        jnp.broadcast_to(prefix_id.astype(jnp.bfloat16)[:, None], (rows_dev, LANES))
    )
    packed = jnp.concatenate([own_half_query.reshape(query_rows, LANES), id_block], axis=0)
    fanned = jnp.broadcast_to(packed[None], (row_count,) + packed.shape)
    gathered = lax.all_to_all(fanned, "row", split_axis=0, concat_axis=0, tiled=True)
    total_rows = row_count * rows_dev
    half_query = gathered[:, :query_rows, :].reshape(
        total_rows, step_count, half_kv, groups, HD
    )
    every_prefix = gathered[:, query_rows : query_rows + rows_dev, 0].reshape(total_rows)
    every_prefix = every_prefix.astype(jnp.int32)

    swap = [(c, c ^ 1) for c in range(ctx_count)]
    span_len = prefix_keys.shape[1]
    prefix_count = prefix_keys.shape[0]
    kv_both = jnp.stack(
        [
            prefix_keys.reshape(prefix_count, span_len, KVH, HD),
            prefix_values.reshape(prefix_count, span_len, KVH, HD),
        ]
    )
    own_kv = lax.dynamic_slice_in_dim(kv_both, core_bit * half_kv, half_kv, 3)
    given_kv = lax.dynamic_slice_in_dim(kv_both, (1 - core_bit) * half_kv, half_kv, 3)
    partner_kv = lax.ppermute(given_kv, "ctx", swap)


    kv_pair = jnp.concatenate([own_kv, partner_kv], axis=2)
    row_kv = jnp.take(kv_pair, every_prefix, axis=1).reshape(
        2, total_rows, 2, span_len, half_kv, HD
    )
    pair_scores = (
        jnp.einsum(
            "rskgd,rbtkd->rskgbt", half_query, row_kv[0], preferred_element_type=jnp.float32
        )
        * score_scale
    )
    pair_peak = jnp.max(pair_scores, axis=-1)
    pair_weights = jnp.exp(pair_scores - pair_peak[..., None]).astype(jnp.bfloat16)
    pair_total = jnp.sum(pair_weights.astype(jnp.float32), axis=-1)
    pair_sum = jnp.einsum(
        "rskgbt,rbtkd->rskgbd", pair_weights, row_kv[1], preferred_element_type=jnp.float32
    )
    prefix_stats = combine_pair(
        (pair_peak[..., 0], pair_total[..., 0], pair_sum[..., 0, :]),
        (pair_peak[..., 1], pair_total[..., 1], pair_sum[..., 1, :]),
    )

    def head_half(member, at):
        return lax.dynamic_slice_in_dim(member, at * half_kv, half_kv, 2)

    suffix_packed = jnp.concatenate(
        [suffix_stats[2], suffix_stats[0][..., None], suffix_stats[1][..., None]], axis=-1
    )
    suffix_moved = lax.ppermute(head_half(suffix_packed, 1 - core_bit), "ctx", swap)
    suffix_partner = (suffix_moved[..., HD], suffix_moved[..., HD + 1], suffix_moved[..., :HD])
    suffix_kept = tuple(head_half(member, core_bit) for member in suffix_stats)
    suffix_half = combine_pair(suffix_kept, suffix_partner)

    row_start = row_index * rows_dev
    own_prefix = tuple(
        lax.dynamic_slice_in_dim(member, row_start, rows_dev, 0) for member in prefix_stats
    )
    own_merged = combine_pair(own_prefix, suffix_half)
    peak_all, total_all, sum_all = tuple(
        lax.dynamic_update_slice_in_dim(whole_arr, piece_arr, row_start, 0)
        for whole_arr, piece_arr in zip(prefix_stats, own_merged)
    )

    half_units = rows_dev * step_count * half_heads
    chunk = half_units // ctx_count
    pt_rows = -(-2 * chunk // LANES)
    dests = ctx_count * row_count

    def by_dest(member, tail=()):
        return member.reshape((dests, chunk) + tail)

    pt = jnp.concatenate([by_dest(peak_all), by_dest(total_all)], axis=-1)
    pt = jnp.pad(pt, ((0, 0), (0, pt_rows * LANES - 2 * chunk)))
    outgoing = jnp.concatenate(
        [by_dest(sum_all, (HD,)), pt.reshape(dests, pt_rows, LANES)], axis=1
    )
    incoming = lax.all_to_all(
        outgoing.reshape(dests, 1, (chunk + pt_rows) * LANES),
        ("row", "ctx"),
        split_axis=0,
        concat_axis=0,
        tiled=True,
    )
    incoming = incoming.reshape(dests, chunk + pt_rows, LANES)
    got_pt = incoming[:, chunk:, :].reshape(dests, pt_rows * LANES)
    pairs = ctx_count // 2

    def by_half(member, tail=()):
        shaped = member.reshape((row_count, pairs, 2, chunk) + tail)
        return jnp.moveaxis(shaped, 2, 0).reshape((2, row_count * pairs, chunk) + tail)

    got_peak = by_half(got_pt[:, :chunk])
    got_total = by_half(got_pt[:, chunk : 2 * chunk])
    got_sum = by_half(incoming[:, :chunk, :], (HD,))

    def fresh_chunk(member, tail=()):
        shaped = member.reshape((rows_dev, step_count, 2, half_heads) + tail)
        shaped = jnp.moveaxis(shaped, 2, 0).reshape((2, half_units) + tail)
        return lax.dynamic_slice_in_dim(shaped, ctx_index * chunk, chunk, 1)

    fresh_peak = fresh_chunk(fresh_stats[0])
    fresh_total = fresh_chunk(fresh_stats[1])
    fresh_sum = fresh_chunk(fresh_stats[2], (HD,))

    top = jnp.maximum(jnp.max(got_peak, axis=1), fresh_peak)
    factor = jnp.exp(got_peak - top[:, None])
    fresh_factor = jnp.exp(fresh_peak - top)
    denom = jnp.sum(factor * got_total, axis=1) + fresh_factor * fresh_total
    numer = jnp.sum(factor[..., None] * got_sum, axis=1) + fresh_factor[..., None] * fresh_sum
    result = (numer / denom[..., None]).astype(jnp.bfloat16)
    whole = lax.all_gather(result, "ctx", axis=0, tiled=False)
    whole = jnp.swapaxes(whole, 0, 1).reshape(2, rows_dev, step_count, half_heads, HD)
    whole = jnp.moveaxis(whole, 0, 2)
    return whole.reshape(rows_dev, step_count, H * HD)


def solution(mesh):
    in_specs = (
        P("row", None, None),
        P("row"),
        P(None, ("ctx", "row"), None),
        P(None, ("ctx", "row"), None),
        P(("ctx", "row"), None, None),
        P(("ctx", "row"), None, None),
        P("row", None),
        P("row"),
        P("row", None, None),
        P("row", None, None),
    )
    out_specs = P("row", None, None)
    return jax.shard_map(
        per_device, mesh=mesh, in_specs=in_specs, out_specs=out_specs, check_vma=False
    )
```

```python
import math

import jax
import jax.numpy as jnp
from jax import lax
from jax.sharding import PartitionSpec as P

H = 32
KVH = 4
HD = 128
LANES = 128


MASKED_SCORE = -1e30


def block_stats(scores, valid_mask, values, einsum_form):
    block_peak = jnp.max(jnp.where(valid_mask, scores, MASKED_SCORE), axis=-1)
    weights = jnp.where(valid_mask, jnp.exp(scores - block_peak[..., None]), 0.0).astype(
        jnp.bfloat16
    )
    block_total = jnp.sum(weights.astype(jnp.float32), axis=-1)
    block_sum = jnp.einsum(einsum_form, weights, values, preferred_element_type=jnp.float32)
    return (block_peak, block_total, block_sum)


def combine_pair(earlier, later):
    highest = jnp.maximum(earlier[0], later[0])
    left_factor = jnp.exp(earlier[0] - highest)
    right_factor = jnp.exp(later[0] - highest)
    totals = left_factor * earlier[1] + right_factor * later[1]
    sums = left_factor[..., None] * earlier[2] + right_factor[..., None] * later[2]
    return (highest, totals, sums)


def per_device(
    queries,
    prefix_id,
    prefix_keys,
    prefix_values,
    pool_keys,
    pool_values,
    page_table,
    suffix_len,
    new_keys,
    new_values,
):
    rows_dev, step_count, feature_width = queries.shape
    groups = H // KVH
    score_scale = 1.0 / math.sqrt(HD)
    row_count = lax.axis_size("row")
    ctx_count = lax.axis_size("ctx")
    row_index = lax.axis_index("row")
    ctx_index = lax.axis_index("ctx")
    flat_index = ctx_index * row_count + row_index
    own_query = queries.reshape(rows_dev, step_count, KVH, groups, HD)

    slot_count, page_len, kv_width = pool_keys.shape
    slot_ids = flat_index * slot_count + jnp.arange(slot_count, dtype=jnp.int32)
    slot_match = page_table[:, :, None] == slot_ids[None, None, :]
    entry_pos = jnp.arange(page_table.shape[1], dtype=jnp.int32)
    page_of = jnp.sum(jnp.where(slot_match, entry_pos[None, :, None], 0), axis=1)
    owned = jnp.any(slot_match, axis=1)
    token_pos = (
        page_of[:, :, None] * page_len + jnp.arange(page_len, dtype=jnp.int32)[None, None, :]
    )
    live_mask = owned[:, :, None] & (token_pos < suffix_len[:, None, None])
    live_mask = live_mask.reshape(rows_dev, 1, 1, 1, slot_count * page_len)
    flat_keys = pool_keys.reshape(slot_count * page_len, kv_width)
    flat_values = pool_values.reshape(slot_count * page_len, KVH, HD)
    head_eye = (jnp.arange(KVH)[:, None] == jnp.arange(KVH)[None, :]).reshape(
        1, 1, KVH, 1, KVH, 1
    )
    wide_query = jnp.where(head_eye, own_query[:, :, :, :, None, :], 0).reshape(
        rows_dev, step_count, KVH, groups, kv_width
    )
    suffix_scores = (
        jnp.einsum("rskgw,tw->rskgt", wide_query, flat_keys, preferred_element_type=jnp.float32)
        * score_scale
    )
    suffix_stats = block_stats(suffix_scores, live_mask, flat_values, "rskgt,tkd->rskgd")

    fresh_keys = new_keys.reshape(rows_dev, step_count, KVH, HD)
    fresh_values = new_values.reshape(rows_dev, step_count, KVH, HD)
    fresh_scores = (
        jnp.einsum("rskgd,rtkd->rskgt", own_query, fresh_keys, preferred_element_type=jnp.float32)
        * score_scale
    )
    causal = jnp.arange(step_count)[None, :] <= jnp.arange(step_count)[:, None]
    causal = causal.reshape(1, step_count, 1, 1, step_count)
    fresh_stats = block_stats(fresh_scores, causal, fresh_values, "rskgt,rtkd->rskgd")

    core_bit = ctx_index % 2
    half_kv = KVH // 2
    half_heads = H // 2
    own_half_query = lax.dynamic_slice_in_dim(own_query, core_bit * half_kv, half_kv, 2)
    query_rows = rows_dev * step_count * half_heads * HD // LANES
    id_rows = -(-rows_dev // 16) * 16
    id_block = jnp.zeros((id_rows, LANES), jnp.bfloat16)
    id_block = id_block.at[:rows_dev, :].set(
        jnp.broadcast_to(prefix_id.astype(jnp.bfloat16)[:, None], (rows_dev, LANES))
    )
    packed = jnp.concatenate([own_half_query.reshape(query_rows, LANES), id_block], axis=0)
    fanned = jnp.broadcast_to(packed[None], (row_count,) + packed.shape)
    gathered = lax.all_to_all(fanned, "row", split_axis=0, concat_axis=0, tiled=True)
    total_rows = row_count * rows_dev
    half_query = gathered[:, :query_rows, :].reshape(
        total_rows, step_count, half_kv, groups, HD
    )
    every_prefix = gathered[:, query_rows : query_rows + rows_dev, 0].reshape(total_rows)
    every_prefix = every_prefix.astype(jnp.int32)

    swap = [(c, c ^ 1) for c in range(ctx_count)]
    span_len = prefix_keys.shape[1]
    prefix_count = prefix_keys.shape[0]
    kv_both = jnp.stack(
        [
            prefix_keys.reshape(prefix_count, span_len, KVH, HD),
            prefix_values.reshape(prefix_count, span_len, KVH, HD),
        ]
    )
    own_kv = lax.dynamic_slice_in_dim(kv_both, core_bit * half_kv, half_kv, 3)
    given_kv = lax.dynamic_slice_in_dim(kv_both, (1 - core_bit) * half_kv, half_kv, 3)
    partner_kv = lax.ppermute(given_kv, "ctx", swap)


    def prefix_block(kv):
        row_kv = jnp.take(kv, every_prefix, axis=1)
        row_keys, row_values = row_kv[0], row_kv[1]
        scores = (
            jnp.einsum(
                "rskgd,rtkd->rskgt", half_query, row_keys, preferred_element_type=jnp.float32
            )
            * score_scale
        )
        always = jnp.ones((1, 1, 1, 1, span_len), dtype=bool)
        return block_stats(scores, always, row_values, "rskgt,rtkd->rskgd")

    prefix_stats = combine_pair(prefix_block(own_kv), prefix_block(partner_kv))

    def head_half(member, at):
        return lax.dynamic_slice_in_dim(member, at * half_kv, half_kv, 2)

    suffix_packed = jnp.concatenate(
        [suffix_stats[2], suffix_stats[0][..., None], suffix_stats[1][..., None]], axis=-1
    )
    suffix_moved = lax.ppermute(head_half(suffix_packed, 1 - core_bit), "ctx", swap)
    suffix_partner = (suffix_moved[..., HD], suffix_moved[..., HD + 1], suffix_moved[..., :HD])
    suffix_kept = tuple(head_half(member, core_bit) for member in suffix_stats)
    suffix_half = combine_pair(suffix_kept, suffix_partner)

    row_start = row_index * rows_dev
    own_prefix = tuple(
        lax.dynamic_slice_in_dim(member, row_start, rows_dev, 0) for member in prefix_stats
    )
    own_merged = combine_pair(own_prefix, suffix_half)
    peak_all, total_all, sum_all = tuple(
        lax.dynamic_update_slice_in_dim(whole_arr, piece_arr, row_start, 0)
        for whole_arr, piece_arr in zip(prefix_stats, own_merged)
    )

    half_units = rows_dev * step_count * half_heads
    chunk = half_units // ctx_count
    pt_rows = -(-2 * chunk // LANES)
    dests = ctx_count * row_count

    def by_dest(member, tail=()):
        return member.reshape((dests, chunk) + tail)

    pt = jnp.concatenate([by_dest(peak_all), by_dest(total_all)], axis=-1)
    pt = jnp.pad(pt, ((0, 0), (0, pt_rows * LANES - 2 * chunk)))
    outgoing = jnp.concatenate(
        [by_dest(sum_all, (HD,)), pt.reshape(dests, pt_rows, LANES)], axis=1
    )
    incoming = lax.all_to_all(
        outgoing.reshape(dests, 1, (chunk + pt_rows) * LANES),
        ("row", "ctx"),
        split_axis=0,
        concat_axis=0,
        tiled=True,
    )
    incoming = incoming.reshape(dests, (chunk + pt_rows) * LANES)
    got_pt = incoming[:, chunk * HD : chunk * HD + 2 * chunk]
    pairs = ctx_count // 2

    def by_half(member):
        shaped = member.reshape((row_count, pairs, 2) + member.shape[1:])
        return jnp.moveaxis(shaped, 2, 0).reshape((2, row_count * pairs) + member.shape[1:])

    got_peak = by_half(got_pt[:, :chunk])
    got_total = by_half(got_pt[:, chunk : 2 * chunk])
    got_sum = by_half(incoming[:, : chunk * HD])

    def fresh_chunk(member, tail=()):
        shaped = member.reshape((rows_dev, step_count, 2, half_heads) + tail)
        shaped = jnp.moveaxis(shaped, 2, 0).reshape((2, half_units) + tail)
        return lax.dynamic_slice_in_dim(shaped, ctx_index * chunk, chunk, 1)

    fresh_peak = fresh_chunk(fresh_stats[0])
    fresh_total = fresh_chunk(fresh_stats[1])
    fresh_sum = fresh_chunk(fresh_stats[2], (HD,))

    top = jnp.maximum(jnp.max(got_peak, axis=1), fresh_peak)
    factor = jnp.exp(got_peak - top[:, None])
    fresh_factor = jnp.exp(fresh_peak - top)
    denom = jnp.sum(factor * got_total, axis=1) + fresh_factor * fresh_total
    spread_factor = jnp.repeat(factor, HD, axis=2)
    numer = jnp.sum(spread_factor * got_sum, axis=1).reshape(2, chunk, HD)
    numer = numer + fresh_factor[..., None] * fresh_sum
    result = (numer / denom[..., None]).astype(jnp.bfloat16)
    whole = lax.all_gather(result, "ctx", axis=0, tiled=False)
    whole = jnp.swapaxes(whole, 0, 1).reshape(2, rows_dev, step_count, half_heads, HD)
    whole = jnp.moveaxis(whole, 0, 2)
    return whole.reshape(rows_dev, step_count, H * HD)


def solution(mesh):
    in_specs = (
        P("row", None, None),
        P("row"),
        P(None, ("ctx", "row"), None),
        P(None, ("ctx", "row"), None),
        P(("ctx", "row"), None, None),
        P(("ctx", "row"), None, None),
        P("row", None),
        P("row"),
        P("row", None, None),
        P("row", None, None),
    )
    out_specs = P("row", None, None)
    return jax.shard_map(
        per_device, mesh=mesh, in_specs=in_specs, out_specs=out_specs, check_vma=False
    )
```

```python
import math

import jax
import jax.numpy as jnp
from jax import lax
from jax.sharding import PartitionSpec as P

H = 32
KVH = 4
HD = 128
LANES = 128


MASKED_SCORE = -1e30


def block_stats(scores, valid_mask, values, einsum_form):
    block_peak = jnp.max(jnp.where(valid_mask, scores, MASKED_SCORE), axis=-1)
    weights = jnp.where(valid_mask, jnp.exp(scores - block_peak[..., None]), 0.0).astype(
        jnp.bfloat16
    )
    block_total = jnp.sum(weights.astype(jnp.float32), axis=-1)
    block_sum = jnp.einsum(einsum_form, weights, values, preferred_element_type=jnp.float32)
    return (block_peak, block_total, block_sum)


def combine_pair(earlier, later):
    highest = jnp.maximum(earlier[0], later[0])
    left_factor = jnp.exp(earlier[0] - highest)
    right_factor = jnp.exp(later[0] - highest)
    totals = left_factor * earlier[1] + right_factor * later[1]
    sums = left_factor[..., None] * earlier[2] + right_factor[..., None] * later[2]
    return (highest, totals, sums)


def per_device(
    queries,
    prefix_id,
    prefix_keys,
    prefix_values,
    pool_keys,
    pool_values,
    page_table,
    suffix_len,
    new_keys,
    new_values,
):
    rows_dev, step_count, feature_width = queries.shape
    groups = H // KVH
    score_scale = 1.0 / math.sqrt(HD)
    row_count = lax.axis_size("row")
    ctx_count = lax.axis_size("ctx")
    row_index = lax.axis_index("row")
    ctx_index = lax.axis_index("ctx")
    flat_index = ctx_index * row_count + row_index
    own_query = queries.reshape(rows_dev, step_count, KVH, groups, HD)

    slot_count, page_len, kv_width = pool_keys.shape
    slot_ids = flat_index * slot_count + jnp.arange(slot_count, dtype=jnp.int32)
    slot_match = page_table[:, :, None] == slot_ids[None, None, :]
    entry_pos = jnp.arange(page_table.shape[1], dtype=jnp.int32)
    page_of = jnp.sum(jnp.where(slot_match, entry_pos[None, :, None], 0), axis=1)
    owned = jnp.any(slot_match, axis=1)
    token_pos = (
        page_of[:, :, None] * page_len + jnp.arange(page_len, dtype=jnp.int32)[None, None, :]
    )
    live_mask = owned[:, :, None] & (token_pos < suffix_len[:, None, None])
    live_mask = live_mask.reshape(rows_dev, 1, 1, 1, slot_count * page_len)
    flat_keys = pool_keys.reshape(slot_count * page_len, kv_width)
    flat_values = pool_values.reshape(slot_count * page_len, KVH, HD)
    head_eye = (jnp.arange(KVH)[:, None] == jnp.arange(KVH)[None, :]).reshape(
        1, 1, KVH, 1, KVH, 1
    )
    wide_query = jnp.where(head_eye, own_query[:, :, :, :, None, :], 0).reshape(
        rows_dev, step_count, KVH, groups, kv_width
    )
    suffix_scores = (
        jnp.einsum("rskgw,tw->rskgt", wide_query, flat_keys, preferred_element_type=jnp.float32)
        * score_scale
    )
    suffix_stats = block_stats(suffix_scores, live_mask, flat_values, "rskgt,tkd->rskgd")

    fresh_keys = new_keys.reshape(rows_dev, step_count, KVH, HD)
    fresh_values = new_values.reshape(rows_dev, step_count, KVH, HD)
    fresh_scores = (
        jnp.einsum("rskgd,rtkd->rskgt", own_query, fresh_keys, preferred_element_type=jnp.float32)
        * score_scale
    )
    causal = jnp.arange(step_count)[None, :] <= jnp.arange(step_count)[:, None]
    causal = causal.reshape(1, step_count, 1, 1, step_count)
    fresh_stats = block_stats(fresh_scores, causal, fresh_values, "rskgt,rtkd->rskgd")

    core_bit = ctx_index % 2
    half_kv = KVH // 2
    half_heads = H // 2
    own_half_query = lax.dynamic_slice_in_dim(own_query, core_bit * half_kv, half_kv, 2)
    query_rows = rows_dev * step_count * half_heads * HD // LANES
    id_rows = -(-rows_dev // 16) * 16
    id_block = jnp.zeros((id_rows, LANES), jnp.bfloat16)
    id_block = id_block.at[:rows_dev, :].set(
        jnp.broadcast_to(prefix_id.astype(jnp.bfloat16)[:, None], (rows_dev, LANES))
    )
    packed = jnp.concatenate([own_half_query.reshape(query_rows, LANES), id_block], axis=0)
    fanned = jnp.broadcast_to(packed[None], (row_count,) + packed.shape)
    gathered = lax.all_to_all(fanned, "row", split_axis=0, concat_axis=0, tiled=True)
    total_rows = row_count * rows_dev
    half_query = gathered[:, :query_rows, :].reshape(
        total_rows, step_count, half_kv, groups, HD
    )
    every_prefix = gathered[:, query_rows : query_rows + rows_dev, 0].reshape(total_rows)
    every_prefix = every_prefix.astype(jnp.int32)

    swap = [(c, c ^ 1) for c in range(ctx_count)]
    span_len = prefix_keys.shape[1]
    prefix_count = prefix_keys.shape[0]
    kv_both = jnp.stack(
        [
            prefix_keys.reshape(prefix_count, span_len, KVH, HD),
            prefix_values.reshape(prefix_count, span_len, KVH, HD),
        ]
    )
    own_kv = lax.dynamic_slice_in_dim(kv_both, core_bit * half_kv, half_kv, 3)
    given_kv = lax.dynamic_slice_in_dim(kv_both, (1 - core_bit) * half_kv, half_kv, 3)
    partner_kv = lax.ppermute(given_kv, "ctx", swap)


    def prefix_block(kv):
        row_kv = jnp.take(kv, every_prefix, axis=1)
        row_keys, row_values = row_kv[0], row_kv[1]
        scores = (
            jnp.einsum(
                "rskgd,rtkd->rskgt", half_query, row_keys, preferred_element_type=jnp.float32
            )
            * score_scale
        )
        always = jnp.ones((1, 1, 1, 1, span_len), dtype=bool)
        return block_stats(scores, always, row_values, "rskgt,rtkd->rskgd")

    prefix_stats = combine_pair(prefix_block(own_kv), prefix_block(partner_kv))

    def head_half(member, at):
        return lax.dynamic_slice_in_dim(member, at * half_kv, half_kv, 2)

    suffix_packed = jnp.concatenate(
        [suffix_stats[2], suffix_stats[0][..., None], suffix_stats[1][..., None]], axis=-1
    )
    suffix_moved = lax.ppermute(head_half(suffix_packed, 1 - core_bit), "ctx", swap)
    suffix_partner = (suffix_moved[..., HD], suffix_moved[..., HD + 1], suffix_moved[..., :HD])
    suffix_kept = tuple(head_half(member, core_bit) for member in suffix_stats)
    suffix_half = combine_pair(suffix_kept, suffix_partner)

    row_start = row_index * rows_dev
    own_prefix = tuple(
        lax.dynamic_slice_in_dim(member, row_start, rows_dev, 0) for member in prefix_stats
    )
    own_merged = combine_pair(own_prefix, suffix_half)

    half_units = rows_dev * step_count * half_heads
    chunk = half_units // ctx_count
    pt_rows = -(-2 * chunk // LANES)
    dests = ctx_count * row_count

    def pack(peak, total, sums):
        count = peak.size // chunk
        pt = jnp.concatenate([peak.reshape(count, chunk), total.reshape(count, chunk)], axis=-1)
        pt = jnp.pad(pt, ((0, 0), (0, pt_rows * LANES - 2 * chunk)))
        return jnp.concatenate(
            [sums.reshape(count, chunk, HD), pt.reshape(count, pt_rows, LANES)], axis=1
        )

    outgoing = lax.dynamic_update_slice_in_dim(
        pack(*prefix_stats), pack(*own_merged), row_index * ctx_count, 0
    )
    incoming = lax.all_to_all(
        outgoing.reshape(dests, 1, (chunk + pt_rows) * LANES),
        ("row", "ctx"),
        split_axis=0,
        concat_axis=0,
        tiled=True,
    )
    incoming = incoming.reshape(dests, (chunk + pt_rows) * LANES)
    got_pt = incoming[:, chunk * HD : chunk * HD + 2 * chunk]
    pairs = ctx_count // 2

    def by_half(member):
        shaped = member.reshape((row_count, pairs, 2) + member.shape[1:])
        return jnp.moveaxis(shaped, 2, 0).reshape((2, row_count * pairs) + member.shape[1:])

    got_peak = by_half(got_pt[:, :chunk])
    got_total = by_half(got_pt[:, chunk : 2 * chunk])
    got_sum = by_half(incoming[:, : chunk * HD])

    def fresh_chunk(member, tail=()):
        shaped = member.reshape((rows_dev, step_count, 2, half_heads) + tail)
        shaped = jnp.moveaxis(shaped, 2, 0).reshape((2, half_units) + tail)
        return lax.dynamic_slice_in_dim(shaped, ctx_index * chunk, chunk, 1)

    fresh_peak = fresh_chunk(fresh_stats[0])
    fresh_total = fresh_chunk(fresh_stats[1])
    fresh_sum = fresh_chunk(fresh_stats[2], (HD,))

    top = jnp.maximum(jnp.max(got_peak, axis=1), fresh_peak)
    factor = jnp.exp(got_peak - top[:, None])
    fresh_factor = jnp.exp(fresh_peak - top)
    denom = jnp.sum(factor * got_total, axis=1) + fresh_factor * fresh_total
    spread_factor = jnp.repeat(factor, HD, axis=2)
    numer = jnp.sum(spread_factor * got_sum, axis=1).reshape(2, chunk, HD)
    numer = numer + fresh_factor[..., None] * fresh_sum
    result = (numer / denom[..., None]).astype(jnp.bfloat16)
    whole = lax.all_gather(result, "ctx", axis=0, tiled=False)
    whole = jnp.swapaxes(whole, 0, 1).reshape(2, rows_dev, step_count, half_heads, HD)
    whole = jnp.moveaxis(whole, 0, 2)
    return whole.reshape(rows_dev, step_count, H * HD)


def solution(mesh):
    in_specs = (
        P("row", None, None),
        P("row"),
        P(None, ("ctx", "row"), None),
        P(None, ("ctx", "row"), None),
        P(("ctx", "row"), None, None),
        P(("ctx", "row"), None, None),
        P("row", None),
        P("row"),
        P("row", None, None),
        P("row", None, None),
    )
    out_specs = P("row", None, None)
    return jax.shard_map(
        per_device, mesh=mesh, in_specs=in_specs, out_specs=out_specs, check_vma=False
    )
```
